32 devices in a mesh: dp: 16 (over z, x, core), head: 2 (over y).
Axes of the slice: x: 2, y: 2, z: 4, core: 2. Of those that a mesh axis runs over, the one named last changes fastest.
Arguments:
- inputs: float32 [512, 96, 512], P('dp', None, 'head'), may hold values from -6 to 6
- out_grad: float32 [512, 96, 512], P('dp', None, 'head'), may hold values from -6 to 6
- modes: int32 [8, 48], P('head'), may hold values from 0 to 48
- gates: int32 [2, 512, 96], P(None, 'dp'), may hold values from 0 to 4
- query_weight: float32 [512, 512], P(None, 'head'), may hold values from -0.25 to 0.25
- mixer_weight: float32 [8, 3072, 128], P('head'), may hold values from -0.42 to 0.42
- output_weight: float32 [512, 512], P('head'), may hold values from -0.25 to 0.25
- inner_weight: float32 [512, 2048], P(None, 'head'), may hold values from -0.25 to 0.25
- outer_weight: float32 [2048, 512], P('head'), may hold values from -0.125 to 0.125
- query_momentum: float32 [512, 512], P('dp', 'head'), may hold values from -80 to 80
- query_average: float32 [512, 512], P('dp', 'head'), may hold values from -0.25 to 0.25
- mixer_momentum: float32 [8, 3072, 128], P('head', 'dp'), may hold values from -32 to 32
- mixer_average: float32 [8, 3072, 128], P('head', 'dp'), may hold values from -0.42 to 0.42
- output_momentum: float32 [512, 512], P('head', 'dp'), may hold values from -128 to 128
- output_average: float32 [512, 512], P('head', 'dp'), may hold values from -0.25 to 0.25
- inner_momentum: float32 [512, 2048], P('dp', 'head'), may hold values from -40 to 40
- inner_average: float32 [512, 2048], P('dp', 'head'), may hold values from -0.25 to 0.25
- outer_momentum: float32 [2048, 512], P('head', 'dp'), may hold values from -80 to 80
- outer_average: float32 [2048, 512], P('head', 'dp'), may hold values from -0.125 to 0.125
Outputs:
- output: float32 [512, 96, 512], P('dp', None, 'head')
- input_grad: float32 [512, 96, 512], P('dp', None, 'head')
- query_momentum_new: float32 [512, 512], P('dp', 'head')
- query_weight_new: float32 [512, 512], P('dp', 'head')
- query_average_new: float32 [512, 512], P('dp', 'head')
- mixer_momentum_new: float32 [8, 3072, 128], P('head', 'dp')
- mixer_weight_new: float32 [8, 3072, 128], P('head', 'dp')
- mixer_average_new: float32 [8, 3072, 128], P('head', 'dp')
- output_momentum_new: float32 [512, 512], P('head', 'dp')
- output_weight_new: float32 [512, 512], P('head', 'dp')
- output_average_new: float32 [512, 512], P('head', 'dp')
- inner_momentum_new: float32 [512, 2048], P('dp', 'head')
- inner_weight_new: float32 [512, 2048], P('dp', 'head')
- inner_average_new: float32 [512, 2048], P('dp', 'head')
- outer_momentum_new: float32 [2048, 512], P('head', 'dp')
- outer_weight_new: float32 [2048, 512], P('head', 'dp')
- outer_average_new: float32 [2048, 512], P('head', 'dp')
The draws below stay inside these ranges and needn't reach their ends.
Inputs may be any that keep to these rules, and one draw needn't show every extreme that they name: `modes`: bins of the real transform of a 96-step window; a head may name a bin more than once. `gates`: number of the pool (sizes 7, 12, 14, 24, 48 in this order).
All inputs are finite; a program needn't handle non-finite values.
Results may differ from the reference program's by a relative error of at most 0.018.
Values may be sent and summed in bfloat16 or wider, within the bound.
No kernel may reach another device: no remote copies, remote signals or barrier semaphores. Data moves between devices by JAX's collectives and lax.ppermute only.
A program may use at most 192 MiB of HBM per device.

```python
import math
import jax
import jax.numpy as jnp
import numpy as np
from jax import lax

D = 512
FF = 2048
H = 8
M = 48
L = 96
E = 64
WIN_DEV = 32
WINDOWS = 512
TOKENS = 49152


def touch_ends(values, rng, low, largest):
    longest = values.shape.index(max(values.shape))
    spots = []
    for shift in (0, 1):
        where = [jax.random.randint(jax.random.fold_in(rng, axis), (), 0, length) for axis, length in enumerate(values.shape)]
        where[longest] = (where[longest] + shift) % values.shape[longest]
        spots.append(tuple(where))
    return values.at[spots[0]].set(low).at[spots[1]].set(largest)


def level_of(stream_key, extent, shards, least, largest):
    def one(axis_at, parts):
        heights = jax.random.uniform(jax.random.fold_in(jax.random.fold_in(stream_key, 6), axis_at), (parts,), jnp.float32, least / len(shards), largest / len(shards))
        return jnp.repeat(jnp.exp(heights), extent[axis_at] // parts).reshape((-1,) + (1,) * (len(extent) - axis_at - 1))

    loudness = one(*shards[0])
    for cut in shards[1:]:
        loudness = loudness * one(*cut)
    return loudness


def centred(rng, extent, scale, limit, cuts=(), kind=jnp.bfloat16):
    drawn = jax.random.normal(rng, extent, jnp.float32) * scale
    if len(cuts) > 0:
        drawn = level_of(rng, extent, cuts, -0.22, 0.18) * drawn
    return jnp.clip(drawn, min=-limit, max=limit).astype(kind)


def setup_inputs(seed: int = 0) -> dict:
    seeds = jax.random.split(jax.random.key(seed), 20)
    inputs = centred(seeds[0], (WINDOWS, L, D), 1.0, 6.0, ((0, 16), (2, 2)), jnp.float32)
    out_grad = centred(seeds[1], (WINDOWS, L, D), 1.0, 6.0, ((0, 16), (2, 2)), jnp.float32)
    modes = touch_ends(jax.random.randint(seeds[2], (H, M), 0, L // 2 + 1), jax.random.fold_in(seeds[2], 1), 0, (L // 2 + 1) - 1).astype(jnp.int32)
    gates = touch_ends(jax.random.randint(seeds[3], (2, WINDOWS, L), 0, 5), jax.random.fold_in(seeds[3], 1), 0, 4).astype(jnp.int32)
    query_weight = centred(seeds[4], (D, D), D ** -0.5, 0.25, ((1, 2),), jnp.float32)
    mixer_weight = centred(seeds[5], (H, M * E, 2 * E), 0.07, 0.42, ((0, 2),), jnp.float32)
    output_weight = centred(seeds[6], (D, D), D ** -0.5, 0.25, ((0, 2),), jnp.float32)
    inner_weight = centred(seeds[7], (D, FF), D ** -0.5, 0.25, ((1, 2),), jnp.float32)
    outer_weight = centred(seeds[8], (FF, D), FF ** -0.5, 0.125, ((0, 2),), jnp.float32)
    query_momentum = centred(seeds[9], (D, D), (0.06 * TOKENS ** 0.5), 80.0, ((0, 16), (1, 2)), jnp.float32)
    query_average = centred(seeds[10], (D, D), D ** -0.5, 0.25, ((0, 16), (1, 2)), jnp.float32)
    mixer_momentum = centred(seeds[11], (H, M * E, 2 * E), (0.025 * TOKENS ** 0.5), 32.0, ((0, 2), (1, 16)), jnp.float32)
    mixer_average = centred(seeds[12], (H, M * E, 2 * E), 0.07, 0.42, ((0, 2), (1, 16)), jnp.float32)
    output_momentum = centred(seeds[13], (D, D), (0.09 * TOKENS ** 0.5), 128.0, ((0, 2), (1, 16)), jnp.float32)
    output_average = centred(seeds[14], (D, D), D ** -0.5, 0.25, ((0, 2), (1, 16)), jnp.float32)
    inner_momentum = centred(seeds[15], (D, FF), (0.03 * TOKENS ** 0.5), 40.0, ((0, 16), (1, 2)), jnp.float32)
    inner_average = centred(seeds[16], (D, FF), D ** -0.5, 0.25, ((0, 16), (1, 2)), jnp.float32)
    outer_momentum = centred(seeds[17], (FF, D), (0.06 * TOKENS ** 0.5), 80.0, ((0, 2), (1, 16)), jnp.float32)
    outer_average = centred(seeds[18], (FF, D), FF ** -0.5, 0.125, ((0, 2), (1, 16)), jnp.float32)
    return {"inputs": inputs, "out_grad": out_grad, "modes": modes, "gates": gates, "query_weight": query_weight, "mixer_weight": mixer_weight, "output_weight": output_weight, "inner_weight": inner_weight, "outer_weight": outer_weight, "query_momentum": query_momentum, "query_average": query_average, "mixer_momentum": mixer_momentum, "mixer_average": mixer_average, "output_momentum": output_momentum, "output_average": output_average, "inner_momentum": inner_momentum, "inner_average": inner_average, "outer_momentum": outer_momentum, "outer_average": outer_average}


highest = lax.Precision.HIGHEST
pool_sizes = (7, 12, 14, 24, 48)
mixer_spread = 0.07
momentum_decay = 0.9
average_decay = 0.9

@jax.custom_vjp
def low(v):
    return lax.optimization_barrier(v.astype(jnp.bfloat16)).astype(jnp.float32)

@jax.custom_vjp
def low_back(v):
    return v

def low_keep(v):
    return (low(v), None)

def low_pass(kept, grad):
    return (grad,)

def back_keep(v):
    return (v, None)

def back_low(kept, grad):
    return (low(grad),)
low.defvjp(low_keep, low_pass)
low_back.defvjp(back_keep, back_low)

def pool_tables(length):
    tables = np.zeros((len(pool_sizes), length, length), np.float32)
    rows_all = np.arange(length)
    for pool_index, pool_width in enumerate(pool_sizes):
        lead_pad = (pool_width - 1) // 2
        for offset in range(pool_width):
            source = np.clip(rows_all - lead_pad + offset, 0, length - 1)
            tables[pool_index][rows_all, source] += np.float32(1.0 / pool_width)
    return jnp.asarray(tables)

def spectral_tables(modes, length):
    positions = jnp.arange(length, dtype=jnp.int32)
    phase = modes[:, :, None] * positions[None, None, :] % length
    angle = phase.astype(jnp.float32) * (2.0 * math.pi / length)
    cosine = jnp.cos(angle)
    sine = jnp.sin(angle)
    doubled = jnp.where((modes == 0) | (2 * modes == length), 1.0, 2.0).astype(jnp.float32) / length
    inv_cos = jnp.transpose(doubled[:, :, None] * cosine, (0, 2, 1))
    inv_sin = jnp.transpose(-doubled[:, :, None] * sine, (0, 2, 1))
    return (cosine, -sine, inv_cos, inv_sin)

def exact(form, left, right):
    return jnp.einsum(form, left, right, precision=highest)

def trend_of(values, picks, pools):
    averaged = exact('kts,wsd->kwtd', pools, values)
    chosen = (picks[None, :, :] == jnp.arange(len(pool_sizes), dtype=jnp.int32)[:, None, None]).astype(jnp.float32)
    return lax.optimization_barrier(jnp.sum(chosen[..., None] * averaged, axis=0))

def mixer_block(mixer_low, head_size):
    head_count = mixer_low.shape[0]
    shaped = mixer_low.reshape(head_count, -1, head_size, 2 * head_size)
    real_part = shaped[..., :head_size]
    imag_part = shaped[..., head_size:]
    upper = jnp.concatenate([real_part, imag_part], axis=-1)
    lower = jnp.concatenate([-imag_part, real_part], axis=-1)
    return jnp.concatenate([upper, lower], axis=2)

def forward(params, inputs, modes, gates):
    query_weight, mixer_weight, output_weight, inner_weight, outer_weight = params
    windows, length, model_width = inputs.shape
    head_count = modes.shape[0]
    head_size = model_width // head_count
    pools = pool_tables(length)
    fwd_cos, fwd_sin, inv_cos, inv_sin = [low(one_table) for one_table in spectral_tables(modes, length)]
    inputs_low = low(inputs)
    query = exact('wtd,de->wte', inputs_low, low(query_weight))
    query = low(low_back(query)).reshape(windows, length, head_count, head_size)
    spectrum = jnp.concatenate([exact('hmt,wthe->whme', fwd_cos, query), exact('hmt,wthe->whme', fwd_sin, query)], axis=-1)
    spectrum = low(low_back(spectrum))
    mixed = exact('whmi,hmio->whmo', spectrum, mixer_block(low(mixer_weight), head_size))
    mixed = low(low_back(mixed))
    field = exact('htm,whme->wthe', inv_cos, mixed[..., :head_size]) + exact('htm,whme->wthe', inv_sin, mixed[..., head_size:])
    field = low(low_back(field.reshape(windows, length, model_width)))
    attended = low_back(exact('wte,ed->wtd', field, low(output_weight)))
    resid_one = inputs + attended
    seasonal = resid_one - trend_of(resid_one, gates[0], pools)
    pre = low_back(exact('wtd,df->wtf', low(seasonal), low(inner_weight)))
    hidden = low(jax.nn.gelu(pre, approximate=False))
    feed = low_back(exact('wtf,fd->wtd', hidden, low(outer_weight)))
    combined = seasonal + feed
    return combined - trend_of(combined, gates[1], pools)

def reference(inputs, out_grad, modes, gates, query_weight, mixer_weight, output_weight, inner_weight, outer_weight, query_momentum, query_average, mixer_momentum, mixer_average, output_momentum, output_average, inner_momentum, inner_average, outer_momentum, outer_average):
    params = (query_weight, mixer_weight, output_weight, inner_weight, outer_weight)
    group = WIN_DEV * 8
    block_count = WINDOWS // group

    def one_block(carry, block_number):
        start = (block_number * group).astype(jnp.int32)
        inputs_block = lax.dynamic_slice_in_dim(inputs, start, group, 0)
        grads_block = lax.dynamic_slice_in_dim(out_grad, start, group, 0)
        picks_block = lax.dynamic_slice_in_dim(gates, start, group, 1)

        def local_forward(param_set, inputs_here):
            return forward(param_set, inputs_here, modes, picks_block)
        result, pullback = jax.vjp(local_forward, params, inputs_block)
        param_grads, inputs_grad = pullback(grads_block)
        carry = jax.tree.map(lambda total, part: total + part, carry, param_grads)
        return (carry, (result, inputs_grad))
    zeros = jax.tree.map(jnp.zeros_like, params)
    totals, (outputs, input_grads) = lax.scan(one_block, zeros, jnp.arange(block_count, dtype=jnp.int32))
    outputs = outputs.reshape(WINDOWS, L, D)
    input_grads = input_grads.reshape(WINDOWS, L, D)
    token_total = WINDOWS * L
    spreads = (D ** (-0.5), mixer_spread, D ** (-0.5), D ** (-0.5), FF ** (-0.5))
    moments = (query_momentum, mixer_momentum, output_momentum, inner_momentum, outer_momentum)
    averages = (query_average, mixer_average, output_average, inner_average, outer_average)
    results = []
    for weight, grad, momentum, average, spread in zip(params, totals, moments, averages, spreads):
        rate = 0.5 * spread / math.sqrt(token_total)
        new_momentum = momentum_decay * momentum + grad
        new_weight = weight - rate * (grad + momentum_decay * new_momentum)
        new_average = average_decay * average + (1 - average_decay) * new_weight
        results.append((new_momentum, new_weight, new_average))
    return (outputs, input_grads, results[0][0], results[0][1], results[0][2], results[1][0], results[1][1], results[1][2], results[2][0], results[2][1], results[2][2], results[3][0], results[3][1], results[3][2], results[4][0], results[4][1], results[4][2])
```

```python
import math

import jax
import jax.numpy as jnp
import numpy as np
from jax import lax
from jax.sharding import PartitionSpec as P

D = 512
FF = 2048


highest = lax.Precision.HIGHEST
pool_sizes = (7, 12, 14, 24, 48)
mixer_spread = 0.07
momentum_decay = 0.9
average_decay = 0.9


def pool_tables(length):
    tables = np.zeros((len(pool_sizes), length, length), np.float32)
    rows_all = np.arange(length)
    for pool_index, pool_width in enumerate(pool_sizes):
        lead_pad = (pool_width - 1) // 2
        for offset in range(pool_width):
            source = np.clip(rows_all - lead_pad + offset, 0, length - 1)
            tables[pool_index][rows_all, source] += np.float32(1.0 / pool_width)
    return jnp.asarray(tables)


def spectral_tables(modes, length):
    positions = jnp.arange(length, dtype=jnp.int32)
    phase = modes[:, :, None] * positions[None, None, :] % length
    angle = phase.astype(jnp.float32) * (2.0 * math.pi / length)
    cosine = jnp.cos(angle)
    sine = jnp.sin(angle)
    doubled = jnp.where((modes == 0) | (2 * modes == length), 1.0, 2.0).astype(jnp.float32) / length
    inv_cos = jnp.transpose(doubled[:, :, None] * cosine, (0, 2, 1))
    inv_sin = jnp.transpose(-doubled[:, :, None] * sine, (0, 2, 1))
    return (cosine, -sine, inv_cos, inv_sin)


def product(form, left, right):
    return jnp.einsum(form, left, right, preferred_element_type=jnp.float32)


def trend_local(values, picks, pools):
    total = jnp.zeros_like(values)
    for pool_index in range(len(pool_sizes)):
        chosen = (picks == pool_index).astype(jnp.float32)[..., None]
        total = total + chosen * jnp.einsum(
            "ts,wsd->wtd", pools[pool_index], values, precision=highest
        )
    return total


def trend_back(grads, picks, pools):
    total = jnp.zeros_like(grads)
    for pool_index in range(len(pool_sizes)):
        chosen = (picks == pool_index).astype(jnp.float32)[..., None]
        total = total + jnp.einsum(
            "ts,wtd->wsd", pools[pool_index], chosen * grads, precision=highest
        )
    return total


def mixer_block(mixer_low, head_size):
    head_count = mixer_low.shape[0]
    shaped = mixer_low.reshape(head_count, -1, head_size, 2 * head_size)
    real_part = shaped[..., :head_size]
    imag_part = shaped[..., head_size:]
    upper = jnp.concatenate([real_part, imag_part], axis=-1)
    lower = jnp.concatenate([-imag_part, real_part], axis=-1)
    return jnp.concatenate([upper, lower], axis=2)


def exact_gelu(values):
    return jax.nn.gelu(values, approximate=False)


def on_device(
    inputs,
    out_grad,
    modes,
    gates,
    query_weight,
    mixer_weight,
    output_weight,
    inner_weight,
    outer_weight,
    query_momentum,
    query_average,
    mixer_momentum,
    mixer_average,
    output_momentum,
    output_average,
    inner_momentum,
    inner_average,
    outer_momentum,
    outer_average,
):
    windows, length, local_width = inputs.shape
    head_count, mode_count = modes.shape
    head_size = local_width // head_count
    hidden_width = inner_weight.shape[1]
    head_parts = lax.axis_size("head")
    me = lax.axis_index("head")
    shifts = list(range(1, head_parts))

    def peer(shift):
        return (me + shift) % head_parts

    def swap(values, shift):
        pairs = [(j, (j + shift) % head_parts) for j in range(head_parts)]
        return lax.ppermute(values, "head", pairs)

    def rows_of(weight, block, size):
        return lax.dynamic_slice_in_dim(weight, block * size, size, 0)

    def cols_of(weight, block, size):
        return lax.dynamic_slice_in_dim(weight, block * size, size, 1)

    def gathered_product(mine, weight_low, size):
        received = {s: swap(mine, s) for s in shifts}
        total = product("wtd,de->wte", mine, rows_of(weight_low, me, size))
        for s in shifts:
            owner = (me - s) % head_parts
            total = total + product("wtd,de->wte", received[s], rows_of(weight_low, owner, size))
        return total, received

    def scattered_product(values, weight_low, size):
        sent = {
            s: swap(product("wte,ed->wtd", values, cols_of(weight_low, peer(s), size)).astype(jnp.bfloat16), s)
            for s in shifts
        }
        total = product("wte,ed->wtd", values, cols_of(weight_low, me, size))
        for s in shifts:
            total = total + sent[s].astype(jnp.float32)
        return total

    def placed_rows(parts, size, total_rows):
        out = jnp.zeros((total_rows,) + parts[0][1].shape[1:], jnp.float32)
        for block, part in parts:
            out = lax.dynamic_update_slice_in_dim(out, part, block * size, 0)
        return out

    def placed_cols(parts, size, total_cols):
        out = jnp.zeros(parts[0][1].shape[:1] + (total_cols,), jnp.float32)
        for block, part in parts:
            out = lax.dynamic_update_slice_in_dim(out, part, block * size, 1)
        return out

    model_width = local_width * head_parts
    pools = pool_tables(length)
    fwd_cos, fwd_sin, inv_cos, inv_sin = [
        one_table.astype(jnp.bfloat16) for one_table in spectral_tables(modes, length)
    ]
    query_low = query_weight.astype(jnp.bfloat16)
    output_low = output_weight.astype(jnp.bfloat16)
    inner_low = inner_weight.astype(jnp.bfloat16)
    outer_low = outer_weight.astype(jnp.bfloat16)
    block = mixer_block(mixer_weight.astype(jnp.bfloat16), head_size)

    grad_comb = out_grad - trend_back(out_grad, gates[1], pools)
    grad_feed_mine = grad_comb.astype(jnp.bfloat16)
    grad_feed_recv = {s: swap(grad_feed_mine, s) for s in shifts}

    inputs_mine = inputs.astype(jnp.bfloat16)
    query, inputs_recv = gathered_product(inputs_mine, query_low, local_width)
    query = query.astype(jnp.bfloat16)
    query_heads = query.reshape(windows, length, head_count, head_size)
    spectrum = jnp.concatenate(
        [
            product("hmt,wthe->whme", fwd_cos, query_heads),
            product("hmt,wthe->whme", fwd_sin, query_heads),
        ],
        axis=-1,
    ).astype(jnp.bfloat16)
    mixed = product("whmi,hmio->whmo", spectrum, block).astype(jnp.bfloat16)
    field = product("htm,whme->wthe", inv_cos, mixed[..., :head_size]) + product(
        "htm,whme->wthe", inv_sin, mixed[..., head_size:]
    )
    field = field.reshape(windows, length, local_width).astype(jnp.bfloat16)
    attended = scattered_product(field, output_low, local_width)
    resid_one = inputs + attended
    seasonal = resid_one - trend_local(resid_one, gates[0], pools)
    seasonal_mine = seasonal.astype(jnp.bfloat16)
    pre, seasonal_recv = gathered_product(seasonal_mine, inner_low, local_width)
    activated, gelu_pull = jax.vjp(exact_gelu, pre)
    hidden = activated.astype(jnp.bfloat16)
    feed = scattered_product(hidden, outer_low, local_width)
    combined = seasonal + feed
    output = combined - trend_local(combined, gates[1], pools)

    outer_grad = placed_cols(
        [(me, product("wtf,wtd->fd", hidden, grad_feed_mine))]
        + [((me - s) % head_parts, product("wtf,wtd->fd", hidden, grad_feed_recv[s])) for s in shifts],
        local_width,
        model_width,
    )
    grad_hidden = product("wtd,fd->wtf", grad_feed_mine, cols_of(outer_low, me, local_width))
    for s in shifts:
        grad_hidden = grad_hidden + product(
            "wtd,fd->wtf", grad_feed_recv[s], cols_of(outer_low, (me - s) % head_parts, local_width)
        )
    grad_pre = gelu_pull(grad_hidden)[0].astype(jnp.bfloat16)
    inner_grad = placed_rows(
        [(me, product("wtd,wtf->df", seasonal_mine, grad_pre))]
        + [((me - s) % head_parts, product("wtd,wtf->df", seasonal_recv[s], grad_pre)) for s in shifts],
        local_width,
        model_width,
    )
    inner_t = jnp.transpose(inner_low)
    grad_season = grad_comb + scattered_product(grad_pre, inner_t, local_width)
    grad_resid = grad_season - trend_back(grad_season, gates[0], pools)
    grad_attend_mine = grad_resid.astype(jnp.bfloat16)
    grad_attend_recv = {s: swap(grad_attend_mine, s) for s in shifts}
    output_grad = placed_cols(
        [(me, product("wte,wtd->ed", field, grad_attend_mine))]
        + [((me - s) % head_parts, product("wte,wtd->ed", field, grad_attend_recv[s])) for s in shifts],
        local_width,
        model_width,
    )
    grad_field = product("wtd,ed->wte", grad_attend_mine, cols_of(output_low, me, local_width))
    for s in shifts:
        grad_field = grad_field + product(
            "wtd,ed->wte", grad_attend_recv[s], cols_of(output_low, (me - s) % head_parts, local_width)
        )
    grad_field = grad_field.astype(jnp.bfloat16)
    grad_field = grad_field.reshape(windows, length, head_count, head_size)
    grad_mixed = jnp.concatenate(
        [
            product("htm,wthe->whme", inv_cos, grad_field),
            product("htm,wthe->whme", inv_sin, grad_field),
        ],
        axis=-1,
    ).astype(jnp.bfloat16)
    grad_spectrum = product("whmo,hmio->whmi", grad_mixed, block).astype(jnp.bfloat16)
    grad_query = product("hmt,whme->wthe", fwd_cos, grad_spectrum[..., :head_size]) + product(
        "hmt,whme->wthe", fwd_sin, grad_spectrum[..., head_size:]
    )
    grad_query = grad_query.reshape(windows, length, local_width).astype(jnp.bfloat16)
    query_grad = placed_rows(
        [(me, product("wtd,wte->de", inputs_mine, grad_query))]
        + [((me - s) % head_parts, product("wtd,wte->de", inputs_recv[s], grad_query)) for s in shifts],
        local_width,
        model_width,
    )
    query_t = jnp.transpose(query_low)
    input_grad = grad_resid + scattered_product(grad_query, query_t, local_width)
    block_grad = product("whmi,whmo->hmio", spectrum, grad_mixed)
    real_grad = block_grad[:, :, :head_size, :head_size] + block_grad[:, :, head_size:, head_size:]
    imag_grad = block_grad[:, :, :head_size, head_size:] - block_grad[:, :, head_size:, :head_size]
    mixer_full = jnp.concatenate([real_grad, imag_grad], axis=-1).reshape(
        head_count, mode_count * head_size, 2 * head_size
    )

    dp_count = lax.axis_size("dp")
    dp_rank = lax.axis_index("dp")

    def lead(grad, axis_number):
        shape = grad.shape
        split = shape[:axis_number] + (dp_count, shape[axis_number] // dp_count) + shape[axis_number + 1 :]
        owned_shape = shape[:axis_number] + (shape[axis_number] // dp_count,) + shape[axis_number + 1 :]
        return jnp.moveaxis(grad.reshape(split), axis_number, 0).reshape(dp_count, -1), owned_shape

    laid = [
        lead(query_grad, 0),
        lead(mixer_full, 1),
        lead(output_grad, 1),
        lead(inner_grad, 0),
        lead(outer_grad, 1),
    ]
    joined = jnp.concatenate([flat for flat, _ in laid], axis=1)
    lanes = 128
    reduced = lax.psum_scatter(
        joined.reshape(-1, lanes), "dp", scatter_dimension=0, tiled=True
    ).reshape(-1)
    parts = []
    offset = 0
    for flat, owned_shape in laid:
        size = flat.shape[1]
        parts.append(reduced[offset : offset + size].reshape(owned_shape))
        offset += size
    query_part, mixer_part, output_part, inner_part, outer_part = parts
    token_total = windows * length * dp_count

    def owned(weight, share, axis_number):
        return lax.dynamic_slice_in_dim(weight, dp_rank * share, share, axis_number)

    def stepped(grad, momentum, average, old_weight, spread):
        rate = 0.5 * spread / math.sqrt(token_total)
        new_momentum = momentum_decay * momentum + grad
        new_weight = old_weight - rate * (grad + momentum_decay * new_momentum)
        new_average = average_decay * average + (1 - average_decay) * new_weight
        return (new_momentum, new_weight, new_average)

    query_new = stepped(
        query_part,
        query_momentum,
        query_average,
        owned(query_weight, query_momentum.shape[0], 0),
        D ** (-0.5),
    )
    mixer_new = stepped(
        mixer_part,
        mixer_momentum,
        mixer_average,
        owned(mixer_weight, mixer_momentum.shape[1], 1),
        mixer_spread,
    )
    output_new = stepped(
        output_part,
        output_momentum,
        output_average,
        owned(output_weight, output_momentum.shape[1], 1),
        D ** (-0.5),
    )
    inner_new = stepped(
        inner_part,
        inner_momentum,
        inner_average,
        owned(inner_weight, inner_momentum.shape[0], 0),
        D ** (-0.5),
    )
    outer_new = stepped(
        outer_part,
        outer_momentum,
        outer_average,
        owned(outer_weight, outer_momentum.shape[1], 1),
        FF ** (-0.5),
    )
    return (
        output,
        input_grad,
        query_new[0],
        query_new[1],
        query_new[2],
        mixer_new[0],
        mixer_new[1],
        mixer_new[2],
        output_new[0],
        output_new[1],
        output_new[2],
        inner_new[0],
        inner_new[1],
        inner_new[2],
        outer_new[0],
        outer_new[1],
        outer_new[2],
    )


def solution(mesh):
    return jax.shard_map(
        on_device,
        mesh=mesh,
        in_specs=(
            P("dp", None, "head"),
            P("dp", None, "head"),
            P("head", None),
            P(None, "dp", None),
            P(None, "head"),
            P("head", None, None),
            P("head", None),
            P(None, "head"),
            P("head", None),
            P("dp", "head"),
            P("dp", "head"),
            P("head", "dp", None),
            P("head", "dp", None),
            P("head", "dp"),
            P("head", "dp"),
            P("dp", "head"),
            P("dp", "head"),
            P("head", "dp"),
            P("head", "dp"),
        ),
        out_specs=(
            P("dp", None, "head"),
            P("dp", None, "head"),
            P("dp", "head"),
            P("dp", "head"),
            P("dp", "head"),
            P("head", "dp", None),
            P("head", "dp", None),
            P("head", "dp", None),
            P("head", "dp"),
            P("head", "dp"),
            P("head", "dp"),
            P("dp", "head"),
            P("dp", "head"),
            P("dp", "head"),
            P("head", "dp"),
            P("head", "dp"),
            P("head", "dp"),
        ),
        check_vma=False,
    )
```

```python
import math

import jax
import jax.numpy as jnp
import numpy as np
from jax import lax
from jax.sharding import PartitionSpec as P

D = 512
FF = 2048


highest = lax.Precision.HIGHEST
pool_sizes = (7, 12, 14, 24, 48)
mixer_spread = 0.07
momentum_decay = 0.9
average_decay = 0.9


def pool_tables(length):
    tables = np.zeros((len(pool_sizes), length, length), np.float32)
    rows_all = np.arange(length)
    for pool_index, pool_width in enumerate(pool_sizes):
        lead_pad = (pool_width - 1) // 2
        for offset in range(pool_width):
            source = np.clip(rows_all - lead_pad + offset, 0, length - 1)
            tables[pool_index][rows_all, source] += np.float32(1.0 / pool_width)
    return jnp.asarray(tables)


def spectral_tables(modes, length):
    positions = jnp.arange(length, dtype=jnp.int32)
    phase = modes[:, :, None] * positions[None, None, :] % length
    angle = phase.astype(jnp.float32) * (2.0 * math.pi / length)
    cosine = jnp.cos(angle)
    sine = jnp.sin(angle)
    doubled = jnp.where((modes == 0) | (2 * modes == length), 1.0, 2.0).astype(jnp.float32) / length
    inv_cos = jnp.transpose(doubled[:, :, None] * cosine, (0, 2, 1))
    inv_sin = jnp.transpose(-doubled[:, :, None] * sine, (0, 2, 1))
    return (cosine, -sine, inv_cos, inv_sin)


def product(form, left, right):
    return jnp.einsum(form, left, right, preferred_element_type=jnp.float32)


def pool_rows(picks, pools):
    rows = jnp.zeros(picks.shape + (pools.shape[-1],), jnp.float32)
    for pool_index in range(len(pool_sizes)):
        rows = jnp.where((picks == pool_index)[..., None], pools[pool_index][None], rows)
    return rows


def trend_local(values, rows):
    return jnp.einsum("wts,wsd->wtd", rows, values, precision=highest)


def trend_back(grads, rows):
    return jnp.einsum("wts,wtd->wsd", rows, grads, precision=highest)


def mixer_block(mixer_low, head_size):
    head_count = mixer_low.shape[0]
    shaped = mixer_low.reshape(head_count, -1, head_size, 2 * head_size)
    real_part = shaped[..., :head_size]
    imag_part = shaped[..., head_size:]
    upper = jnp.concatenate([real_part, imag_part], axis=-1)
    lower = jnp.concatenate([-imag_part, real_part], axis=-1)
    return jnp.concatenate([upper, lower], axis=2)


def exact_gelu(values):
    return jax.nn.gelu(values, approximate=False)


def on_device(
    inputs,
    out_grad,
    modes,
    gates,
    query_weight,
    mixer_weight,
    output_weight,
    inner_weight,
    outer_weight,
    query_momentum,
    query_average,
    mixer_momentum,
    mixer_average,
    output_momentum,
    output_average,
    inner_momentum,
    inner_average,
    outer_momentum,
    outer_average,
):
    windows, length, local_width = inputs.shape
    head_count, mode_count = modes.shape
    head_size = local_width // head_count
    hidden_width = inner_weight.shape[1]
    head_parts = lax.axis_size("head")
    me = lax.axis_index("head")
    shifts = list(range(1, head_parts))

    def peer(shift):
        return (me + shift) % head_parts

    def swap(values, shift):
        pairs = [(j, (j + shift) % head_parts) for j in range(head_parts)]
        return lax.ppermute(values, "head", pairs)

    def rows_of(weight, block, size):
        return lax.dynamic_slice_in_dim(weight, block * size, size, 0)

    def cols_of(weight, block, size):
        return lax.dynamic_slice_in_dim(weight, block * size, size, 1)

    def gathered_product(mine, weight_low, size):
        received = {s: swap(mine, s) for s in shifts}
        total = product("wtd,de->wte", mine, rows_of(weight_low, me, size))
        for s in shifts:
            owner = (me - s) % head_parts
            total = total + product("wtd,de->wte", received[s], rows_of(weight_low, owner, size))
        return total, received

    def scattered_product(values, weight_low, size):
        sent = {
            s: swap(product("wte,ed->wtd", values, cols_of(weight_low, peer(s), size)).astype(jnp.bfloat16), s)
            for s in shifts
        }
        total = product("wte,ed->wtd", values, cols_of(weight_low, me, size))
        for s in shifts:
            total = total + sent[s].astype(jnp.float32)
        return total

    def placed_rows(parts, size, total_rows):
        out = jnp.zeros((total_rows,) + parts[0][1].shape[1:], jnp.float32)
        for block, part in parts:
            out = lax.dynamic_update_slice_in_dim(out, part, block * size, 0)
        return out

    def placed_cols(parts, size, total_cols):
        out = jnp.zeros(parts[0][1].shape[:1] + (total_cols,), jnp.float32)
        for block, part in parts:
            out = lax.dynamic_update_slice_in_dim(out, part, block * size, 1)
        return out

    model_width = local_width * head_parts
    pools = pool_tables(length)
    fwd_cos, fwd_sin, inv_cos, inv_sin = [
        one_table.astype(jnp.bfloat16) for one_table in spectral_tables(modes, length)
    ]
    query_low = query_weight.astype(jnp.bfloat16)
    output_low = output_weight.astype(jnp.bfloat16)
    inner_low = inner_weight.astype(jnp.bfloat16)
    outer_low = outer_weight.astype(jnp.bfloat16)
    inner_t = jnp.transpose(inner_low)
    query_t = jnp.transpose(query_low)
    block = mixer_block(mixer_weight.astype(jnp.bfloat16), head_size)

    def chunk_pass(inputs, out_grad, first_rows, second_rows):
        windows = inputs.shape[0]
        grad_comb = out_grad - trend_back(out_grad, second_rows)
        grad_feed_mine = grad_comb.astype(jnp.bfloat16)
        grad_feed_recv = {s: swap(grad_feed_mine, s) for s in shifts}

        inputs_mine = inputs.astype(jnp.bfloat16)
        query, inputs_recv = gathered_product(inputs_mine, query_low, local_width)
        query = query.astype(jnp.bfloat16)
        query_heads = query.reshape(windows, length, head_count, head_size)
        spectrum = jnp.concatenate(
            [
                product("hmt,wthe->whme", fwd_cos, query_heads),
                product("hmt,wthe->whme", fwd_sin, query_heads),
            ],
            axis=-1,
        ).astype(jnp.bfloat16)
        mixed = product("whmi,hmio->whmo", spectrum, block).astype(jnp.bfloat16)
        field = product("htm,whme->wthe", inv_cos, mixed[..., :head_size]) + product(
            "htm,whme->wthe", inv_sin, mixed[..., head_size:]
        )
        field = field.reshape(windows, length, local_width).astype(jnp.bfloat16)
        attended = scattered_product(field, output_low, local_width)
        resid_one = inputs + attended
        seasonal = resid_one - trend_local(resid_one, first_rows)
        seasonal_mine = seasonal.astype(jnp.bfloat16)
        pre, seasonal_recv = gathered_product(seasonal_mine, inner_low, local_width)
        activated, gelu_pull = jax.vjp(exact_gelu, pre)
        hidden = activated.astype(jnp.bfloat16)
        feed = scattered_product(hidden, outer_low, local_width)
        combined = seasonal + feed
        output = combined - trend_local(combined, second_rows)

        outer_grad = placed_cols(
            [(me, product("wtf,wtd->fd", hidden, grad_feed_mine))]
            + [((me - s) % head_parts, product("wtf,wtd->fd", hidden, grad_feed_recv[s])) for s in shifts],
            local_width,
            model_width,
        )
        grad_hidden = product("wtd,fd->wtf", grad_feed_mine, cols_of(outer_low, me, local_width))
        for s in shifts:
            grad_hidden = grad_hidden + product(
                "wtd,fd->wtf", grad_feed_recv[s], cols_of(outer_low, (me - s) % head_parts, local_width)
            )
        grad_pre = gelu_pull(grad_hidden)[0].astype(jnp.bfloat16)
        inner_grad = placed_rows(
            [(me, product("wtd,wtf->df", seasonal_mine, grad_pre))]
            + [((me - s) % head_parts, product("wtd,wtf->df", seasonal_recv[s], grad_pre)) for s in shifts],
            local_width,
            model_width,
        )
        grad_season = grad_comb + scattered_product(grad_pre, inner_t, local_width)
        grad_resid = grad_season - trend_back(grad_season, first_rows)
        grad_attend_mine = grad_resid.astype(jnp.bfloat16)
        grad_attend_recv = {s: swap(grad_attend_mine, s) for s in shifts}
        output_grad = placed_cols(
            [(me, product("wte,wtd->ed", field, grad_attend_mine))]
            + [((me - s) % head_parts, product("wte,wtd->ed", field, grad_attend_recv[s])) for s in shifts],
            local_width,
            model_width,
        )
        grad_field = product("wtd,ed->wte", grad_attend_mine, cols_of(output_low, me, local_width))
        for s in shifts:
            grad_field = grad_field + product(
                "wtd,ed->wte", grad_attend_recv[s], cols_of(output_low, (me - s) % head_parts, local_width)
            )
        grad_field = grad_field.astype(jnp.bfloat16)
        grad_field = grad_field.reshape(windows, length, head_count, head_size)
        grad_mixed = jnp.concatenate(
            [
                product("htm,wthe->whme", inv_cos, grad_field),
                product("htm,wthe->whme", inv_sin, grad_field),
            ],
            axis=-1,
        ).astype(jnp.bfloat16)
        grad_spectrum = product("whmo,hmio->whmi", grad_mixed, block).astype(jnp.bfloat16)
        grad_query = product("hmt,whme->wthe", fwd_cos, grad_spectrum[..., :head_size]) + product(
            "hmt,whme->wthe", fwd_sin, grad_spectrum[..., head_size:]
        )
        grad_query = grad_query.reshape(windows, length, local_width).astype(jnp.bfloat16)
        query_grad = placed_rows(
            [(me, product("wtd,wte->de", inputs_mine, grad_query))]
            + [((me - s) % head_parts, product("wtd,wte->de", inputs_recv[s], grad_query)) for s in shifts],
            local_width,
            model_width,
        )
        input_grad = grad_resid + scattered_product(grad_query, query_t, local_width)
        block_grad = product("whmi,whmo->hmio", spectrum, grad_mixed)
        real_grad = block_grad[:, :, :head_size, :head_size] + block_grad[:, :, head_size:, head_size:]
        imag_grad = block_grad[:, :, :head_size, head_size:] - block_grad[:, :, head_size:, :head_size]
        mixer_full = jnp.concatenate([real_grad, imag_grad], axis=-1).reshape(
            head_count, mode_count * head_size, 2 * head_size
        )
        return output, input_grad, (query_grad, mixer_full, output_grad, inner_grad, outer_grad)

    chunks = 2 if windows % 2 == 0 else 1
    span = windows // chunks
    first_all = pool_rows(gates[0], pools)
    second_all = pool_rows(gates[1], pools)
    results = [
        chunk_pass(
            inputs[c * span : (c + 1) * span],
            out_grad[c * span : (c + 1) * span],
            first_all[c * span : (c + 1) * span],
            second_all[c * span : (c + 1) * span],
        )
        for c in range(chunks)
    ]
    output = jnp.concatenate([r[0] for r in results], axis=0)
    input_grad = jnp.concatenate([r[1] for r in results], axis=0)
    query_grad, mixer_full, output_grad, inner_grad, outer_grad = [
        sum(r[2][i] for r in results[1:]) + results[0][2][i] if chunks > 1 else results[0][2][i]
        for i in range(5)
    ]

    dp_count = lax.axis_size("dp")
    dp_rank = lax.axis_index("dp")

    def lead(grad, axis_number):
        shape = grad.shape
        split = shape[:axis_number] + (dp_count, shape[axis_number] // dp_count) + shape[axis_number + 1 :]
        owned_shape = shape[:axis_number] + (shape[axis_number] // dp_count,) + shape[axis_number + 1 :]
        return jnp.moveaxis(grad.reshape(split), axis_number, 0).reshape(dp_count, -1), owned_shape

    laid = [
        lead(query_grad, 0),
        lead(mixer_full, 1),
        lead(output_grad, 1),
        lead(inner_grad, 0),
        lead(outer_grad, 1),
    ]
    joined = jnp.concatenate([flat for flat, _ in laid], axis=1)
    lanes = 128
    reduced = lax.psum_scatter(
        joined.reshape(-1, lanes), "dp", scatter_dimension=0, tiled=True
    ).reshape(-1)
    parts = []
    offset = 0
    for flat, owned_shape in laid:
        size = flat.shape[1]
        parts.append(reduced[offset : offset + size].reshape(owned_shape))
        offset += size
    query_part, mixer_part, output_part, inner_part, outer_part = parts
    token_total = windows * length * dp_count

    def owned(weight, share, axis_number):
        return lax.dynamic_slice_in_dim(weight, dp_rank * share, share, axis_number)

    def stepped(grad, momentum, average, old_weight, spread):
        rate = 0.5 * spread / math.sqrt(token_total)
        new_momentum = momentum_decay * momentum + grad
        new_weight = old_weight - rate * (grad + momentum_decay * new_momentum)
        new_average = average_decay * average + (1 - average_decay) * new_weight
        return (new_momentum, new_weight, new_average)

    query_new = stepped(
        query_part,
        query_momentum,
        query_average,
        owned(query_weight, query_momentum.shape[0], 0),
        D ** (-0.5),
    )
    mixer_new = stepped(
        mixer_part,
        mixer_momentum,
        mixer_average,
        owned(mixer_weight, mixer_momentum.shape[1], 1),
        mixer_spread,
    )
    output_new = stepped(
        output_part,
        output_momentum,
        output_average,
        owned(output_weight, output_momentum.shape[1], 1),
        D ** (-0.5),
    )
    inner_new = stepped(
        inner_part,
        inner_momentum,
        inner_average,
        owned(inner_weight, inner_momentum.shape[0], 0),
        D ** (-0.5),
    )
    outer_new = stepped(
        outer_part,
        outer_momentum,
        outer_average,
        owned(outer_weight, outer_momentum.shape[1], 1),
        FF ** (-0.5),
    )
    return (
        output,
        input_grad,
        query_new[0],
        query_new[1],
        query_new[2],
        mixer_new[0],
        mixer_new[1],
        mixer_new[2],
        output_new[0],
        output_new[1],
        output_new[2],
        inner_new[0],
        inner_new[1],
        inner_new[2],
        outer_new[0],
        outer_new[1],
        outer_new[2],
    )


def solution(mesh):
    return jax.shard_map(
        on_device,
        mesh=mesh,
        in_specs=(
            P("dp", None, "head"),
            P("dp", None, "head"),
            P("head", None),
            P(None, "dp", None),
            P(None, "head"),
            P("head", None, None),
            P("head", None),
            P(None, "head"),
            P("head", None),
            P("dp", "head"),
            P("dp", "head"),
            P("head", "dp", None),
            P("head", "dp", None),
            P("head", "dp"),
            P("head", "dp"),
            P("dp", "head"),
            P("dp", "head"),
            P("head", "dp"),
            P("head", "dp"),
        ),
        out_specs=(
            P("dp", None, "head"),
            P("dp", None, "head"),
            P("dp", "head"),
            P("dp", "head"),
            P("dp", "head"),
            P("head", "dp", None),
            P("head", "dp", None),
            P("head", "dp", None),
            P("head", "dp"),
            P("head", "dp"),
            P("head", "dp"),
            P("dp", "head"),
            P("dp", "head"),
            P("dp", "head"),
            P("head", "dp"),
            P("head", "dp"),
            P("head", "dp"),
        ),
        check_vma=False,
    )
```

```python
import math

import jax
import jax.numpy as jnp
import numpy as np
from jax import lax
from jax.sharding import PartitionSpec as P

D = 512
FF = 2048


highest = lax.Precision.HIGHEST
pool_sizes = (7, 12, 14, 24, 48)
mixer_spread = 0.07
momentum_decay = 0.9
average_decay = 0.9


def pool_tables(length):
    tables = np.zeros((len(pool_sizes), length, length), np.float32)
    rows_all = np.arange(length)
    for pool_index, pool_width in enumerate(pool_sizes):
        lead_pad = (pool_width - 1) // 2
        for offset in range(pool_width):
            source = np.clip(rows_all - lead_pad + offset, 0, length - 1)
            tables[pool_index][rows_all, source] += np.float32(1.0 / pool_width)
    return jnp.asarray(tables)


def spectral_tables(modes, length):
    positions = jnp.arange(length, dtype=jnp.int32)
    phase = modes[:, :, None] * positions[None, None, :] % length
    angle = phase.astype(jnp.float32) * (2.0 * math.pi / length)
    cosine = jnp.cos(angle)
    sine = jnp.sin(angle)
    doubled = jnp.where((modes == 0) | (2 * modes == length), 1.0, 2.0).astype(jnp.float32) / length
    inv_cos = jnp.transpose(doubled[:, :, None] * cosine, (0, 2, 1))
    inv_sin = jnp.transpose(-doubled[:, :, None] * sine, (0, 2, 1))
    return (cosine, -sine, inv_cos, inv_sin)


def product(form, left, right):
    return jnp.einsum(form, left, right, preferred_element_type=jnp.float32)


def pool_rows(picks, pools):
    rows = jnp.zeros(picks.shape + (pools.shape[-1],), jnp.float32)
    for pool_index in range(len(pool_sizes)):
        rows = jnp.where((picks == pool_index)[..., None], pools[pool_index][None], rows)
    return rows


def trend_local(values, rows):
    return jnp.einsum("wts,wsd->wtd", rows, values, precision=highest)


def trend_back(grads, rows):
    return jnp.einsum("wts,wtd->wsd", rows, grads, precision=highest)


def mixer_block(mixer_low, head_size):
    head_count = mixer_low.shape[0]
    shaped = mixer_low.reshape(head_count, -1, head_size, 2 * head_size)
    real_part = shaped[..., :head_size]
    imag_part = shaped[..., head_size:]
    upper = jnp.concatenate([real_part, imag_part], axis=-1)
    lower = jnp.concatenate([-imag_part, real_part], axis=-1)
    return jnp.concatenate([upper, lower], axis=2)


def exact_gelu(values):
    return jax.nn.gelu(values, approximate=False)


def on_device(
    inputs,
    out_grad,
    modes,
    gates,
    query_weight,
    mixer_weight,
    output_weight,
    inner_weight,
    outer_weight,
    query_momentum,
    query_average,
    mixer_momentum,
    mixer_average,
    output_momentum,
    output_average,
    inner_momentum,
    inner_average,
    outer_momentum,
    outer_average,
):
    windows, length, local_width = inputs.shape
    head_count, mode_count = modes.shape
    head_size = local_width // head_count
    hidden_width = inner_weight.shape[1]
    head_parts = lax.axis_size("head")
    me = lax.axis_index("head")
    shifts = list(range(1, head_parts))

    def peer(shift):
        return (me + shift) % head_parts

    def swap(values, shift):
        pairs = [(j, (j + shift) % head_parts) for j in range(head_parts)]
        return lax.ppermute(values, "head", pairs)

    def rows_of(weight, block, size):
        return lax.dynamic_slice_in_dim(weight, block * size, size, 0)

    def cols_of(weight, block, size):
        return lax.dynamic_slice_in_dim(weight, block * size, size, 1)

    def gathered_product(mine, weight_low, size):
        received = {s: swap(mine, s) for s in shifts}
        total = product("wtd,de->wte", mine, rows_of(weight_low, me, size))
        for s in shifts:
            owner = (me - s) % head_parts
            total = total + product("wtd,de->wte", received[s], rows_of(weight_low, owner, size))
        return total, received

    def scattered_product(values, weight_low, size):
        sent = {
            s: swap(product("wte,ed->wtd", values, cols_of(weight_low, peer(s), size)).astype(jnp.bfloat16), s)
            for s in shifts
        }
        total = product("wte,ed->wtd", values, cols_of(weight_low, me, size))
        for s in shifts:
            total = total + sent[s].astype(jnp.float32)
        return total

    def placed_rows(parts, size, total_rows):
        out = jnp.zeros((total_rows,) + parts[0][1].shape[1:], jnp.float32)
        for block, part in parts:
            out = lax.dynamic_update_slice_in_dim(out, part, block * size, 0)
        return out

    def placed_cols(parts, size, total_cols):
        out = jnp.zeros(parts[0][1].shape[:1] + (total_cols,), jnp.float32)
        for block, part in parts:
            out = lax.dynamic_update_slice_in_dim(out, part, block * size, 1)
        return out

    model_width = local_width * head_parts
    pools = pool_tables(length)
    fwd_cos, fwd_sin, inv_cos, inv_sin = [
        one_table.astype(jnp.bfloat16) for one_table in spectral_tables(modes, length)
    ]
    query_low = query_weight.astype(jnp.bfloat16)
    output_low = output_weight.astype(jnp.bfloat16)
    inner_low = inner_weight.astype(jnp.bfloat16)
    outer_low = outer_weight.astype(jnp.bfloat16)
    inner_t = jnp.transpose(inner_low)
    query_t = jnp.transpose(query_low)
    block = mixer_block(mixer_weight.astype(jnp.bfloat16), head_size)

    def chunk_pass(inputs, out_grad, first_rows, second_rows):
        windows = inputs.shape[0]
        grad_comb = out_grad - trend_back(out_grad, second_rows)
        grad_feed_mine = grad_comb.astype(jnp.bfloat16)
        grad_feed_recv = {s: swap(grad_feed_mine, s) for s in shifts}

        inputs_mine = inputs.astype(jnp.bfloat16)
        query, inputs_recv = gathered_product(inputs_mine, query_low, local_width)
        query = query.astype(jnp.bfloat16)
        query_heads = query.reshape(windows, length, head_count, head_size)
        spectrum = jnp.concatenate(
            [
                product("hmt,wthe->whme", fwd_cos, query_heads),
                product("hmt,wthe->whme", fwd_sin, query_heads),
            ],
            axis=-1,
        ).astype(jnp.bfloat16)
        mixed = product("whmi,hmio->whmo", spectrum, block).astype(jnp.bfloat16)
        field = product("htm,whme->wthe", inv_cos, mixed[..., :head_size]) + product(
            "htm,whme->wthe", inv_sin, mixed[..., head_size:]
        )
        field = field.reshape(windows, length, local_width).astype(jnp.bfloat16)
        attended = scattered_product(field, output_low, local_width)
        resid_one = inputs + attended
        seasonal = resid_one - trend_local(resid_one, first_rows)
        seasonal_mine = seasonal.astype(jnp.bfloat16)
        pre, seasonal_recv = gathered_product(seasonal_mine, inner_low, local_width)
        activated, gelu_pull = jax.vjp(exact_gelu, pre)
        hidden = activated.astype(jnp.bfloat16)
        feed = scattered_product(hidden, outer_low, local_width)
        combined = seasonal + feed
        output = combined - trend_local(combined, second_rows)

        outer_grad_t = placed_rows(
            [(me, product("wtd,wtf->df", grad_feed_mine, hidden))]
            + [((me - s) % head_parts, product("wtd,wtf->df", grad_feed_recv[s], hidden)) for s in shifts],
            local_width,
            model_width,
        )
        grad_hidden = product("wtd,fd->wtf", grad_feed_mine, cols_of(outer_low, me, local_width))
        for s in shifts:
            grad_hidden = grad_hidden + product(
                "wtd,fd->wtf", grad_feed_recv[s], cols_of(outer_low, (me - s) % head_parts, local_width)
            )
        grad_pre = gelu_pull(grad_hidden)[0].astype(jnp.bfloat16)
        inner_grad = placed_rows(
            [(me, product("wtd,wtf->df", seasonal_mine, grad_pre))]
            + [((me - s) % head_parts, product("wtd,wtf->df", seasonal_recv[s], grad_pre)) for s in shifts],
            local_width,
            model_width,
        )
        grad_season = grad_comb + scattered_product(grad_pre, inner_t, local_width)
        grad_resid = grad_season - trend_back(grad_season, first_rows)
        grad_attend_mine = grad_resid.astype(jnp.bfloat16)
        grad_attend_recv = {s: swap(grad_attend_mine, s) for s in shifts}
        output_grad_t = placed_rows(
            [(me, product("wtd,wte->de", grad_attend_mine, field))]
            + [((me - s) % head_parts, product("wtd,wte->de", grad_attend_recv[s], field)) for s in shifts],
            local_width,
            model_width,
        )
        grad_field = product("wtd,ed->wte", grad_attend_mine, cols_of(output_low, me, local_width))
        for s in shifts:
            grad_field = grad_field + product(
                "wtd,ed->wte", grad_attend_recv[s], cols_of(output_low, (me - s) % head_parts, local_width)
            )
        grad_field = grad_field.astype(jnp.bfloat16)
        grad_field = grad_field.reshape(windows, length, head_count, head_size)
        grad_mixed = jnp.concatenate(
            [
                product("htm,wthe->whme", inv_cos, grad_field),
                product("htm,wthe->whme", inv_sin, grad_field),
            ],
            axis=-1,
        ).astype(jnp.bfloat16)
        grad_spectrum = product("whmo,hmio->whmi", grad_mixed, block).astype(jnp.bfloat16)
        grad_query = product("hmt,whme->wthe", fwd_cos, grad_spectrum[..., :head_size]) + product(
            "hmt,whme->wthe", fwd_sin, grad_spectrum[..., head_size:]
        )
        grad_query = grad_query.reshape(windows, length, local_width).astype(jnp.bfloat16)
        query_grad = placed_rows(
            [(me, product("wtd,wte->de", inputs_mine, grad_query))]
            + [((me - s) % head_parts, product("wtd,wte->de", inputs_recv[s], grad_query)) for s in shifts],
            local_width,
            model_width,
        )
        input_grad = grad_resid + scattered_product(grad_query, query_t, local_width)
        spectrum_parts = spectrum.reshape(windows, head_count, mode_count, 2, head_size)
        grad_real = grad_mixed[..., :head_size]
        grad_imag = grad_mixed[..., head_size:]
        paired = jnp.stack(
            [grad_mixed, jnp.concatenate([grad_imag, -grad_real], axis=-1)], axis=3
        )
        mixer_full = product("whmci,whmco->hmio", spectrum_parts, paired).reshape(
            head_count, mode_count * head_size, 2 * head_size
        )
        return output, input_grad, (query_grad, mixer_full, output_grad_t, inner_grad, outer_grad_t)

    chunks = 2 if windows % 2 == 0 else 1
    span = windows // chunks
    first_all = pool_rows(gates[0], pools)
    second_all = pool_rows(gates[1], pools)
    results = [
        chunk_pass(
            inputs[c * span : (c + 1) * span],
            out_grad[c * span : (c + 1) * span],
            first_all[c * span : (c + 1) * span],
            second_all[c * span : (c + 1) * span],
        )
        for c in range(chunks)
    ]
    output = jnp.concatenate([r[0] for r in results], axis=0)
    input_grad = jnp.concatenate([r[1] for r in results], axis=0)
    query_grad, mixer_full, output_grad_t, inner_grad, outer_grad_t = [
        sum(r[2][i] for r in results[1:]) + results[0][2][i] if chunks > 1 else results[0][2][i]
        for i in range(5)
    ]

    dp_count = lax.axis_size("dp")
    dp_rank = lax.axis_index("dp")

    lanes = 128

    def lead(grad, axis_number):
        shape = grad.shape
        split = shape[:axis_number] + (dp_count, shape[axis_number] // dp_count) + shape[axis_number + 1 :]
        owned_shape = shape[:axis_number] + (shape[axis_number] // dp_count,) + shape[axis_number + 1 :]
        return jnp.moveaxis(grad.reshape(split), axis_number, 0).reshape(dp_count, -1, lanes), owned_shape

    def reduced_over_dp(grads_axes):
        laid = [lead(grad, axis_number) for grad, axis_number in grads_axes]
        joined = jnp.concatenate([flat for flat, _ in laid], axis=1)
        reduced = lax.psum_scatter(
            joined.reshape(-1, lanes), "dp", scatter_dimension=0, tiled=True
        )
        parts = []
        offset = 0
        for flat, owned_shape in laid:
            rows = flat.shape[1]
            parts.append(reduced[offset : offset + rows].reshape(owned_shape))
            offset += rows
        return parts

    inner_part, outer_part_t = reduced_over_dp([(inner_grad, 0), (outer_grad_t, 0)])
    mixer_part, output_part_t, query_part = reduced_over_dp(
        [(mixer_full, 1), (output_grad_t, 0), (query_grad, 0)]
    )
    output_part = jnp.transpose(output_part_t)
    outer_part = jnp.transpose(outer_part_t)
    token_total = windows * length * dp_count

    def owned(weight, share, axis_number):
        return lax.dynamic_slice_in_dim(weight, dp_rank * share, share, axis_number)

    def stepped(grad, momentum, average, old_weight, spread):
        rate = 0.5 * spread / math.sqrt(token_total)
        new_momentum = momentum_decay * momentum + grad
        new_weight = old_weight - rate * (grad + momentum_decay * new_momentum)
        new_average = average_decay * average + (1 - average_decay) * new_weight
        return (new_momentum, new_weight, new_average)

    query_new = stepped(
        query_part,
        query_momentum,
        query_average,
        owned(query_weight, query_momentum.shape[0], 0),
        D ** (-0.5),
    )
    mixer_new = stepped(
        mixer_part,
        mixer_momentum,
        mixer_average,
        owned(mixer_weight, mixer_momentum.shape[1], 1),
        mixer_spread,
    )
    output_new = stepped(
        output_part,
        output_momentum,
        output_average,
        owned(output_weight, output_momentum.shape[1], 1),
        D ** (-0.5),
    )
    inner_new = stepped(
        inner_part,
        inner_momentum,
        inner_average,
        owned(inner_weight, inner_momentum.shape[0], 0),
        D ** (-0.5),
    )
    outer_new = stepped(
        outer_part,
        outer_momentum,
        outer_average,
        owned(outer_weight, outer_momentum.shape[1], 1),
        FF ** (-0.5),
    )
    return (
        output,
        input_grad,
        query_new[0],
        query_new[1],
        query_new[2],
        mixer_new[0],
        mixer_new[1],
        mixer_new[2],
        output_new[0],
        output_new[1],
        output_new[2],
        inner_new[0],
        inner_new[1],
        inner_new[2],
        outer_new[0],
        outer_new[1],
        outer_new[2],
    )


def solution(mesh):
    return jax.shard_map(
        on_device,
        mesh=mesh,
        in_specs=(
            P("dp", None, "head"),
            P("dp", None, "head"),
            P("head", None),
            P(None, "dp", None),
            P(None, "head"),
            P("head", None, None),
            P("head", None),
            P(None, "head"),
            P("head", None),
            P("dp", "head"),
            P("dp", "head"),
            P("head", "dp", None),
            P("head", "dp", None),
            P("head", "dp"),
            P("head", "dp"),
            P("dp", "head"),
            P("dp", "head"),
            P("head", "dp"),
            P("head", "dp"),
        ),
        out_specs=(
            P("dp", None, "head"),
            P("dp", None, "head"),
            P("dp", "head"),
            P("dp", "head"),
            P("dp", "head"),
            P("head", "dp", None),
            P("head", "dp", None),
            P("head", "dp", None),
            P("head", "dp"),
            P("head", "dp"),
            P("head", "dp"),
            P("dp", "head"),
            P("dp", "head"),
            P("dp", "head"),
            P("head", "dp"),
            P("head", "dp"),
            P("head", "dp"),
        ),
        check_vma=False,
    )
```

```python
import math

import jax
import jax.numpy as jnp
import numpy as np
from jax import lax
from jax.sharding import PartitionSpec as P

D = 512
FF = 2048


highest = lax.Precision.HIGHEST
pool_sizes = (7, 12, 14, 24, 48)
mixer_spread = 0.07
momentum_decay = 0.9
average_decay = 0.9


def pool_tables(length):
    tables = np.zeros((len(pool_sizes), length, length), np.float32)
    rows_all = np.arange(length)
    for pool_index, pool_width in enumerate(pool_sizes):
        lead_pad = (pool_width - 1) // 2
        for offset in range(pool_width):
            source = np.clip(rows_all - lead_pad + offset, 0, length - 1)
            tables[pool_index][rows_all, source] += np.float32(1.0 / pool_width)
    return jnp.asarray(tables)


def spectral_tables(modes, length):
    positions = jnp.arange(length, dtype=jnp.int32)
    phase = modes[:, :, None] * positions[None, None, :] % length
    angle = phase.astype(jnp.float32) * (2.0 * math.pi / length)
    cosine = jnp.cos(angle)
    sine = jnp.sin(angle)
    doubled = jnp.where((modes == 0) | (2 * modes == length), 1.0, 2.0).astype(jnp.float32) / length
    inv_cos = jnp.transpose(doubled[:, :, None] * cosine, (0, 2, 1))
    inv_sin = jnp.transpose(-doubled[:, :, None] * sine, (0, 2, 1))
    return (cosine, -sine, inv_cos, inv_sin)


def product(form, left, right):
    return jnp.einsum(form, left, right, preferred_element_type=jnp.float32)


def pool_rows(picks, pools):
    rows = jnp.zeros(picks.shape + (pools.shape[-1],), jnp.float32)
    for pool_index in range(len(pool_sizes)):
        rows = jnp.where((picks == pool_index)[..., None], pools[pool_index][None], rows)
    return rows


def trend_local(values, rows):
    return jnp.einsum("wts,wsd->wtd", rows, values, precision=highest)


def trend_back(grads, rows):
    return jnp.einsum("wts,wtd->wsd", rows, grads, precision=highest)


def mixer_block(mixer_low, head_size):
    head_count = mixer_low.shape[0]
    shaped = mixer_low.reshape(head_count, -1, head_size, 2 * head_size)
    real_part = shaped[..., :head_size]
    imag_part = shaped[..., head_size:]
    upper = jnp.concatenate([real_part, imag_part], axis=-1)
    lower = jnp.concatenate([-imag_part, real_part], axis=-1)
    return jnp.concatenate([upper, lower], axis=2)


def exact_gelu(values):
    return jax.nn.gelu(values, approximate=False)


def on_device(
    inputs,
    out_grad,
    modes,
    gates,
    query_weight,
    mixer_weight,
    output_weight,
    inner_weight,
    outer_weight,
    query_momentum,
    query_average,
    mixer_momentum,
    mixer_average,
    output_momentum,
    output_average,
    inner_momentum,
    inner_average,
    outer_momentum,
    outer_average,
):
    windows, length, local_width = inputs.shape
    head_count, mode_count = modes.shape
    head_size = local_width // head_count
    hidden_width = inner_weight.shape[1]
    head_parts = lax.axis_size("head")
    me = lax.axis_index("head")
    shifts = list(range(1, head_parts))

    def peer(shift):
        return (me + shift) % head_parts

    def swap(values, shift):
        pairs = [(j, (j + shift) % head_parts) for j in range(head_parts)]
        return lax.ppermute(values, "head", pairs)

    def rows_of(weight, block, size):
        return lax.dynamic_slice_in_dim(weight, block * size, size, 0)

    def cols_of(weight, block, size):
        return lax.dynamic_slice_in_dim(weight, block * size, size, 1)

    def gathered_product(mine, weight_low, size):
        received = {s: swap(mine, s) for s in shifts}
        total = product("wtd,de->wte", mine, rows_of(weight_low, me, size))
        for s in shifts:
            owner = (me - s) % head_parts
            total = total + product("wtd,de->wte", received[s], rows_of(weight_low, owner, size))
        return total, received

    def scattered_product(values, weight_low, size):
        sent = {
            s: swap(product("wte,ed->wtd", values, cols_of(weight_low, peer(s), size)).astype(jnp.bfloat16), s)
            for s in shifts
        }
        total = product("wte,ed->wtd", values, cols_of(weight_low, me, size))
        for s in shifts:
            total = total + sent[s].astype(jnp.float32)
        return total

    def placed_rows(parts, size, total_rows):
        out = jnp.zeros((total_rows,) + parts[0][1].shape[1:], jnp.float32)
        for block, part in parts:
            out = lax.dynamic_update_slice_in_dim(out, part, block * size, 0)
        return out

    def placed_cols(parts, size, total_cols):
        out = jnp.zeros(parts[0][1].shape[:1] + (total_cols,), jnp.float32)
        for block, part in parts:
            out = lax.dynamic_update_slice_in_dim(out, part, block * size, 1)
        return out

    model_width = local_width * head_parts
    pools = pool_tables(length)
    fwd_cos, fwd_sin, inv_cos, inv_sin = [
        one_table.astype(jnp.bfloat16) for one_table in spectral_tables(modes, length)
    ]
    query_low = query_weight.astype(jnp.bfloat16)
    output_low = output_weight.astype(jnp.bfloat16)
    inner_low = inner_weight.astype(jnp.bfloat16)
    outer_low = outer_weight.astype(jnp.bfloat16)
    inner_t = jnp.transpose(inner_low)
    query_t = jnp.transpose(query_low)
    block = mixer_block(mixer_weight.astype(jnp.bfloat16), head_size)

    def chunk_pass(inputs, out_grad, first_rows, second_rows):
        windows = inputs.shape[0]
        grad_comb = out_grad - trend_back(out_grad, second_rows)
        grad_feed_mine = grad_comb.astype(jnp.bfloat16)
        grad_feed_recv = {s: swap(grad_feed_mine, s) for s in shifts}

        inputs_mine = inputs.astype(jnp.bfloat16)
        query, inputs_recv = gathered_product(inputs_mine, query_low, local_width)
        query = query.astype(jnp.bfloat16)
        query_heads = query.reshape(windows, length, head_count, head_size)
        spectrum = jnp.concatenate(
            [
                product("hmt,wthe->whme", fwd_cos, query_heads),
                product("hmt,wthe->whme", fwd_sin, query_heads),
            ],
            axis=-1,
        ).astype(jnp.bfloat16)
        mixed = product("whmi,hmio->whmo", spectrum, block).astype(jnp.bfloat16)
        field = product("htm,whme->wthe", inv_cos, mixed[..., :head_size]) + product(
            "htm,whme->wthe", inv_sin, mixed[..., head_size:]
        )
        field = field.reshape(windows, length, local_width).astype(jnp.bfloat16)
        attended = scattered_product(field, output_low, local_width)
        resid_one = inputs + attended
        seasonal = resid_one - trend_local(resid_one, first_rows)
        seasonal_mine = seasonal.astype(jnp.bfloat16)
        pre, seasonal_recv = gathered_product(seasonal_mine, inner_low, local_width)
        activated, gelu_pull = jax.vjp(exact_gelu, pre)
        hidden = activated.astype(jnp.bfloat16)
        feed = scattered_product(hidden, outer_low, local_width)
        combined = seasonal + feed
        output = combined - trend_local(combined, second_rows)

        outer_grad_t = placed_rows(
            [(me, product("wtd,wtf->df", grad_feed_mine, hidden))]
            + [((me - s) % head_parts, product("wtd,wtf->df", grad_feed_recv[s], hidden)) for s in shifts],
            local_width,
            model_width,
        )
        grad_hidden = product("wtd,fd->wtf", grad_feed_mine, cols_of(outer_low, me, local_width))
        for s in shifts:
            grad_hidden = grad_hidden + product(
                "wtd,fd->wtf", grad_feed_recv[s], cols_of(outer_low, (me - s) % head_parts, local_width)
            )
        grad_pre = gelu_pull(grad_hidden)[0].astype(jnp.bfloat16)
        inner_grad = placed_rows(
            [(me, product("wtd,wtf->df", seasonal_mine, grad_pre))]
            + [((me - s) % head_parts, product("wtd,wtf->df", seasonal_recv[s], grad_pre)) for s in shifts],
            local_width,
            model_width,
        )
        grad_season = grad_comb + scattered_product(grad_pre, inner_t, local_width)
        grad_resid = grad_season - trend_back(grad_season, first_rows)
        grad_attend_mine = grad_resid.astype(jnp.bfloat16)
        grad_attend_recv = {s: swap(grad_attend_mine, s) for s in shifts}
        output_grad_t = placed_rows(
            [(me, product("wtd,wte->de", grad_attend_mine, field))]
            + [((me - s) % head_parts, product("wtd,wte->de", grad_attend_recv[s], field)) for s in shifts],
            local_width,
            model_width,
        )
        grad_field = product("wtd,ed->wte", grad_attend_mine, cols_of(output_low, me, local_width))
        for s in shifts:
            grad_field = grad_field + product(
                "wtd,ed->wte", grad_attend_recv[s], cols_of(output_low, (me - s) % head_parts, local_width)
            )
        grad_field = grad_field.astype(jnp.bfloat16)
        grad_field = grad_field.reshape(windows, length, head_count, head_size)
        grad_mixed = jnp.concatenate(
            [
                product("htm,wthe->whme", inv_cos, grad_field),
                product("htm,wthe->whme", inv_sin, grad_field),
            ],
            axis=-1,
        ).astype(jnp.bfloat16)
        grad_spectrum = product("whmo,hmio->whmi", grad_mixed, block).astype(jnp.bfloat16)
        grad_query = product("hmt,whme->wthe", fwd_cos, grad_spectrum[..., :head_size]) + product(
            "hmt,whme->wthe", fwd_sin, grad_spectrum[..., head_size:]
        )
        grad_query = grad_query.reshape(windows, length, local_width).astype(jnp.bfloat16)
        query_grad = placed_rows(
            [(me, product("wtd,wte->de", inputs_mine, grad_query))]
            + [((me - s) % head_parts, product("wtd,wte->de", inputs_recv[s], grad_query)) for s in shifts],
            local_width,
            model_width,
        )
        input_grad = grad_resid + scattered_product(grad_query, query_t, local_width)
        spectrum_parts = spectrum.reshape(windows, head_count, mode_count, 2, head_size)
        grad_real = grad_mixed[..., :head_size]
        grad_imag = grad_mixed[..., head_size:]
        paired = jnp.stack(
            [grad_mixed, jnp.concatenate([grad_imag, -grad_real], axis=-1)], axis=3
        )
        mixer_full = product("whmci,whmco->hmio", spectrum_parts, paired).reshape(
            head_count, mode_count * head_size, 2 * head_size
        )
        return output, input_grad, (query_grad, mixer_full, output_grad_t, inner_grad, outer_grad_t)

    chunks = 1
    span = windows // chunks
    first_all = pool_rows(gates[0], pools)
    second_all = pool_rows(gates[1], pools)
    results = [
        chunk_pass(
            inputs[c * span : (c + 1) * span],
            out_grad[c * span : (c + 1) * span],
            first_all[c * span : (c + 1) * span],
            second_all[c * span : (c + 1) * span],
        )
        for c in range(chunks)
    ]
    output = jnp.concatenate([r[0] for r in results], axis=0)
    input_grad = jnp.concatenate([r[1] for r in results], axis=0)
    query_grad, mixer_full, output_grad_t, inner_grad, outer_grad_t = [
        sum(r[2][i] for r in results[1:]) + results[0][2][i] if chunks > 1 else results[0][2][i]
        for i in range(5)
    ]

    dp_count = lax.axis_size("dp")
    dp_rank = lax.axis_index("dp")

    lanes = 128

    def lead(grad, axis_number):
        shape = grad.shape
        split = shape[:axis_number] + (dp_count, shape[axis_number] // dp_count) + shape[axis_number + 1 :]
        owned_shape = shape[:axis_number] + (shape[axis_number] // dp_count,) + shape[axis_number + 1 :]
        return jnp.moveaxis(grad.reshape(split), axis_number, 0).reshape(dp_count, -1, lanes), owned_shape

    def reduced_over_dp(grads_axes):
        laid = [lead(grad, axis_number) for grad, axis_number in grads_axes]
        joined = jnp.concatenate([flat for flat, _ in laid], axis=1)
        reduced = lax.psum_scatter(
            joined.reshape(-1, lanes), "dp", scatter_dimension=0, tiled=True
        )
        parts = []
        offset = 0
        for flat, owned_shape in laid:
            rows = flat.shape[1]
            parts.append(reduced[offset : offset + rows].reshape(owned_shape))
            offset += rows
        return parts

    inner_part, outer_part_t = reduced_over_dp([(inner_grad, 0), (outer_grad_t, 0)])
    mixer_part, output_part_t, query_part = reduced_over_dp(
        [(mixer_full, 1), (output_grad_t, 0), (query_grad, 0)]
    )
    output_part = jnp.transpose(output_part_t)
    outer_part = jnp.transpose(outer_part_t)
    token_total = windows * length * dp_count

    def owned(weight, share, axis_number):
        return lax.dynamic_slice_in_dim(weight, dp_rank * share, share, axis_number)

    def stepped(grad, momentum, average, old_weight, spread):
        rate = 0.5 * spread / math.sqrt(token_total)
        new_momentum = momentum_decay * momentum + grad
        new_weight = old_weight - rate * (grad + momentum_decay * new_momentum)
        new_average = average_decay * average + (1 - average_decay) * new_weight
        return (new_momentum, new_weight, new_average)

    query_new = stepped(
        query_part,
        query_momentum,
        query_average,
        owned(query_weight, query_momentum.shape[0], 0),
        D ** (-0.5),
    )
    mixer_new = stepped(
        mixer_part,
        mixer_momentum,
        mixer_average,
        owned(mixer_weight, mixer_momentum.shape[1], 1),
        mixer_spread,
    )
    output_new = stepped(
        output_part,
        output_momentum,
        output_average,
        owned(output_weight, output_momentum.shape[1], 1),
        D ** (-0.5),
    )
    inner_new = stepped(
        inner_part,
        inner_momentum,
        inner_average,
        owned(inner_weight, inner_momentum.shape[0], 0),
        D ** (-0.5),
    )
    outer_new = stepped(
        outer_part,
        outer_momentum,
        outer_average,
        owned(outer_weight, outer_momentum.shape[1], 1),
        FF ** (-0.5),
    )
    return (
        output,
        input_grad,
        query_new[0],
        query_new[1],
        query_new[2],
        mixer_new[0],
        mixer_new[1],
        mixer_new[2],
        output_new[0],
        output_new[1],
        output_new[2],
        inner_new[0],
        inner_new[1],
        inner_new[2],
        outer_new[0],
        outer_new[1],
        outer_new[2],
    )


def solution(mesh):
    return jax.shard_map(
        on_device,
        mesh=mesh,
        in_specs=(
            P("dp", None, "head"),
            P("dp", None, "head"),
            P("head", None),
            P(None, "dp", None),
            P(None, "head"),
            P("head", None, None),
            P("head", None),
            P(None, "head"),
            P("head", None),
            P("dp", "head"),
            P("dp", "head"),
            P("head", "dp", None),
            P("head", "dp", None),
            P("head", "dp"),
            P("head", "dp"),
            P("dp", "head"),
            P("dp", "head"),
            P("head", "dp"),
            P("head", "dp"),
        ),
        out_specs=(
            P("dp", None, "head"),
            P("dp", None, "head"),
            P("dp", "head"),
            P("dp", "head"),
            P("dp", "head"),
            P("head", "dp", None),
            P("head", "dp", None),
            P("head", "dp", None),
            P("head", "dp"),
            P("head", "dp"),
            P("head", "dp"),
            P("dp", "head"),
            P("dp", "head"),
            P("dp", "head"),
            P("head", "dp"),
            P("head", "dp"),
            P("head", "dp"),
        ),
        check_vma=False,
    )
```

```python
import math

import jax
import jax.numpy as jnp
import numpy as np
from jax import lax
from jax.sharding import PartitionSpec as P

D = 512
FF = 2048


highest = lax.Precision.HIGHEST
pool_sizes = (7, 12, 14, 24, 48)
mixer_spread = 0.07
momentum_decay = 0.9
average_decay = 0.9


def pool_tables(length):
    tables = np.zeros((len(pool_sizes), length, length), np.float32)
    rows_all = np.arange(length)
    for pool_index, pool_width in enumerate(pool_sizes):
        lead_pad = (pool_width - 1) // 2
        for offset in range(pool_width):
            source = np.clip(rows_all - lead_pad + offset, 0, length - 1)
            tables[pool_index][rows_all, source] += np.float32(1.0 / pool_width)
    return jnp.asarray(tables)


def spectral_tables(modes, length):
    positions = jnp.arange(length, dtype=jnp.int32)
    phase = modes[:, :, None] * positions[None, None, :] % length
    angle = phase.astype(jnp.float32) * (2.0 * math.pi / length)
    cosine = jnp.cos(angle)
    sine = jnp.sin(angle)
    doubled = jnp.where((modes == 0) | (2 * modes == length), 1.0, 2.0).astype(jnp.float32) / length
    inv_cos = jnp.transpose(doubled[:, :, None] * cosine, (0, 2, 1))
    inv_sin = jnp.transpose(-doubled[:, :, None] * sine, (0, 2, 1))
    return (cosine, -sine, inv_cos, inv_sin)


def product(form, left, right):
    return jnp.einsum(form, left, right, preferred_element_type=jnp.float32)


def pool_counts(length):
    counts = np.zeros((len(pool_sizes), length, length), np.float32)
    rows_all = np.arange(length)
    for pool_index, pool_width in enumerate(pool_sizes):
        lead_pad = (pool_width - 1) // 2
        for offset in range(pool_width):
            source = np.clip(rows_all - lead_pad + offset, 0, length - 1)
            counts[pool_index][rows_all, source] += 1.0
    return counts


def pool_rows(picks, length):
    counts = pool_counts(length)
    rows = jnp.zeros(picks.shape + (length,), jnp.float32)
    scale = jnp.zeros(picks.shape, jnp.float32)
    for pool_index, pool_width in enumerate(pool_sizes):
        chosen = picks == pool_index
        rows = jnp.where(chosen[..., None], jnp.asarray(counts[pool_index])[None], rows)
        scale = jnp.where(chosen, np.float32(1.0 / pool_width), scale)
    return rows.astype(jnp.bfloat16), scale


def split_three(values):
    high = values.astype(jnp.bfloat16)
    rest = values - high.astype(jnp.float32)
    middle = rest.astype(jnp.bfloat16)
    low = (rest - middle.astype(jnp.float32)).astype(jnp.bfloat16)
    return high, middle, low


def trend_local(values, rows):
    counts, scale = rows
    parts = jnp.concatenate(split_three(values), axis=1)
    tiled = jnp.concatenate([counts] * 3, axis=2)
    summed = jnp.einsum("wts,wsd->wtd", tiled, parts, preferred_element_type=jnp.float32)
    return summed * scale[..., None]


def trend_back(grads, rows):
    counts, scale = rows
    parts = jnp.concatenate(split_three(grads * scale[..., None]), axis=1)
    tiled = jnp.concatenate([counts] * 3, axis=1)
    return jnp.einsum("wts,wtd->wsd", tiled, parts, preferred_element_type=jnp.float32)


def mixer_block(mixer_low, head_size):
    head_count = mixer_low.shape[0]
    shaped = mixer_low.reshape(head_count, -1, head_size, 2 * head_size)
    real_part = shaped[..., :head_size]
    imag_part = shaped[..., head_size:]
    upper = jnp.concatenate([real_part, imag_part], axis=-1)
    lower = jnp.concatenate([-imag_part, real_part], axis=-1)
    return jnp.concatenate([upper, lower], axis=2)


def exact_gelu(values):
    return jax.nn.gelu(values, approximate=False)


def on_device(
    inputs,
    out_grad,
    modes,
    gates,
    query_weight,
    mixer_weight,
    output_weight,
    inner_weight,
    outer_weight,
    query_momentum,
    query_average,
    mixer_momentum,
    mixer_average,
    output_momentum,
    output_average,
    inner_momentum,
    inner_average,
    outer_momentum,
    outer_average,
):
    windows, length, local_width = inputs.shape
    head_count, mode_count = modes.shape
    head_size = local_width // head_count
    hidden_width = inner_weight.shape[1]
    head_parts = lax.axis_size("head")
    me = lax.axis_index("head")
    shifts = list(range(1, head_parts))

    def peer(shift):
        return (me + shift) % head_parts

    def swap(values, shift):
        pairs = [(j, (j + shift) % head_parts) for j in range(head_parts)]
        return lax.ppermute(values, "head", pairs)

    def rows_of(weight, block, size):
        return lax.dynamic_slice_in_dim(weight, block * size, size, 0)

    def cols_of(weight, block, size):
        return lax.dynamic_slice_in_dim(weight, block * size, size, 1)

    def gathered_product(mine, weight_low, size):
        received = {s: swap(mine, s) for s in shifts}
        total = product("wtd,de->wte", mine, rows_of(weight_low, me, size))
        for s in shifts:
            owner = (me - s) % head_parts
            total = total + product("wtd,de->wte", received[s], rows_of(weight_low, owner, size))
        return total, received

    def scattered_product(values, weight_low, size):
        sent = {
            s: swap(product("wte,ed->wtd", values, cols_of(weight_low, peer(s), size)).astype(jnp.bfloat16), s)
            for s in shifts
        }
        total = product("wte,ed->wtd", values, cols_of(weight_low, me, size))
        for s in shifts:
            total = total + sent[s].astype(jnp.float32)
        return total

    def placed_rows(parts, size, total_rows):
        out = jnp.zeros((total_rows,) + parts[0][1].shape[1:], jnp.float32)
        for block, part in parts:
            out = lax.dynamic_update_slice_in_dim(out, part, block * size, 0)
        return out

    def placed_cols(parts, size, total_cols):
        out = jnp.zeros(parts[0][1].shape[:1] + (total_cols,), jnp.float32)
        for block, part in parts:
            out = lax.dynamic_update_slice_in_dim(out, part, block * size, 1)
        return out

    model_width = local_width * head_parts
    pools = pool_tables(length)
    fwd_cos, fwd_sin, inv_cos, inv_sin = [
        one_table.astype(jnp.bfloat16) for one_table in spectral_tables(modes, length)
    ]
    query_low = query_weight.astype(jnp.bfloat16)
    output_low = output_weight.astype(jnp.bfloat16)
    inner_low = inner_weight.astype(jnp.bfloat16)
    outer_low = outer_weight.astype(jnp.bfloat16)
    inner_t = jnp.transpose(inner_low)
    query_t = jnp.transpose(query_low)
    block = mixer_block(mixer_weight.astype(jnp.bfloat16), head_size)

    def chunk_pass(inputs, out_grad, first_rows, second_rows):
        windows = inputs.shape[0]
        grad_comb = out_grad - trend_back(out_grad, second_rows)
        grad_feed_mine = grad_comb.astype(jnp.bfloat16)

        inputs_mine = inputs.astype(jnp.bfloat16)
        query, inputs_recv = gathered_product(inputs_mine, query_low, local_width)
        grad_feed_mine, _ = lax.optimization_barrier((grad_feed_mine, tuple(inputs_recv.values())))
        grad_feed_recv = {s: swap(grad_feed_mine, s) for s in shifts}
        query = query.astype(jnp.bfloat16)
        query_heads = query.reshape(windows, length, head_count, head_size)
        spectrum = jnp.concatenate(
            [
                product("hmt,wthe->whme", fwd_cos, query_heads),
                product("hmt,wthe->whme", fwd_sin, query_heads),
            ],
            axis=-1,
        ).astype(jnp.bfloat16)
        mixed = product("whmi,hmio->whmo", spectrum, block).astype(jnp.bfloat16)
        field = product("htm,whme->wthe", inv_cos, mixed[..., :head_size]) + product(
            "htm,whme->wthe", inv_sin, mixed[..., head_size:]
        )
        field = field.reshape(windows, length, local_width).astype(jnp.bfloat16)
        field, _ = lax.optimization_barrier((field, tuple(grad_feed_recv.values())))
        attended = scattered_product(field, output_low, local_width)
        resid_one = inputs + attended
        seasonal = resid_one - trend_local(resid_one, first_rows)
        seasonal_mine = seasonal.astype(jnp.bfloat16)
        pre, seasonal_recv = gathered_product(seasonal_mine, inner_low, local_width)
        activated, gelu_pull = jax.vjp(exact_gelu, pre)
        hidden = activated.astype(jnp.bfloat16)
        feed = scattered_product(hidden, outer_low, local_width)
        combined = seasonal + feed
        output = combined - trend_local(combined, second_rows)

        outer_grad_t = placed_rows(
            [(me, product("wtd,wtf->df", grad_feed_mine, hidden))]
            + [((me - s) % head_parts, product("wtd,wtf->df", grad_feed_recv[s], hidden)) for s in shifts],
            local_width,
            model_width,
        )
        grad_hidden = product("wtd,fd->wtf", grad_feed_mine, cols_of(outer_low, me, local_width))
        for s in shifts:
            grad_hidden = grad_hidden + product(
                "wtd,fd->wtf", grad_feed_recv[s], cols_of(outer_low, (me - s) % head_parts, local_width)
            )
        grad_pre = gelu_pull(grad_hidden)[0].astype(jnp.bfloat16)
        inner_grad = placed_rows(
            [(me, product("wtd,wtf->df", seasonal_mine, grad_pre))]
            + [((me - s) % head_parts, product("wtd,wtf->df", seasonal_recv[s], grad_pre)) for s in shifts],
            local_width,
            model_width,
        )
        grad_season = grad_comb + scattered_product(grad_pre, inner_t, local_width)
        grad_resid = grad_season - trend_back(grad_season, first_rows)
        grad_attend_mine = grad_resid.astype(jnp.bfloat16)
        grad_attend_recv = {s: swap(grad_attend_mine, s) for s in shifts}
        output_grad_t = placed_rows(
            [(me, product("wtd,wte->de", grad_attend_mine, field))]
            + [((me - s) % head_parts, product("wtd,wte->de", grad_attend_recv[s], field)) for s in shifts],
            local_width,
            model_width,
        )
        grad_field = product("wtd,ed->wte", grad_attend_mine, cols_of(output_low, me, local_width))
        for s in shifts:
            grad_field = grad_field + product(
                "wtd,ed->wte", grad_attend_recv[s], cols_of(output_low, (me - s) % head_parts, local_width)
            )
        grad_field = grad_field.astype(jnp.bfloat16)
        grad_field = grad_field.reshape(windows, length, head_count, head_size)
        grad_mixed = jnp.concatenate(
            [
                product("htm,wthe->whme", inv_cos, grad_field),
                product("htm,wthe->whme", inv_sin, grad_field),
            ],
            axis=-1,
        ).astype(jnp.bfloat16)
        grad_spectrum = product("whmo,hmio->whmi", grad_mixed, block).astype(jnp.bfloat16)
        grad_query = product("hmt,whme->wthe", fwd_cos, grad_spectrum[..., :head_size]) + product(
            "hmt,whme->wthe", fwd_sin, grad_spectrum[..., head_size:]
        )
        grad_query = grad_query.reshape(windows, length, local_width).astype(jnp.bfloat16)
        query_grad = placed_rows(
            [(me, product("wtd,wte->de", inputs_mine, grad_query))]
            + [((me - s) % head_parts, product("wtd,wte->de", inputs_recv[s], grad_query)) for s in shifts],
            local_width,
            model_width,
        )
        input_grad = grad_resid + scattered_product(grad_query, query_t, local_width)
        spectrum_parts = spectrum.reshape(windows, head_count, mode_count, 2, head_size)
        grad_real = grad_mixed[..., :head_size]
        grad_imag = grad_mixed[..., head_size:]
        paired = jnp.stack(
            [grad_mixed, jnp.concatenate([grad_imag, -grad_real], axis=-1)], axis=3
        )
        mixer_full = product("whmci,whmco->hmio", spectrum_parts, paired).reshape(
            head_count, mode_count * head_size, 2 * head_size
        )
        return output, input_grad, (query_grad, mixer_full, output_grad_t, inner_grad, outer_grad_t)

    chunks = 1
    span = windows // chunks
    first_all = pool_rows(gates[0], length)
    second_all = pool_rows(gates[1], length)
    results = [
        chunk_pass(
            inputs[c * span : (c + 1) * span],
            out_grad[c * span : (c + 1) * span],
            tuple(part[c * span : (c + 1) * span] for part in first_all),
            tuple(part[c * span : (c + 1) * span] for part in second_all),
        )
        for c in range(chunks)
    ]
    output = jnp.concatenate([r[0] for r in results], axis=0)
    input_grad = jnp.concatenate([r[1] for r in results], axis=0)
    query_grad, mixer_full, output_grad_t, inner_grad, outer_grad_t = [
        sum(r[2][i] for r in results[1:]) + results[0][2][i] if chunks > 1 else results[0][2][i]
        for i in range(5)
    ]

    dp_count = lax.axis_size("dp")
    dp_rank = lax.axis_index("dp")

    lanes = 128

    def lead(grad, axis_number):
        shape = grad.shape
        split = shape[:axis_number] + (dp_count, shape[axis_number] // dp_count) + shape[axis_number + 1 :]
        owned_shape = shape[:axis_number] + (shape[axis_number] // dp_count,) + shape[axis_number + 1 :]
        return jnp.moveaxis(grad.reshape(split), axis_number, 0).reshape(dp_count, -1, lanes), owned_shape

    def reduced_over_dp(grads_axes):
        laid = [lead(grad, axis_number) for grad, axis_number in grads_axes]
        joined = jnp.concatenate([flat for flat, _ in laid], axis=1)
        reduced = lax.psum_scatter(
            joined.reshape(-1, lanes), "dp", scatter_dimension=0, tiled=True
        )
        parts = []
        offset = 0
        for flat, owned_shape in laid:
            rows = flat.shape[1]
            parts.append(reduced[offset : offset + rows].reshape(owned_shape))
            offset += rows
        return parts

    inner_part, outer_part_t = reduced_over_dp([(inner_grad, 0), (outer_grad_t, 0)])
    mixer_part, output_part_t, query_part = reduced_over_dp(
        [(mixer_full, 1), (output_grad_t, 0), (query_grad, 0)]
    )
    output_part = jnp.transpose(output_part_t)
    outer_part = jnp.transpose(outer_part_t)
    token_total = windows * length * dp_count

    def owned(weight, share, axis_number):
        return lax.dynamic_slice_in_dim(weight, dp_rank * share, share, axis_number)

    def stepped(grad, momentum, average, old_weight, spread):
        rate = 0.5 * spread / math.sqrt(token_total)
        new_momentum = momentum_decay * momentum + grad
        new_weight = old_weight - rate * (grad + momentum_decay * new_momentum)
        new_average = average_decay * average + (1 - average_decay) * new_weight
        return (new_momentum, new_weight, new_average)

    query_new = stepped(
        query_part,
        query_momentum,
        query_average,
        owned(query_weight, query_momentum.shape[0], 0),
        D ** (-0.5),
    )
    mixer_new = stepped(
        mixer_part,
        mixer_momentum,
        mixer_average,
        owned(mixer_weight, mixer_momentum.shape[1], 1),
        mixer_spread,
    )
    output_new = stepped(
        output_part,
        output_momentum,
        output_average,
        owned(output_weight, output_momentum.shape[1], 1),
        D ** (-0.5),
    )
    inner_new = stepped(
        inner_part,
        inner_momentum,
        inner_average,
        owned(inner_weight, inner_momentum.shape[0], 0),
        D ** (-0.5),
    )
    outer_new = stepped(
        outer_part,
        outer_momentum,
        outer_average,
        owned(outer_weight, outer_momentum.shape[1], 1),
        FF ** (-0.5),
    )
    return (
        output,
        input_grad,
        query_new[0],
        query_new[1],
        query_new[2],
        mixer_new[0],
        mixer_new[1],
        mixer_new[2],
        output_new[0],
        output_new[1],
        output_new[2],
        inner_new[0],
        inner_new[1],
        inner_new[2],
        outer_new[0],
        outer_new[1],
        outer_new[2],
    )


def solution(mesh):
    return jax.shard_map(
        on_device,
        mesh=mesh,
        in_specs=(
            P("dp", None, "head"),
            P("dp", None, "head"),
            P("head", None),
            P(None, "dp", None),
            P(None, "head"),
            P("head", None, None),
            P("head", None),
            P(None, "head"),
            P("head", None),
            P("dp", "head"),
            P("dp", "head"),
            P("head", "dp", None),
            P("head", "dp", None),
            P("head", "dp"),
            P("head", "dp"),
            P("dp", "head"),
            P("dp", "head"),
            P("head", "dp"),
            P("head", "dp"),
        ),
        out_specs=(
            P("dp", None, "head"),
            P("dp", None, "head"),
            P("dp", "head"),
            P("dp", "head"),
            P("dp", "head"),
            P("head", "dp", None),
            P("head", "dp", None),
            P("head", "dp", None),
            P("head", "dp"),
            P("head", "dp"),
            P("head", "dp"),
            P("dp", "head"),
            P("dp", "head"),
            P("dp", "head"),
            P("head", "dp"),
            P("head", "dp"),
            P("head", "dp"),
        ),
        check_vma=False,
    )
```

```python
import math

import jax
import jax.numpy as jnp
import numpy as np
from jax import lax
from jax.sharding import PartitionSpec as P

D = 512
FF = 2048


highest = lax.Precision.HIGHEST
pool_sizes = (7, 12, 14, 24, 48)
mixer_spread = 0.07
momentum_decay = 0.9
average_decay = 0.9


def pool_tables(length):
    tables = np.zeros((len(pool_sizes), length, length), np.float32)
    rows_all = np.arange(length)
    for pool_index, pool_width in enumerate(pool_sizes):
        lead_pad = (pool_width - 1) // 2
        for offset in range(pool_width):
            source = np.clip(rows_all - lead_pad + offset, 0, length - 1)
            tables[pool_index][rows_all, source] += np.float32(1.0 / pool_width)
    return jnp.asarray(tables)


def spectral_tables(modes, length):
    positions = jnp.arange(length, dtype=jnp.int32)
    phase = modes[:, :, None] * positions[None, None, :] % length
    angle = phase.astype(jnp.float32) * (2.0 * math.pi / length)
    cosine = jnp.cos(angle)
    sine = jnp.sin(angle)
    doubled = jnp.where((modes == 0) | (2 * modes == length), 1.0, 2.0).astype(jnp.float32) / length
    inv_cos = jnp.transpose(doubled[:, :, None] * cosine, (0, 2, 1))
    inv_sin = jnp.transpose(-doubled[:, :, None] * sine, (0, 2, 1))
    return (cosine, -sine, inv_cos, inv_sin)


def product(form, left, right):
    return jnp.einsum(form, left, right, preferred_element_type=jnp.float32)


def pool_counts(length):
    counts = np.zeros((len(pool_sizes), length, length), np.float32)
    rows_all = np.arange(length)
    for pool_index, pool_width in enumerate(pool_sizes):
        lead_pad = (pool_width - 1) // 2
        for offset in range(pool_width):
            source = np.clip(rows_all - lead_pad + offset, 0, length - 1)
            counts[pool_index][rows_all, source] += 1.0
    return counts


def pool_rows(picks, length):
    counts = pool_counts(length)
    rows = jnp.zeros(picks.shape + (length,), jnp.float32)
    scale = jnp.zeros(picks.shape, jnp.float32)
    for pool_index, pool_width in enumerate(pool_sizes):
        chosen = picks == pool_index
        rows = jnp.where(chosen[..., None], jnp.asarray(counts[pool_index])[None], rows)
        scale = jnp.where(chosen, np.float32(1.0 / pool_width), scale)
    return rows.astype(jnp.bfloat16), scale


def split_three(values):
    high = values.astype(jnp.bfloat16)
    rest = values - high.astype(jnp.float32)
    middle = rest.astype(jnp.bfloat16)
    low = (rest - middle.astype(jnp.float32)).astype(jnp.bfloat16)
    return high, middle, low


def trend_local(values, rows):
    counts, scale = rows
    parts = jnp.concatenate(split_three(values), axis=1)
    tiled = jnp.concatenate([counts] * 3, axis=2)
    summed = jnp.einsum("wts,wsd->wtd", tiled, parts, preferred_element_type=jnp.float32)
    return summed * scale[..., None]


def trend_back(grads, rows):
    counts, scale = rows
    parts = jnp.concatenate(split_three(grads * scale[..., None]), axis=1)
    tiled = jnp.concatenate([counts] * 3, axis=1)
    return jnp.einsum("wts,wtd->wsd", tiled, parts, preferred_element_type=jnp.float32)


def mixer_block(mixer_low, head_size):
    head_count = mixer_low.shape[0]
    shaped = mixer_low.reshape(head_count, -1, head_size, 2 * head_size)
    real_part = shaped[..., :head_size]
    imag_part = shaped[..., head_size:]
    upper = jnp.concatenate([real_part, imag_part], axis=-1)
    lower = jnp.concatenate([-imag_part, real_part], axis=-1)
    return jnp.concatenate([upper, lower], axis=2)


def exact_gelu(values):
    return jax.nn.gelu(values, approximate=False)


def on_device(
    inputs,
    out_grad,
    modes,
    gates,
    query_weight,
    mixer_weight,
    output_weight,
    inner_weight,
    outer_weight,
    query_momentum,
    query_average,
    mixer_momentum,
    mixer_average,
    output_momentum,
    output_average,
    inner_momentum,
    inner_average,
    outer_momentum,
    outer_average,
):
    windows, length, local_width = inputs.shape
    head_count, mode_count = modes.shape
    head_size = local_width // head_count
    hidden_width = inner_weight.shape[1]
    head_parts = lax.axis_size("head")
    me = lax.axis_index("head")
    shifts = list(range(1, head_parts))

    def peer(shift):
        return (me + shift) % head_parts

    def swap(values, shift):
        pairs = [(j, (j + shift) % head_parts) for j in range(head_parts)]
        return lax.ppermute(values, "head", pairs)

    def rows_of(weight, block, size):
        return lax.dynamic_slice_in_dim(weight, block * size, size, 0)

    def cols_of(weight, block, size):
        return lax.dynamic_slice_in_dim(weight, block * size, size, 1)

    def gathered_product(mine, weight_low, size):
        received = {s: swap(mine, s) for s in shifts}
        total = product("wtd,de->wte", mine, rows_of(weight_low, me, size))
        for s in shifts:
            owner = (me - s) % head_parts
            total = total + product("wtd,de->wte", received[s], rows_of(weight_low, owner, size))
        return total, received

    def scattered_product(values, weight_low, size, after=()):
        outgoing = {
            s: product("wte,ed->wtd", values, cols_of(weight_low, peer(s), size)).astype(jnp.bfloat16)
            for s in shifts
        }
        if after:
            outgoing, _ = lax.optimization_barrier((outgoing, tuple(after)))
        sent = {s: swap(outgoing[s], s) for s in shifts}
        total = product("wte,ed->wtd", values, cols_of(weight_low, me, size))
        for s in shifts:
            total = total + sent[s].astype(jnp.float32)
        return total, sent

    def placed_rows(parts, size, total_rows):
        out = jnp.zeros((total_rows,) + parts[0][1].shape[1:], jnp.float32)
        for block, part in parts:
            out = lax.dynamic_update_slice_in_dim(out, part, block * size, 0)
        return out

    def placed_cols(parts, size, total_cols):
        out = jnp.zeros(parts[0][1].shape[:1] + (total_cols,), jnp.float32)
        for block, part in parts:
            out = lax.dynamic_update_slice_in_dim(out, part, block * size, 1)
        return out

    model_width = local_width * head_parts
    pools = pool_tables(length)
    fwd_cos, fwd_sin, inv_cos, inv_sin = [
        one_table.astype(jnp.bfloat16) for one_table in spectral_tables(modes, length)
    ]
    query_low = query_weight.astype(jnp.bfloat16)
    output_low = output_weight.astype(jnp.bfloat16)
    inner_low = inner_weight.astype(jnp.bfloat16)
    outer_low = outer_weight.astype(jnp.bfloat16)
    inner_t = jnp.transpose(inner_low)
    query_t = jnp.transpose(query_low)
    block = mixer_block(mixer_weight.astype(jnp.bfloat16), head_size)

    def chunk_pass(inputs, out_grad, first_rows, second_rows):
        windows = inputs.shape[0]
        grad_comb = out_grad - trend_back(out_grad, second_rows)
        grad_feed_mine = grad_comb.astype(jnp.bfloat16)

        inputs_mine = inputs.astype(jnp.bfloat16)
        query, inputs_recv = gathered_product(inputs_mine, query_low, local_width)
        grad_feed_recv = {s: swap(grad_feed_mine, s) for s in shifts}
        query = query.astype(jnp.bfloat16)
        query_heads = query.reshape(windows, length, head_count, head_size)
        spectrum = jnp.concatenate(
            [
                product("hmt,wthe->whme", fwd_cos, query_heads),
                product("hmt,wthe->whme", fwd_sin, query_heads),
            ],
            axis=-1,
        ).astype(jnp.bfloat16)
        mixed = product("whmi,hmio->whmo", spectrum, block).astype(jnp.bfloat16)
        field = product("htm,whme->wthe", inv_cos, mixed[..., :head_size]) + product(
            "htm,whme->wthe", inv_sin, mixed[..., head_size:]
        )
        field = field.reshape(windows, length, local_width).astype(jnp.bfloat16)
        attended, _ = scattered_product(field, output_low, local_width)
        resid_one = inputs + attended
        seasonal = resid_one - trend_local(resid_one, first_rows)
        seasonal_mine = seasonal.astype(jnp.bfloat16)
        pre, seasonal_recv = gathered_product(seasonal_mine, inner_low, local_width)
        activated, gelu_pull = jax.vjp(exact_gelu, pre)
        hidden = activated.astype(jnp.bfloat16)

        outer_grad_t = placed_rows(
            [(me, product("wtd,wtf->df", grad_feed_mine, hidden))]
            + [((me - s) % head_parts, product("wtd,wtf->df", grad_feed_recv[s], hidden)) for s in shifts],
            local_width,
            model_width,
        )
        grad_hidden = product("wtd,fd->wtf", grad_feed_mine, cols_of(outer_low, me, local_width))
        for s in shifts:
            grad_hidden = grad_hidden + product(
                "wtd,fd->wtf", grad_feed_recv[s], cols_of(outer_low, (me - s) % head_parts, local_width)
            )
        grad_pre = gelu_pull(grad_hidden)[0].astype(jnp.bfloat16)
        inner_grad = placed_rows(
            [(me, product("wtd,wtf->df", seasonal_mine, grad_pre))]
            + [((me - s) % head_parts, product("wtd,wtf->df", seasonal_recv[s], grad_pre)) for s in shifts],
            local_width,
            model_width,
        )
        grad_season_part, _ = scattered_product(grad_pre, inner_t, local_width)
        grad_season = grad_comb + grad_season_part
        grad_resid = grad_season - trend_back(grad_season, first_rows)
        grad_attend_mine = grad_resid.astype(jnp.bfloat16)
        grad_attend_recv = {s: swap(grad_attend_mine, s) for s in shifts}
        feed, feed_sent = scattered_product(hidden, outer_low, local_width, after=grad_attend_recv.values())
        combined = seasonal + feed
        output = combined - trend_local(combined, second_rows)
        output_grad_t = placed_rows(
            [(me, product("wtd,wte->de", grad_attend_mine, field))]
            + [((me - s) % head_parts, product("wtd,wte->de", grad_attend_recv[s], field)) for s in shifts],
            local_width,
            model_width,
        )
        grad_field = product("wtd,ed->wte", grad_attend_mine, cols_of(output_low, me, local_width))
        for s in shifts:
            grad_field = grad_field + product(
                "wtd,ed->wte", grad_attend_recv[s], cols_of(output_low, (me - s) % head_parts, local_width)
            )
        grad_field = grad_field.astype(jnp.bfloat16)
        grad_field = grad_field.reshape(windows, length, head_count, head_size)
        grad_mixed = jnp.concatenate(
            [
                product("htm,wthe->whme", inv_cos, grad_field),
                product("htm,wthe->whme", inv_sin, grad_field),
            ],
            axis=-1,
        ).astype(jnp.bfloat16)
        grad_spectrum = product("whmo,hmio->whmi", grad_mixed, block).astype(jnp.bfloat16)
        grad_query = product("hmt,whme->wthe", fwd_cos, grad_spectrum[..., :head_size]) + product(
            "hmt,whme->wthe", fwd_sin, grad_spectrum[..., head_size:]
        )
        grad_query = grad_query.reshape(windows, length, local_width).astype(jnp.bfloat16)
        query_grad = placed_rows(
            [(me, product("wtd,wte->de", inputs_mine, grad_query))]
            + [((me - s) % head_parts, product("wtd,wte->de", inputs_recv[s], grad_query)) for s in shifts],
            local_width,
            model_width,
        )
        input_part, _ = scattered_product(grad_query, query_t, local_width, after=feed_sent.values())
        input_grad = grad_resid + input_part
        spectrum_parts = spectrum.reshape(windows, head_count, mode_count, 2, head_size)
        grad_real = grad_mixed[..., :head_size]
        grad_imag = grad_mixed[..., head_size:]
        paired = jnp.stack(
            [grad_mixed, jnp.concatenate([grad_imag, -grad_real], axis=-1)], axis=3
        )
        mixer_full = product("whmci,whmco->hmio", spectrum_parts, paired).reshape(
            head_count, mode_count * head_size, 2 * head_size
        )
        return output, input_grad, (query_grad, mixer_full, output_grad_t, inner_grad, outer_grad_t)

    chunks = 1
    span = windows // chunks
    first_all = pool_rows(gates[0], length)
    second_all = pool_rows(gates[1], length)
    results = [
        chunk_pass(
            inputs[c * span : (c + 1) * span],
            out_grad[c * span : (c + 1) * span],
            tuple(part[c * span : (c + 1) * span] for part in first_all),
            tuple(part[c * span : (c + 1) * span] for part in second_all),
        )
        for c in range(chunks)
    ]
    output = jnp.concatenate([r[0] for r in results], axis=0)
    input_grad = jnp.concatenate([r[1] for r in results], axis=0)
    query_grad, mixer_full, output_grad_t, inner_grad, outer_grad_t = [
        sum(r[2][i] for r in results[1:]) + results[0][2][i] if chunks > 1 else results[0][2][i]
        for i in range(5)
    ]

    dp_count = lax.axis_size("dp")
    dp_rank = lax.axis_index("dp")

    lanes = 128

    def lead(grad, axis_number):
        shape = grad.shape
        split = shape[:axis_number] + (dp_count, shape[axis_number] // dp_count) + shape[axis_number + 1 :]
        owned_shape = shape[:axis_number] + (shape[axis_number] // dp_count,) + shape[axis_number + 1 :]
        return jnp.moveaxis(grad.reshape(split), axis_number, 0).reshape(dp_count, -1, lanes), owned_shape

    def reduced_over_dp(grads_axes):
        laid = [lead(grad, axis_number) for grad, axis_number in grads_axes]
        joined = jnp.concatenate([flat for flat, _ in laid], axis=1)
        reduced = lax.psum_scatter(
            joined.reshape(-1, lanes), "dp", scatter_dimension=0, tiled=True
        )
        parts = []
        offset = 0
        for flat, owned_shape in laid:
            rows = flat.shape[1]
            parts.append(reduced[offset : offset + rows].reshape(owned_shape))
            offset += rows
        return parts

    inner_part, outer_part_t = reduced_over_dp([(inner_grad, 0), (outer_grad_t, 0)])
    mixer_part, output_part_t, query_part = reduced_over_dp(
        [(mixer_full, 1), (output_grad_t, 0), (query_grad, 0)]
    )
    output_part = jnp.transpose(output_part_t)
    outer_part = jnp.transpose(outer_part_t)
    token_total = windows * length * dp_count

    def owned(weight, share, axis_number):
        return lax.dynamic_slice_in_dim(weight, dp_rank * share, share, axis_number)

    def stepped(grad, momentum, average, old_weight, spread):
        rate = 0.5 * spread / math.sqrt(token_total)
        new_momentum = momentum_decay * momentum + grad
        new_weight = old_weight - rate * (grad + momentum_decay * new_momentum)
        new_average = average_decay * average + (1 - average_decay) * new_weight
        return (new_momentum, new_weight, new_average)

    query_new = stepped(
        query_part,
        query_momentum,
        query_average,
        owned(query_weight, query_momentum.shape[0], 0),
        D ** (-0.5),
    )
    mixer_new = stepped(
        mixer_part,
        mixer_momentum,
        mixer_average,
        owned(mixer_weight, mixer_momentum.shape[1], 1),
        mixer_spread,
    )
    output_new = stepped(
        output_part,
        output_momentum,
        output_average,
        owned(output_weight, output_momentum.shape[1], 1),
        D ** (-0.5),
    )
    inner_new = stepped(
        inner_part,
        inner_momentum,
        inner_average,
        owned(inner_weight, inner_momentum.shape[0], 0),
        D ** (-0.5),
    )
    outer_new = stepped(
        outer_part,
        outer_momentum,
        outer_average,
        owned(outer_weight, outer_momentum.shape[1], 1),
        FF ** (-0.5),
    )
    return (
        output,
        input_grad,
        query_new[0],
        query_new[1],
        query_new[2],
        mixer_new[0],
        mixer_new[1],
        mixer_new[2],
        output_new[0],
        output_new[1],
        output_new[2],
        inner_new[0],
        inner_new[1],
        inner_new[2],
        outer_new[0],
        outer_new[1],
        outer_new[2],
    )


def solution(mesh):
    return jax.shard_map(
        on_device,
        mesh=mesh,
        in_specs=(
            P("dp", None, "head"),
            P("dp", None, "head"),
            P("head", None),
            P(None, "dp", None),
            P(None, "head"),
            P("head", None, None),
            P("head", None),
            P(None, "head"),
            P("head", None),
            P("dp", "head"),
            P("dp", "head"),
            P("head", "dp", None),
            P("head", "dp", None),
            P("head", "dp"),
            P("head", "dp"),
            P("dp", "head"),
            P("dp", "head"),
            P("head", "dp"),
            P("head", "dp"),
        ),
        out_specs=(
            P("dp", None, "head"),
            P("dp", None, "head"),
            P("dp", "head"),
            P("dp", "head"),
            P("dp", "head"),
            P("head", "dp", None),
            P("head", "dp", None),
            P("head", "dp", None),
            P("head", "dp"),
            P("head", "dp"),
            P("head", "dp"),
            P("dp", "head"),
            P("dp", "head"),
            P("dp", "head"),
            P("head", "dp"),
            P("head", "dp"),
            P("head", "dp"),
        ),
        check_vma=False,
    )
```

```python
import math

import jax
import jax.numpy as jnp
import numpy as np
from jax import lax
from jax.sharding import PartitionSpec as P

D = 512
FF = 2048


highest = lax.Precision.HIGHEST
pool_sizes = (7, 12, 14, 24, 48)
mixer_spread = 0.07
momentum_decay = 0.9
average_decay = 0.9


def pool_tables(length):
    tables = np.zeros((len(pool_sizes), length, length), np.float32)
    rows_all = np.arange(length)
    for pool_index, pool_width in enumerate(pool_sizes):
        lead_pad = (pool_width - 1) // 2
        for offset in range(pool_width):
            source = np.clip(rows_all - lead_pad + offset, 0, length - 1)
            tables[pool_index][rows_all, source] += np.float32(1.0 / pool_width)
    return jnp.asarray(tables)


def spectral_tables(modes, length):
    positions = jnp.arange(length, dtype=jnp.int32)
    phase = modes[:, :, None] * positions[None, None, :] % length
    angle = phase.astype(jnp.float32) * (2.0 * math.pi / length)
    cosine = jnp.cos(angle)
    sine = jnp.sin(angle)
    doubled = jnp.where((modes == 0) | (2 * modes == length), 1.0, 2.0).astype(jnp.float32) / length
    inv_cos = jnp.transpose(doubled[:, :, None] * cosine, (0, 2, 1))
    inv_sin = jnp.transpose(-doubled[:, :, None] * sine, (0, 2, 1))
    return (cosine, -sine, inv_cos, inv_sin)


def product(form, left, right):
    return jnp.einsum(form, left, right, preferred_element_type=jnp.float32)


def pool_counts(length):
    counts = np.zeros((len(pool_sizes), length, length), np.float32)
    rows_all = np.arange(length)
    for pool_index, pool_width in enumerate(pool_sizes):
        lead_pad = (pool_width - 1) // 2
        for offset in range(pool_width):
            source = np.clip(rows_all - lead_pad + offset, 0, length - 1)
            counts[pool_index][rows_all, source] += 1.0
    return counts


def pool_rows(picks, length):
    counts = pool_counts(length)
    rows = jnp.zeros(picks.shape + (length,), jnp.float32)
    scale = jnp.zeros(picks.shape, jnp.float32)
    for pool_index, pool_width in enumerate(pool_sizes):
        chosen = picks == pool_index
        rows = jnp.where(chosen[..., None], jnp.asarray(counts[pool_index])[None], rows)
        scale = jnp.where(chosen, np.float32(1.0 / pool_width), scale)
    return rows.astype(jnp.bfloat16), scale


def split_three(values):
    high = values.astype(jnp.bfloat16)
    rest = values - high.astype(jnp.float32)
    middle = rest.astype(jnp.bfloat16)
    low = (rest - middle.astype(jnp.float32)).astype(jnp.bfloat16)
    return high, middle, low


def trend_local(values, rows):
    counts, scale = rows
    parts = jnp.concatenate(split_three(values), axis=1)
    tiled = jnp.concatenate([counts] * 3, axis=2)
    summed = jnp.einsum("wts,wsd->wtd", tiled, parts, preferred_element_type=jnp.float32)
    return summed * scale[..., None]


def trend_back(grads, rows):
    counts, scale = rows
    parts = jnp.concatenate(split_three(grads * scale[..., None]), axis=1)
    tiled = jnp.concatenate([counts] * 3, axis=1)
    return jnp.einsum("wts,wtd->wsd", tiled, parts, preferred_element_type=jnp.float32)


def mixer_block(mixer_low, head_size):
    head_count = mixer_low.shape[0]
    shaped = mixer_low.reshape(head_count, -1, head_size, 2 * head_size)
    real_part = shaped[..., :head_size]
    imag_part = shaped[..., head_size:]
    upper = jnp.concatenate([real_part, imag_part], axis=-1)
    lower = jnp.concatenate([-imag_part, real_part], axis=-1)
    return jnp.concatenate([upper, lower], axis=2)


def exact_gelu(values):
    return jax.nn.gelu(values, approximate=False)


def on_device(
    inputs,
    out_grad,
    modes,
    gates,
    query_weight,
    mixer_weight,
    output_weight,
    inner_weight,
    outer_weight,
    query_momentum,
    query_average,
    mixer_momentum,
    mixer_average,
    output_momentum,
    output_average,
    inner_momentum,
    inner_average,
    outer_momentum,
    outer_average,
):
    windows, length, local_width = inputs.shape
    head_count, mode_count = modes.shape
    head_size = local_width // head_count
    hidden_width = inner_weight.shape[1]
    head_parts = lax.axis_size("head")
    me = lax.axis_index("head")
    shifts = list(range(1, head_parts))

    def peer(shift):
        return (me + shift) % head_parts

    def swap(values, shift):
        pairs = [(j, (j + shift) % head_parts) for j in range(head_parts)]
        return lax.ppermute(values, "head", pairs)

    def rows_of(weight, block, size):
        return lax.dynamic_slice_in_dim(weight, block * size, size, 0)

    def cols_of(weight, block, size):
        return lax.dynamic_slice_in_dim(weight, block * size, size, 1)

    def gathered_product(mine, weight_low, size):
        received = {s: swap(mine, s) for s in shifts}
        total = product("wtd,de->wte", mine, rows_of(weight_low, me, size))
        for s in shifts:
            owner = (me - s) % head_parts
            total = total + product("wtd,de->wte", received[s], rows_of(weight_low, owner, size))
        return total, received

    def scattered_product(values, weight_low, size, after=()):
        outgoing = {
            s: product("wte,ed->wtd", values, cols_of(weight_low, peer(s), size)).astype(jnp.bfloat16)
            for s in shifts
        }
        if after:
            outgoing, _ = lax.optimization_barrier((outgoing, tuple(after)))
        sent = {s: swap(outgoing[s], s) for s in shifts}
        total = product("wte,ed->wtd", values, cols_of(weight_low, me, size))
        for s in shifts:
            total = total + sent[s].astype(jnp.float32)
        return total, sent

    def placed_rows(parts, size, total_rows):
        out = jnp.zeros((total_rows,) + parts[0][1].shape[1:], jnp.float32)
        for block, part in parts:
            out = lax.dynamic_update_slice_in_dim(out, part, block * size, 0)
        return out

    def placed_cols(parts, size, total_cols):
        out = jnp.zeros(parts[0][1].shape[:1] + (total_cols,), jnp.float32)
        for block, part in parts:
            out = lax.dynamic_update_slice_in_dim(out, part, block * size, 1)
        return out

    model_width = local_width * head_parts
    pools = pool_tables(length)
    fwd_cos, fwd_sin, inv_cos, inv_sin = [
        one_table.astype(jnp.bfloat16) for one_table in spectral_tables(modes, length)
    ]
    query_low = query_weight.astype(jnp.bfloat16)
    output_low = output_weight.astype(jnp.bfloat16)
    inner_low = inner_weight.astype(jnp.bfloat16)
    outer_low = outer_weight.astype(jnp.bfloat16)
    inner_t = jnp.transpose(inner_low)
    query_t = jnp.transpose(query_low)
    block = mixer_block(mixer_weight.astype(jnp.bfloat16), head_size)

    def chunk_pass(inputs, out_grad, first_rows, second_rows):
        windows = inputs.shape[0]
        grad_comb = out_grad - trend_back(out_grad, second_rows)
        grad_feed_mine = grad_comb.astype(jnp.bfloat16)

        inputs_mine = inputs.astype(jnp.bfloat16)
        query, inputs_recv = gathered_product(inputs_mine, query_low, local_width)
        grad_feed_recv = {s: swap(grad_feed_mine, s) for s in shifts}
        query = query.astype(jnp.bfloat16)
        query_heads = query.reshape(windows, length, head_count, head_size)
        spectrum = jnp.concatenate(
            [
                product("hmt,wthe->whme", fwd_cos, query_heads),
                product("hmt,wthe->whme", fwd_sin, query_heads),
            ],
            axis=-1,
        ).astype(jnp.bfloat16)
        mixed = product("whmi,hmio->whmo", spectrum, block).astype(jnp.bfloat16)
        field = product("htm,whme->wthe", inv_cos, mixed[..., :head_size]) + product(
            "htm,whme->wthe", inv_sin, mixed[..., head_size:]
        )
        field = field.reshape(windows, length, local_width).astype(jnp.bfloat16)
        attended, _ = scattered_product(field, output_low, local_width)
        resid_one = inputs + attended
        seasonal = resid_one - trend_local(resid_one, first_rows)
        seasonal_mine = seasonal.astype(jnp.bfloat16)
        pre, seasonal_recv = gathered_product(seasonal_mine, inner_low, local_width)
        activated, gelu_pull = jax.vjp(exact_gelu, pre)
        hidden = activated.astype(jnp.bfloat16)

        outer_grad_t = placed_rows(
            [(me, product("wtd,wtf->df", grad_feed_mine, hidden))]
            + [((me - s) % head_parts, product("wtd,wtf->df", grad_feed_recv[s], hidden)) for s in shifts],
            local_width,
            model_width,
        )
        grad_hidden = product("wtd,fd->wtf", grad_feed_mine, cols_of(outer_low, me, local_width))
        for s in shifts:
            grad_hidden = grad_hidden + product(
                "wtd,fd->wtf", grad_feed_recv[s], cols_of(outer_low, (me - s) % head_parts, local_width)
            )
        grad_pre = gelu_pull(grad_hidden)[0].astype(jnp.bfloat16)
        inner_grad = placed_rows(
            [(me, product("wtd,wtf->df", seasonal_mine, grad_pre))]
            + [((me - s) % head_parts, product("wtd,wtf->df", seasonal_recv[s], grad_pre)) for s in shifts],
            local_width,
            model_width,
        )
        grad_season_part, _ = scattered_product(grad_pre, inner_t, local_width)
        grad_season = grad_comb + grad_season_part
        grad_resid = grad_season - trend_back(grad_season, first_rows)
        grad_attend_mine = grad_resid.astype(jnp.bfloat16)
        grad_attend_recv = {s: swap(grad_attend_mine, s) for s in shifts}
        feed, feed_sent = scattered_product(hidden, outer_low, local_width, after=grad_attend_recv.values())
        combined = seasonal + feed
        output = combined - trend_local(combined, second_rows)
        output_grad_t = placed_rows(
            [(me, product("wtd,wte->de", grad_attend_mine, field))]
            + [((me - s) % head_parts, product("wtd,wte->de", grad_attend_recv[s], field)) for s in shifts],
            local_width,
            model_width,
        )
        grad_field = product("wtd,ed->wte", grad_attend_mine, cols_of(output_low, me, local_width))
        for s in shifts:
            grad_field = grad_field + product(
                "wtd,ed->wte", grad_attend_recv[s], cols_of(output_low, (me - s) % head_parts, local_width)
            )
        grad_field = grad_field.astype(jnp.bfloat16)
        grad_field = grad_field.reshape(windows, length, head_count, head_size)
        grad_mixed = jnp.concatenate(
            [
                product("htm,wthe->whme", inv_cos, grad_field),
                product("htm,wthe->whme", inv_sin, grad_field),
            ],
            axis=-1,
        ).astype(jnp.bfloat16)
        grad_spectrum = product("whmo,hmio->whmi", grad_mixed, block).astype(jnp.bfloat16)
        grad_query = product("hmt,whme->wthe", fwd_cos, grad_spectrum[..., :head_size]) + product(
            "hmt,whme->wthe", fwd_sin, grad_spectrum[..., head_size:]
        )
        grad_query = grad_query.reshape(windows, length, local_width).astype(jnp.bfloat16)
        query_grad = placed_rows(
            [(me, product("wtd,wte->de", inputs_mine, grad_query))]
            + [((me - s) % head_parts, product("wtd,wte->de", inputs_recv[s], grad_query)) for s in shifts],
            local_width,
            model_width,
        )
        input_part, _ = scattered_product(grad_query, query_t, local_width, after=feed_sent.values())
        input_grad = grad_resid + input_part
        spectrum_parts = spectrum.reshape(windows, head_count, mode_count, 2, head_size)
        grad_real = grad_mixed[..., :head_size]
        grad_imag = grad_mixed[..., head_size:]
        paired = jnp.stack(
            [grad_mixed, jnp.concatenate([grad_imag, -grad_real], axis=-1)], axis=3
        )
        mixer_full = product("whmci,whmco->hmio", spectrum_parts, paired).reshape(
            head_count, mode_count * head_size, 2 * head_size
        )
        return output, input_grad, (query_grad, mixer_full, output_grad_t, inner_grad, outer_grad_t)

    chunks = 1
    span = windows // chunks
    first_all = pool_rows(gates[0], length)
    second_all = pool_rows(gates[1], length)
    results = [
        chunk_pass(
            inputs[c * span : (c + 1) * span],
            out_grad[c * span : (c + 1) * span],
            tuple(part[c * span : (c + 1) * span] for part in first_all),
            tuple(part[c * span : (c + 1) * span] for part in second_all),
        )
        for c in range(chunks)
    ]
    output = jnp.concatenate([r[0] for r in results], axis=0)
    input_grad = jnp.concatenate([r[1] for r in results], axis=0)
    query_grad, mixer_full, output_grad_t, inner_grad, outer_grad_t = [
        sum(r[2][i] for r in results[1:]) + results[0][2][i] if chunks > 1 else results[0][2][i]
        for i in range(5)
    ]

    dp_count = lax.axis_size("dp")
    dp_rank = lax.axis_index("dp")

    lanes = 128

    def lead(grad, axis_number):
        shape = grad.shape
        split = shape[:axis_number] + (dp_count, shape[axis_number] // dp_count) + shape[axis_number + 1 :]
        owned_shape = shape[:axis_number] + (shape[axis_number] // dp_count,) + shape[axis_number + 1 :]
        return jnp.moveaxis(grad.reshape(split), axis_number, 0).reshape(dp_count, -1, lanes), owned_shape

    def reduced_over_dp(grads_axes):
        laid = [lead(grad, axis_number) for grad, axis_number in grads_axes]
        joined = jnp.concatenate([flat for flat, _ in laid], axis=1)
        reduced = lax.psum_scatter(
            joined.reshape(-1, lanes), "dp", scatter_dimension=0, tiled=True
        )
        parts = []
        offset = 0
        for flat, owned_shape in laid:
            rows = flat.shape[1]
            parts.append(reduced[offset : offset + rows].reshape(owned_shape))
            offset += rows
        return parts

    def summed_over_dp(grads_axes):
        laid = [lead(grad, axis_number) for grad, axis_number in grads_axes]
        joined = jnp.concatenate([flat for flat, _ in laid], axis=1)
        rows = joined.shape[1]
        arrived = lax.all_to_all(
            joined.astype(jnp.bfloat16).reshape(-1, lanes), "dp", 0, 0, tiled=True
        )
        reduced = jnp.sum(arrived.astype(jnp.float32).reshape(dp_count, rows, lanes), axis=0)
        parts = []
        offset = 0
        for flat, owned_shape in laid:
            size = flat.shape[1]
            parts.append(reduced[offset : offset + size].reshape(owned_shape))
            offset += size
        return parts

    inner_part, outer_part_t = reduced_over_dp([(inner_grad, 0), (outer_grad_t, 0)])
    mixer_part, output_part_t, query_part = summed_over_dp(
        [(mixer_full, 1), (output_grad_t, 0), (query_grad, 0)]
    )
    output_part = jnp.transpose(output_part_t)
    outer_part = jnp.transpose(outer_part_t)
    token_total = windows * length * dp_count

    def owned(weight, share, axis_number):
        return lax.dynamic_slice_in_dim(weight, dp_rank * share, share, axis_number)

    def stepped(grad, momentum, average, old_weight, spread):
        rate = 0.5 * spread / math.sqrt(token_total)
        new_momentum = momentum_decay * momentum + grad
        new_weight = old_weight - rate * (grad + momentum_decay * new_momentum)
        new_average = average_decay * average + (1 - average_decay) * new_weight
        return (new_momentum, new_weight, new_average)

    query_new = stepped(
        query_part,
        query_momentum,
        query_average,
        owned(query_weight, query_momentum.shape[0], 0),
        D ** (-0.5),
    )
    mixer_new = stepped(
        mixer_part,
        mixer_momentum,
        mixer_average,
        owned(mixer_weight, mixer_momentum.shape[1], 1),
        mixer_spread,
    )
    output_new = stepped(
        output_part,
        output_momentum,
        output_average,
        owned(output_weight, output_momentum.shape[1], 1),
        D ** (-0.5),
    )
    inner_new = stepped(
        inner_part,
        inner_momentum,
        inner_average,
        owned(inner_weight, inner_momentum.shape[0], 0),
        D ** (-0.5),
    )
    outer_new = stepped(
        outer_part,
        outer_momentum,
        outer_average,
        owned(outer_weight, outer_momentum.shape[1], 1),
        FF ** (-0.5),
    )
    return (
        output,
        input_grad,
        query_new[0],
        query_new[1],
        query_new[2],
        mixer_new[0],
        mixer_new[1],
        mixer_new[2],
        output_new[0],
        output_new[1],
        output_new[2],
        inner_new[0],
        inner_new[1],
        inner_new[2],
        outer_new[0],
        outer_new[1],
        outer_new[2],
    )


def solution(mesh):
    return jax.shard_map(
        on_device,
        mesh=mesh,
        in_specs=(
            P("dp", None, "head"),
            P("dp", None, "head"),
            P("head", None),
            P(None, "dp", None),
            P(None, "head"),
            P("head", None, None),
            P("head", None),
            P(None, "head"),
            P("head", None),
            P("dp", "head"),
            P("dp", "head"),
            P("head", "dp", None),
            P("head", "dp", None),
            P("head", "dp"),
            P("head", "dp"),
            P("dp", "head"),
            P("dp", "head"),
            P("head", "dp"),
            P("head", "dp"),
        ),
        out_specs=(
            P("dp", None, "head"),
            P("dp", None, "head"),
            P("dp", "head"),
            P("dp", "head"),
            P("dp", "head"),
            P("head", "dp", None),
            P("head", "dp", None),
            P("head", "dp", None),
            P("head", "dp"),
            P("head", "dp"),
            P("head", "dp"),
            P("dp", "head"),
            P("dp", "head"),
            P("dp", "head"),
            P("head", "dp"),
            P("head", "dp"),
            P("head", "dp"),
        ),
        check_vma=False,
    )
```

```python
import math

import jax
import jax.numpy as jnp
import numpy as np
from jax import lax
from jax.sharding import PartitionSpec as P


D = 512
FF = 2048


pool_sizes = (7, 12, 14, 24, 48)
mixer_spread = 0.07
momentum_decay = 0.9
average_decay = 0.9


def pool_tables(length):
    tables = np.zeros((len(pool_sizes), length, length), np.float32)
    rows_all = np.arange(length)
    for pool_index, pool_width in enumerate(pool_sizes):
        lead_pad = (pool_width - 1) // 2
        for offset in range(pool_width):
            source = np.clip(rows_all - lead_pad + offset, 0, length - 1)
            tables[pool_index][rows_all, source] += np.float32(1.0 / pool_width)
    return jnp.asarray(tables)


def spectral_tables(modes, length):
    positions = jnp.arange(length, dtype=jnp.int32)
    phase = modes[:, :, None] * positions[None, None, :] % length
    angle = phase.astype(jnp.float32) * (2.0 * math.pi / length)
    cosine = jnp.cos(angle)
    sine = jnp.sin(angle)
    doubled = jnp.where((modes == 0) | (2 * modes == length), 1.0, 2.0).astype(jnp.float32) / length
    inv_cos = jnp.transpose(doubled[:, :, None] * cosine, (0, 2, 1))
    inv_sin = jnp.transpose(-doubled[:, :, None] * sine, (0, 2, 1))
    return (cosine, -sine, inv_cos, inv_sin)


def product(form, left, right):
    return jnp.einsum(form, left, right, preferred_element_type=jnp.float32)


def pool_counts(length):
    counts = np.zeros((len(pool_sizes), length, length), np.float32)
    rows_all = np.arange(length)
    for pool_index, pool_width in enumerate(pool_sizes):
        lead_pad = (pool_width - 1) // 2
        for offset in range(pool_width):
            source = np.clip(rows_all - lead_pad + offset, 0, length - 1)
            counts[pool_index][rows_all, source] += 1.0
    return counts


def pool_rows(picks, length):
    counts = pool_counts(length)
    rows = jnp.zeros(picks.shape + (length,), jnp.float32)
    scale = jnp.zeros(picks.shape, jnp.float32)
    for pool_index, pool_width in enumerate(pool_sizes):
        chosen = picks == pool_index
        rows = jnp.where(chosen[..., None], jnp.asarray(counts[pool_index])[None], rows)
        scale = jnp.where(chosen, np.float32(1.0 / pool_width), scale)
    return rows.astype(jnp.bfloat16), scale


def split_three(values):
    high = values.astype(jnp.bfloat16)
    rest = values - high.astype(jnp.float32)
    middle = rest.astype(jnp.bfloat16)
    low = (rest - middle.astype(jnp.float32)).astype(jnp.bfloat16)
    return high, middle, low


def trend_local(values, rows):
    counts, scale = rows
    parts = jnp.concatenate(split_three(values), axis=1)
    tiled = jnp.concatenate([counts] * 3, axis=2)
    summed = jnp.einsum("wts,wsd->wtd", tiled, parts, preferred_element_type=jnp.float32)
    return summed * scale[..., None]


def trend_back(grads, rows):
    counts, scale = rows
    parts = jnp.concatenate(split_three(grads * scale[..., None]), axis=1)
    tiled = jnp.concatenate([counts] * 3, axis=1)
    return jnp.einsum("wts,wtd->wsd", tiled, parts, preferred_element_type=jnp.float32)


def mixer_block(mixer_low, head_size):
    head_count = mixer_low.shape[0]
    shaped = mixer_low.reshape(head_count, -1, head_size, 2 * head_size)
    real_part = shaped[..., :head_size]
    imag_part = shaped[..., head_size:]
    upper = jnp.concatenate([real_part, imag_part], axis=-1)
    lower = jnp.concatenate([-imag_part, real_part], axis=-1)
    return jnp.concatenate([upper, lower], axis=2)


def exact_gelu(values):
    return jax.nn.gelu(values, approximate=False)


def on_device(
    inputs,
    out_grad,
    modes,
    gates,
    query_weight,
    mixer_weight,
    output_weight,
    inner_weight,
    outer_weight,
    query_momentum,
    query_average,
    mixer_momentum,
    mixer_average,
    output_momentum,
    output_average,
    inner_momentum,
    inner_average,
    outer_momentum,
    outer_average,
):
    windows, length, local_width = inputs.shape
    head_count, mode_count = modes.shape
    head_size = local_width // head_count
    head_parts = lax.axis_size("head")
    me = lax.axis_index("head")
    shifts = list(range(1, head_parts))

    def peer(shift):
        return (me + shift) % head_parts

    def swap(values, shift):
        pairs = [(j, (j + shift) % head_parts) for j in range(head_parts)]
        return lax.ppermute(values, "head", pairs)

    def rows_of(weight, block, size):
        return lax.dynamic_slice_in_dim(weight, block * size, size, 0)

    def cols_of(weight, block, size):
        return lax.dynamic_slice_in_dim(weight, block * size, size, 1)

    def gathered_product(mine, weight_low, size):
        received = {s: swap(mine, s) for s in shifts}
        total = product("wtd,de->wte", mine, rows_of(weight_low, me, size))
        for s in shifts:
            owner = (me - s) % head_parts
            total = total + product("wtd,de->wte", received[s], rows_of(weight_low, owner, size))
        return total, received

    def scattered_product(values, weight_low, size, after=()):
        outgoing = {
            s: product("wte,ed->wtd", values, cols_of(weight_low, peer(s), size)).astype(jnp.bfloat16)
            for s in shifts
        }
        if after:
            outgoing, _ = lax.optimization_barrier((outgoing, tuple(after)))
        sent = {s: swap(outgoing[s], s) for s in shifts}
        total = product("wte,ed->wtd", values, cols_of(weight_low, me, size))
        for s in shifts:
            total = total + sent[s].astype(jnp.float32)
        return total, sent

    def placed_rows(parts, size, total_rows):
        out = jnp.zeros((total_rows,) + parts[0][1].shape[1:], jnp.float32)
        for block, part in parts:
            out = lax.dynamic_update_slice_in_dim(out, part, block * size, 0)
        return out

    model_width = local_width * head_parts
    pools = pool_tables(length)
    fwd_cos, fwd_sin, inv_cos, inv_sin = [
        one_table.astype(jnp.bfloat16) for one_table in spectral_tables(modes, length)
    ]
    query_low = query_weight.astype(jnp.bfloat16)
    output_low = output_weight.astype(jnp.bfloat16)
    inner_low = inner_weight.astype(jnp.bfloat16)
    outer_low = outer_weight.astype(jnp.bfloat16)
    inner_t = jnp.transpose(inner_low)
    query_t = jnp.transpose(query_low)
    block = mixer_block(mixer_weight.astype(jnp.bfloat16), head_size)

    def chunk_pass(inputs, out_grad, first_rows, second_rows):
        windows = inputs.shape[0]
        grad_comb = out_grad - trend_back(out_grad, second_rows)
        grad_feed_mine = grad_comb.astype(jnp.bfloat16)

        inputs_mine = inputs.astype(jnp.bfloat16)
        query, inputs_recv = gathered_product(inputs_mine, query_low, local_width)
        grad_feed_recv = {s: swap(grad_feed_mine, s) for s in shifts}
        query = query.astype(jnp.bfloat16)
        query_heads = query.reshape(windows, length, head_count, head_size)
        spectrum = jnp.concatenate(
            [
                product("hmt,wthe->whme", fwd_cos, query_heads),
                product("hmt,wthe->whme", fwd_sin, query_heads),
            ],
            axis=-1,
        ).astype(jnp.bfloat16)
        mixed = product("whmi,hmio->whmo", spectrum, block).astype(jnp.bfloat16)
        field = product("htm,whme->wthe", inv_cos, mixed[..., :head_size]) + product(
            "htm,whme->wthe", inv_sin, mixed[..., head_size:]
        )
        field = field.reshape(windows, length, local_width).astype(jnp.bfloat16)
        attended, _ = scattered_product(field, output_low, local_width)
        resid_one = inputs + attended
        seasonal = resid_one - trend_local(resid_one, first_rows)
        seasonal_mine = seasonal.astype(jnp.bfloat16)
        pre, seasonal_recv = gathered_product(seasonal_mine, inner_low, local_width)
        activated, gelu_pull = jax.vjp(exact_gelu, pre)
        hidden = activated.astype(jnp.bfloat16)

        outer_grad_t = placed_rows(
            [(me, product("wtd,wtf->df", grad_feed_mine, hidden))]
            + [((me - s) % head_parts, product("wtd,wtf->df", grad_feed_recv[s], hidden)) for s in shifts],
            local_width,
            model_width,
        )
        grad_hidden = product("wtd,fd->wtf", grad_feed_mine, cols_of(outer_low, me, local_width))
        for s in shifts:
            grad_hidden = grad_hidden + product(
                "wtd,fd->wtf", grad_feed_recv[s], cols_of(outer_low, (me - s) % head_parts, local_width)
            )
        grad_pre = gelu_pull(grad_hidden)[0].astype(jnp.bfloat16)
        inner_grad = placed_rows(
            [(me, product("wtd,wtf->df", seasonal_mine, grad_pre))]
            + [((me - s) % head_parts, product("wtd,wtf->df", seasonal_recv[s], grad_pre)) for s in shifts],
            local_width,
            model_width,
        )
        grad_season_part, _ = scattered_product(grad_pre, inner_t, local_width)
        grad_season = grad_comb + grad_season_part
        grad_resid = grad_season - trend_back(grad_season, first_rows)
        grad_attend_mine = grad_resid.astype(jnp.bfloat16)
        grad_attend_recv = {s: swap(grad_attend_mine, s) for s in shifts}
        feed, feed_sent = scattered_product(hidden, outer_low, local_width, after=grad_attend_recv.values())
        combined = seasonal + feed
        output = combined - trend_local(combined, second_rows)
        output_grad_t = placed_rows(
            [(me, product("wtd,wte->de", grad_attend_mine, field))]
            + [((me - s) % head_parts, product("wtd,wte->de", grad_attend_recv[s], field)) for s in shifts],
            local_width,
            model_width,
        )
        grad_field = product("wtd,ed->wte", grad_attend_mine, cols_of(output_low, me, local_width))
        for s in shifts:
            grad_field = grad_field + product(
                "wtd,ed->wte", grad_attend_recv[s], cols_of(output_low, (me - s) % head_parts, local_width)
            )
        grad_field = grad_field.astype(jnp.bfloat16)
        grad_field = grad_field.reshape(windows, length, head_count, head_size)
        grad_mixed = jnp.concatenate(
            [
                product("htm,wthe->whme", inv_cos, grad_field),
                product("htm,wthe->whme", inv_sin, grad_field),
            ],
            axis=-1,
        ).astype(jnp.bfloat16)
        grad_spectrum = product("whmo,hmio->whmi", grad_mixed, block).astype(jnp.bfloat16)
        grad_query = product("hmt,whme->wthe", fwd_cos, grad_spectrum[..., :head_size]) + product(
            "hmt,whme->wthe", fwd_sin, grad_spectrum[..., head_size:]
        )
        grad_query = grad_query.reshape(windows, length, local_width).astype(jnp.bfloat16)
        query_grad = placed_rows(
            [(me, product("wtd,wte->de", inputs_mine, grad_query))]
            + [((me - s) % head_parts, product("wtd,wte->de", inputs_recv[s], grad_query)) for s in shifts],
            local_width,
            model_width,
        )
        input_part, _ = scattered_product(grad_query, query_t, local_width, after=feed_sent.values())
        input_grad = grad_resid + input_part
        spectrum_parts = spectrum.reshape(windows, head_count, mode_count, 2, head_size)
        grad_real = grad_mixed[..., :head_size]
        grad_imag = grad_mixed[..., head_size:]
        paired = jnp.stack(
            [grad_mixed, jnp.concatenate([grad_imag, -grad_real], axis=-1)], axis=3
        )
        mixer_full = product("whmci,whmco->hmio", spectrum_parts, paired).reshape(
            head_count, mode_count * head_size, 2 * head_size
        )
        return output, input_grad, (query_grad, mixer_full, output_grad_t, inner_grad, outer_grad_t)

    chunks = 1
    span = windows // chunks
    first_all = pool_rows(gates[0], length)
    second_all = pool_rows(gates[1], length)
    results = [
        chunk_pass(
            inputs[c * span : (c + 1) * span],
            out_grad[c * span : (c + 1) * span],
            tuple(part[c * span : (c + 1) * span] for part in first_all),
            tuple(part[c * span : (c + 1) * span] for part in second_all),
        )
        for c in range(chunks)
    ]
    output = jnp.concatenate([r[0] for r in results], axis=0)
    input_grad = jnp.concatenate([r[1] for r in results], axis=0)
    query_grad, mixer_full, output_grad_t, inner_grad, outer_grad_t = [
        sum(r[2][i] for r in results[1:]) + results[0][2][i] if chunks > 1 else results[0][2][i]
        for i in range(5)
    ]

    dp_count = lax.axis_size("dp")
    dp_rank = lax.axis_index("dp")

    lanes = 128

    def lead(grad, axis_number):
        shape = grad.shape
        split = shape[:axis_number] + (dp_count, shape[axis_number] // dp_count) + shape[axis_number + 1 :]
        owned_shape = shape[:axis_number] + (shape[axis_number] // dp_count,) + shape[axis_number + 1 :]
        return jnp.moveaxis(grad.reshape(split), axis_number, 0).reshape(dp_count, -1, lanes), owned_shape

    def reduced_over_dp(grads_axes):
        laid = [lead(grad, axis_number) for grad, axis_number in grads_axes]
        joined = jnp.concatenate([flat for flat, _ in laid], axis=1)
        reduced = lax.psum_scatter(
            joined.reshape(-1, lanes), "dp", scatter_dimension=0, tiled=True
        )
        parts = []
        offset = 0
        for flat, owned_shape in laid:
            rows = flat.shape[1]
            parts.append(reduced[offset : offset + rows].reshape(owned_shape))
            offset += rows
        return parts

    def summed_over_dp(grads_axes):
        laid = [lead(grad, axis_number) for grad, axis_number in grads_axes]
        joined = jnp.concatenate([flat for flat, _ in laid], axis=1)
        rows = joined.shape[1]
        arrived = lax.all_to_all(
            joined.astype(jnp.bfloat16).reshape(-1, lanes), "dp", 0, 0, tiled=True
        )
        reduced = jnp.sum(arrived.astype(jnp.float32).reshape(dp_count, rows, lanes), axis=0)
        parts = []
        offset = 0
        for flat, owned_shape in laid:
            size = flat.shape[1]
            parts.append(reduced[offset : offset + size].reshape(owned_shape))
            offset += size
        return parts

    inner_part, outer_part_t = reduced_over_dp([(inner_grad, 0), (outer_grad_t, 0)])
    mixer_part, output_part_t, query_part = summed_over_dp(
        [(mixer_full, 1), (output_grad_t, 0), (query_grad, 0)]
    )
    output_part = jnp.transpose(output_part_t)
    outer_part = jnp.transpose(outer_part_t)
    token_total = windows * length * dp_count

    def owned(weight, share, axis_number):
        return lax.dynamic_slice_in_dim(weight, dp_rank * share, share, axis_number)

    def stepped(grad, momentum, average, old_weight, spread):
        rate = 0.5 * spread / math.sqrt(token_total)
        new_momentum = momentum_decay * momentum + grad
        new_weight = old_weight - rate * (grad + momentum_decay * new_momentum)
        new_average = average_decay * average + (1 - average_decay) * new_weight
        return (new_momentum, new_weight, new_average)

    query_new = stepped(
        query_part,
        query_momentum,
        query_average,
        owned(query_weight, query_momentum.shape[0], 0),
        D ** (-0.5),
    )
    mixer_new = stepped(
        mixer_part,
        mixer_momentum,
        mixer_average,
        owned(mixer_weight, mixer_momentum.shape[1], 1),
        mixer_spread,
    )
    output_new = stepped(
        output_part,
        output_momentum,
        output_average,
        owned(output_weight, output_momentum.shape[1], 1),
        D ** (-0.5),
    )
    inner_new = stepped(
        inner_part,
        inner_momentum,
        inner_average,
        owned(inner_weight, inner_momentum.shape[0], 0),
        D ** (-0.5),
    )
    outer_new = stepped(
        outer_part,
        outer_momentum,
        outer_average,
        owned(outer_weight, outer_momentum.shape[1], 1),
        FF ** (-0.5),
    )
    return (
        output,
        input_grad,
        query_new[0],
        query_new[1],
        query_new[2],
        mixer_new[0],
        mixer_new[1],
        mixer_new[2],
        output_new[0],
        output_new[1],
        output_new[2],
        inner_new[0],
        inner_new[1],
        inner_new[2],
        outer_new[0],
        outer_new[1],
        outer_new[2],
    )


def solution(mesh):
    return jax.shard_map(
        on_device,
        mesh=mesh,
        in_specs=(
            P("dp", None, "head"),
            P("dp", None, "head"),
            P("head", None),
            P(None, "dp", None),
            P(None, "head"),
            P("head", None, None),
            P("head", None),
            P(None, "head"),
            P("head", None),
            P("dp", "head"),
            P("dp", "head"),
            P("head", "dp", None),
            P("head", "dp", None),
            P("head", "dp"),
            P("head", "dp"),
            P("dp", "head"),
            P("dp", "head"),
            P("head", "dp"),
            P("head", "dp"),
        ),
        out_specs=(
            P("dp", None, "head"),
            P("dp", None, "head"),
            P("dp", "head"),
            P("dp", "head"),
            P("dp", "head"),
            P("head", "dp", None),
            P("head", "dp", None),
            P("head", "dp", None),
            P("head", "dp"),
            P("head", "dp"),
            P("head", "dp"),
            P("dp", "head"),
            P("dp", "head"),
            P("dp", "head"),
            P("head", "dp"),
            P("head", "dp"),
            P("head", "dp"),
        ),
        check_vma=False,
    )
```

```python
import math

import jax
import jax.numpy as jnp
import numpy as np
from jax import lax
from jax.sharding import PartitionSpec as P


D = 512
FF = 2048


pool_sizes = (7, 12, 14, 24, 48)
mixer_spread = 0.07
momentum_decay = 0.9
average_decay = 0.9


def pool_tables(length):
    tables = np.zeros((len(pool_sizes), length, length), np.float32)
    rows_all = np.arange(length)
    for pool_index, pool_width in enumerate(pool_sizes):
        lead_pad = (pool_width - 1) // 2
        for offset in range(pool_width):
            source = np.clip(rows_all - lead_pad + offset, 0, length - 1)
            tables[pool_index][rows_all, source] += np.float32(1.0 / pool_width)
    return jnp.asarray(tables)


def spectral_tables(modes, length):
    positions = jnp.arange(length, dtype=jnp.int32)
    phase = modes[:, :, None] * positions[None, None, :] % length
    angle = phase.astype(jnp.float32) * (2.0 * math.pi / length)
    cosine = jnp.cos(angle)
    sine = jnp.sin(angle)
    doubled = jnp.where((modes == 0) | (2 * modes == length), 1.0, 2.0).astype(jnp.float32) / length
    inv_cos = jnp.transpose(doubled[:, :, None] * cosine, (0, 2, 1))
    inv_sin = jnp.transpose(-doubled[:, :, None] * sine, (0, 2, 1))
    return (cosine, -sine, inv_cos, inv_sin)


def product(form, left, right):
    return jnp.einsum(form, left, right, preferred_element_type=jnp.float32)


def pool_counts(length):
    counts = np.zeros((len(pool_sizes), length, length), np.float32)
    rows_all = np.arange(length)
    for pool_index, pool_width in enumerate(pool_sizes):
        lead_pad = (pool_width - 1) // 2
        for offset in range(pool_width):
            source = np.clip(rows_all - lead_pad + offset, 0, length - 1)
            counts[pool_index][rows_all, source] += 1.0
    return counts


def pool_rows(picks, length):
    counts = pool_counts(length)
    rows = jnp.zeros(picks.shape + (length,), jnp.float32)
    scale = jnp.zeros(picks.shape, jnp.float32)
    for pool_index, pool_width in enumerate(pool_sizes):
        chosen = picks == pool_index
        rows = jnp.where(chosen[..., None], jnp.asarray(counts[pool_index])[None], rows)
        scale = jnp.where(chosen, np.float32(1.0 / pool_width), scale)
    return rows.astype(jnp.bfloat16), scale


def split_three(values):
    high = values.astype(jnp.bfloat16)
    rest = values - high.astype(jnp.float32)
    middle = rest.astype(jnp.bfloat16)
    low = (rest - middle.astype(jnp.float32)).astype(jnp.bfloat16)
    return high, middle, low


def trend_local(values, rows):
    counts, scale = rows
    parts = jnp.concatenate(split_three(values), axis=1)
    tiled = jnp.concatenate([counts] * 3, axis=2)
    summed = jnp.einsum("wts,wsd->wtd", tiled, parts, preferred_element_type=jnp.float32)
    return summed * scale[..., None]


def trend_back(grads, rows):
    counts, scale = rows
    parts = jnp.concatenate(split_three(grads * scale[..., None]), axis=1)
    tiled = jnp.concatenate([counts] * 3, axis=1)
    return jnp.einsum("wts,wtd->wsd", tiled, parts, preferred_element_type=jnp.float32)


def mixer_block(mixer_low, head_size):
    head_count = mixer_low.shape[0]
    shaped = mixer_low.reshape(head_count, -1, head_size, 2 * head_size)
    real_part = shaped[..., :head_size]
    imag_part = shaped[..., head_size:]
    upper = jnp.concatenate([real_part, imag_part], axis=-1)
    lower = jnp.concatenate([-imag_part, real_part], axis=-1)
    return jnp.concatenate([upper, lower], axis=2)


def exact_gelu(values):
    return jax.nn.gelu(values, approximate=False)


def on_device(
    inputs,
    out_grad,
    modes,
    gates,
    query_weight,
    mixer_weight,
    output_weight,
    inner_weight,
    outer_weight,
    query_momentum,
    query_average,
    mixer_momentum,
    mixer_average,
    output_momentum,
    output_average,
    inner_momentum,
    inner_average,
    outer_momentum,
    outer_average,
):
    windows, length, local_width = inputs.shape
    head_count, mode_count = modes.shape
    head_size = local_width // head_count
    head_parts = lax.axis_size("head")
    me = lax.axis_index("head")
    shifts = list(range(1, head_parts))

    def peer(shift):
        return (me + shift) % head_parts

    def swap(values, shift):
        pairs = [(j, (j + shift) % head_parts) for j in range(head_parts)]
        return lax.ppermute(values, "head", pairs)

    def rows_of(weight, block, size):
        return lax.dynamic_slice_in_dim(weight, block * size, size, 0)

    def cols_of(weight, block, size):
        return lax.dynamic_slice_in_dim(weight, block * size, size, 1)

    def gathered_product(mine, weight_low, size):
        received = {s: swap(mine, s) for s in shifts}
        total = product("wtd,de->wte", mine, rows_of(weight_low, me, size))
        for s in shifts:
            owner = (me - s) % head_parts
            total = total + product("wtd,de->wte", received[s], rows_of(weight_low, owner, size))
        return total, received

    def scattered_product(values, weight_low, size, after=()):
        outgoing = {
            s: product("wte,ed->wtd", values, cols_of(weight_low, peer(s), size)).astype(jnp.bfloat16)
            for s in shifts
        }
        if after:
            outgoing, _ = lax.optimization_barrier((outgoing, tuple(after)))
        sent = {s: swap(outgoing[s], s) for s in shifts}
        total = product("wte,ed->wtd", values, cols_of(weight_low, me, size))
        for s in shifts:
            total = total + sent[s].astype(jnp.float32)
        return total, sent

    def placed_rows(parts, size, total_rows):
        out = jnp.zeros((total_rows,) + parts[0][1].shape[1:], jnp.float32)
        for block, part in parts:
            out = lax.dynamic_update_slice_in_dim(out, part, block * size, 0)
        return out

    model_width = local_width * head_parts
    pools = pool_tables(length)
    fwd_cos, fwd_sin, inv_cos, inv_sin = [
        one_table.astype(jnp.bfloat16) for one_table in spectral_tables(modes, length)
    ]
    query_low = query_weight.astype(jnp.bfloat16)
    output_low = output_weight.astype(jnp.bfloat16)
    inner_low = inner_weight.astype(jnp.bfloat16)
    outer_low = outer_weight.astype(jnp.bfloat16)
    inner_t = jnp.transpose(inner_low)
    query_t = jnp.transpose(query_low)
    block = mixer_block(mixer_weight.astype(jnp.bfloat16), head_size)
    fwd_stack = jnp.concatenate([fwd_cos, fwd_sin], axis=1)

    def chunk_pass(inputs, out_grad, first_rows, second_rows):
        windows = inputs.shape[0]
        grad_comb = out_grad - trend_back(out_grad, second_rows)
        grad_feed_mine = grad_comb.astype(jnp.bfloat16)

        inputs_mine = inputs.astype(jnp.bfloat16)
        query, inputs_recv = gathered_product(inputs_mine, query_low, local_width)
        input_spectra = [(me, product("hkt,wtd->whkd", fwd_stack, inputs_mine).astype(jnp.bfloat16))] + [
            ((me - s) % head_parts, product("hkt,wtd->whkd", fwd_stack, inputs_recv[s]).astype(jnp.bfloat16))
            for s in shifts
        ]
        grad_feed_recv = {s: swap(grad_feed_mine, s) for s in shifts}
        query = query.astype(jnp.bfloat16)
        query_heads = query.reshape(windows, length, head_count, head_size)
        spectrum = jnp.concatenate(
            [
                product("hmt,wthe->whme", fwd_cos, query_heads),
                product("hmt,wthe->whme", fwd_sin, query_heads),
            ],
            axis=-1,
        ).astype(jnp.bfloat16)
        mixed = product("whmi,hmio->whmo", spectrum, block).astype(jnp.bfloat16)
        field = product("htm,whme->wthe", inv_cos, mixed[..., :head_size]) + product(
            "htm,whme->wthe", inv_sin, mixed[..., head_size:]
        )
        field = field.reshape(windows, length, local_width).astype(jnp.bfloat16)
        attended, _ = scattered_product(field, output_low, local_width)
        resid_one = inputs + attended
        seasonal = resid_one - trend_local(resid_one, first_rows)
        seasonal_mine = seasonal.astype(jnp.bfloat16)
        pre, seasonal_recv = gathered_product(seasonal_mine, inner_low, local_width)
        activated, gelu_pull = jax.vjp(exact_gelu, pre)
        hidden = activated.astype(jnp.bfloat16)

        outer_grad_t = placed_rows(
            [(me, product("wtd,wtf->df", grad_feed_mine, hidden))]
            + [((me - s) % head_parts, product("wtd,wtf->df", grad_feed_recv[s], hidden)) for s in shifts],
            local_width,
            model_width,
        )
        grad_hidden = product("wtd,fd->wtf", grad_feed_mine, cols_of(outer_low, me, local_width))
        for s in shifts:
            grad_hidden = grad_hidden + product(
                "wtd,fd->wtf", grad_feed_recv[s], cols_of(outer_low, (me - s) % head_parts, local_width)
            )
        grad_pre = gelu_pull(grad_hidden)[0].astype(jnp.bfloat16)
        inner_grad = placed_rows(
            [(me, product("wtd,wtf->df", seasonal_mine, grad_pre))]
            + [((me - s) % head_parts, product("wtd,wtf->df", seasonal_recv[s], grad_pre)) for s in shifts],
            local_width,
            model_width,
        )
        grad_season_part, _ = scattered_product(grad_pre, inner_t, local_width)
        grad_season = grad_comb + grad_season_part
        grad_resid = grad_season - trend_back(grad_season, first_rows)
        grad_attend_mine = grad_resid.astype(jnp.bfloat16)
        grad_attend_recv = {s: swap(grad_attend_mine, s) for s in shifts}
        feed, feed_sent = scattered_product(hidden, outer_low, local_width, after=grad_attend_recv.values())
        combined = seasonal + feed
        output = combined - trend_local(combined, second_rows)
        output_grad_t = placed_rows(
            [(me, product("wtd,wte->de", grad_attend_mine, field))]
            + [((me - s) % head_parts, product("wtd,wte->de", grad_attend_recv[s], field)) for s in shifts],
            local_width,
            model_width,
        )
        grad_field = product("wtd,ed->wte", grad_attend_mine, cols_of(output_low, me, local_width))
        for s in shifts:
            grad_field = grad_field + product(
                "wtd,ed->wte", grad_attend_recv[s], cols_of(output_low, (me - s) % head_parts, local_width)
            )
        grad_field = grad_field.astype(jnp.bfloat16)
        grad_field = grad_field.reshape(windows, length, head_count, head_size)
        grad_mixed = jnp.concatenate(
            [
                product("htm,wthe->whme", inv_cos, grad_field),
                product("htm,wthe->whme", inv_sin, grad_field),
            ],
            axis=-1,
        ).astype(jnp.bfloat16)
        grad_spectrum = product("whmo,hmio->whmi", grad_mixed, block).astype(jnp.bfloat16)
        spectrum_grad_k = jnp.moveaxis(
            grad_spectrum.reshape(windows, head_count, mode_count, 2, head_size), 3, 2
        ).reshape(windows, head_count, 2 * mode_count, head_size)
        query_grad = placed_rows(
            [
                (block_index, product("whkd,whke->dhe", spectra, spectrum_grad_k).reshape(local_width, local_width))
                for block_index, spectra in input_spectra
            ],
            local_width,
            model_width,
        )
        grad_query = product("hmt,whme->wthe", fwd_cos, grad_spectrum[..., :head_size]) + product(
            "hmt,whme->wthe", fwd_sin, grad_spectrum[..., head_size:]
        )
        grad_query = grad_query.reshape(windows, length, local_width).astype(jnp.bfloat16)
        input_part, _ = scattered_product(grad_query, query_t, local_width, after=feed_sent.values())
        input_grad = grad_resid + input_part
        spectrum_parts = spectrum.reshape(windows, head_count, mode_count, 2, head_size)
        grad_real = grad_mixed[..., :head_size]
        grad_imag = grad_mixed[..., head_size:]
        paired = jnp.stack(
            [grad_mixed, jnp.concatenate([grad_imag, -grad_real], axis=-1)], axis=3
        )
        mixer_full = product("whmci,whmco->hmio", spectrum_parts, paired).reshape(
            head_count, mode_count * head_size, 2 * head_size
        )
        return output, input_grad, (query_grad, mixer_full, output_grad_t, inner_grad, outer_grad_t)

    chunks = 1
    span = windows // chunks
    first_all = pool_rows(gates[0], length)
    second_all = pool_rows(gates[1], length)
    results = [
        chunk_pass(
            inputs[c * span : (c + 1) * span],
            out_grad[c * span : (c + 1) * span],
            tuple(part[c * span : (c + 1) * span] for part in first_all),
            tuple(part[c * span : (c + 1) * span] for part in second_all),
        )
        for c in range(chunks)
    ]
    output = jnp.concatenate([r[0] for r in results], axis=0)
    input_grad = jnp.concatenate([r[1] for r in results], axis=0)
    query_grad, mixer_full, output_grad_t, inner_grad, outer_grad_t = [
        sum(r[2][i] for r in results[1:]) + results[0][2][i] if chunks > 1 else results[0][2][i]
        for i in range(5)
    ]

    dp_count = lax.axis_size("dp")
    dp_rank = lax.axis_index("dp")

    lanes = 128

    def lead(grad, axis_number):
        shape = grad.shape
        split = shape[:axis_number] + (dp_count, shape[axis_number] // dp_count) + shape[axis_number + 1 :]
        owned_shape = shape[:axis_number] + (shape[axis_number] // dp_count,) + shape[axis_number + 1 :]
        return jnp.moveaxis(grad.reshape(split), axis_number, 0).reshape(dp_count, -1, lanes), owned_shape

    def reduced_over_dp(grads_axes):
        laid = [lead(grad, axis_number) for grad, axis_number in grads_axes]
        joined = jnp.concatenate([flat for flat, _ in laid], axis=1)
        reduced = lax.psum_scatter(
            joined.reshape(-1, lanes), "dp", scatter_dimension=0, tiled=True
        )
        parts = []
        offset = 0
        for flat, owned_shape in laid:
            rows = flat.shape[1]
            parts.append(reduced[offset : offset + rows].reshape(owned_shape))
            offset += rows
        return parts

    def summed_over_dp(grads_axes):
        laid = [lead(grad, axis_number) for grad, axis_number in grads_axes]
        joined = jnp.concatenate([flat for flat, _ in laid], axis=1)
        rows = joined.shape[1]
        arrived = lax.all_to_all(
            joined.astype(jnp.bfloat16).reshape(-1, lanes), "dp", 0, 0, tiled=True
        )
        reduced = jnp.sum(arrived.astype(jnp.float32).reshape(dp_count, rows, lanes), axis=0)
        parts = []
        offset = 0
        for flat, owned_shape in laid:
            size = flat.shape[1]
            parts.append(reduced[offset : offset + size].reshape(owned_shape))
            offset += size
        return parts

    inner_part, outer_part_t = reduced_over_dp([(inner_grad, 0), (outer_grad_t, 0)])
    mixer_part, output_part_t, query_part = summed_over_dp(
        [(mixer_full, 1), (output_grad_t, 0), (query_grad, 0)]
    )
    output_part = jnp.transpose(output_part_t)
    outer_part = jnp.transpose(outer_part_t)
    token_total = windows * length * dp_count

    def owned(weight, share, axis_number):
        return lax.dynamic_slice_in_dim(weight, dp_rank * share, share, axis_number)

    def stepped(grad, momentum, average, old_weight, spread):
        rate = 0.5 * spread / math.sqrt(token_total)
        new_momentum = momentum_decay * momentum + grad
        new_weight = old_weight - rate * (grad + momentum_decay * new_momentum)
        new_average = average_decay * average + (1 - average_decay) * new_weight
        return (new_momentum, new_weight, new_average)

    query_new = stepped(
        query_part,
        query_momentum,
        query_average,
        owned(query_weight, query_momentum.shape[0], 0),
        D ** (-0.5),
    )
    mixer_new = stepped(
        mixer_part,
        mixer_momentum,
        mixer_average,
        owned(mixer_weight, mixer_momentum.shape[1], 1),
        mixer_spread,
    )
    output_new = stepped(
        output_part,
        output_momentum,
        output_average,
        owned(output_weight, output_momentum.shape[1], 1),
        D ** (-0.5),
    )
    inner_new = stepped(
        inner_part,
        inner_momentum,
        inner_average,
        owned(inner_weight, inner_momentum.shape[0], 0),
        D ** (-0.5),
    )
    outer_new = stepped(
        outer_part,
        outer_momentum,
        outer_average,
        owned(outer_weight, outer_momentum.shape[1], 1),
        FF ** (-0.5),
    )
    return (
        output,
        input_grad,
        query_new[0],
        query_new[1],
        query_new[2],
        mixer_new[0],
        mixer_new[1],
        mixer_new[2],
        output_new[0],
        output_new[1],
        output_new[2],
        inner_new[0],
        inner_new[1],
        inner_new[2],
        outer_new[0],
        outer_new[1],
        outer_new[2],
    )


def solution(mesh):
    return jax.shard_map(
        on_device,
        mesh=mesh,
        in_specs=(
            P("dp", None, "head"),
            P("dp", None, "head"),
            P("head", None),
            P(None, "dp", None),
            P(None, "head"),
            P("head", None, None),
            P("head", None),
            P(None, "head"),
            P("head", None),
            P("dp", "head"),
            P("dp", "head"),
            P("head", "dp", None),
            P("head", "dp", None),
            P("head", "dp"),
            P("head", "dp"),
            P("dp", "head"),
            P("dp", "head"),
            P("head", "dp"),
            P("head", "dp"),
        ),
        out_specs=(
            P("dp", None, "head"),
            P("dp", None, "head"),
            P("dp", "head"),
            P("dp", "head"),
            P("dp", "head"),
            P("head", "dp", None),
            P("head", "dp", None),
            P("head", "dp", None),
            P("head", "dp"),
            P("head", "dp"),
            P("head", "dp"),
            P("dp", "head"),
            P("dp", "head"),
            P("dp", "head"),
            P("head", "dp"),
            P("head", "dp"),
            P("head", "dp"),
        ),
        check_vma=False,
    )
```

```python
import math

import jax
import jax.numpy as jnp
import numpy as np
from jax import lax
from jax.sharding import PartitionSpec as P


D = 512
FF = 2048


pool_sizes = (7, 12, 14, 24, 48)
mixer_spread = 0.07
momentum_decay = 0.9
average_decay = 0.9


def pool_tables(length):
    tables = np.zeros((len(pool_sizes), length, length), np.float32)
    rows_all = np.arange(length)
    for pool_index, pool_width in enumerate(pool_sizes):
        lead_pad = (pool_width - 1) // 2
        for offset in range(pool_width):
            source = np.clip(rows_all - lead_pad + offset, 0, length - 1)
            tables[pool_index][rows_all, source] += np.float32(1.0 / pool_width)
    return jnp.asarray(tables)


def spectral_tables(modes, length):
    positions = jnp.arange(length, dtype=jnp.int32)
    phase = modes[:, :, None] * positions[None, None, :] % length
    angle = phase.astype(jnp.float32) * (2.0 * math.pi / length)
    cosine = jnp.cos(angle)
    sine = jnp.sin(angle)
    doubled = jnp.where((modes == 0) | (2 * modes == length), 1.0, 2.0).astype(jnp.float32) / length
    inv_cos = jnp.transpose(doubled[:, :, None] * cosine, (0, 2, 1))
    inv_sin = jnp.transpose(-doubled[:, :, None] * sine, (0, 2, 1))
    return (cosine, -sine, inv_cos, inv_sin)


def product(form, left, right):
    return jnp.einsum(form, left, right, preferred_element_type=jnp.float32)


def pool_counts(length):
    counts = np.zeros((len(pool_sizes), length, length), np.float32)
    rows_all = np.arange(length)
    for pool_index, pool_width in enumerate(pool_sizes):
        lead_pad = (pool_width - 1) // 2
        for offset in range(pool_width):
            source = np.clip(rows_all - lead_pad + offset, 0, length - 1)
            counts[pool_index][rows_all, source] += 1.0
    return counts


def pool_rows(picks, length):
    counts = pool_counts(length)
    rows = jnp.zeros(picks.shape + (length,), jnp.float32)
    scale = jnp.zeros(picks.shape, jnp.float32)
    for pool_index, pool_width in enumerate(pool_sizes):
        chosen = picks == pool_index
        rows = jnp.where(chosen[..., None], jnp.asarray(counts[pool_index])[None], rows)
        scale = jnp.where(chosen, np.float32(1.0 / pool_width), scale)
    return rows.astype(jnp.bfloat16), scale


def split_three(values):
    high = values.astype(jnp.bfloat16)
    rest = values - high.astype(jnp.float32)
    middle = rest.astype(jnp.bfloat16)
    low = (rest - middle.astype(jnp.float32)).astype(jnp.bfloat16)
    return high, middle, low


def trend_local(values, rows):
    counts, scale = rows
    parts = jnp.concatenate(split_three(values), axis=1)
    tiled = jnp.concatenate([counts] * 3, axis=2)
    summed = jnp.einsum("wts,wsd->wtd", tiled, parts, preferred_element_type=jnp.float32)
    return summed * scale[..., None]


def trend_back(grads, rows):
    counts, scale = rows
    parts = jnp.concatenate(split_three(grads * scale[..., None]), axis=1)
    tiled = jnp.concatenate([counts] * 3, axis=1)
    return jnp.einsum("wts,wtd->wsd", tiled, parts, preferred_element_type=jnp.float32)


def mixer_block(mixer_low, head_size):
    head_count = mixer_low.shape[0]
    shaped = mixer_low.reshape(head_count, -1, head_size, 2 * head_size)
    real_part = shaped[..., :head_size]
    imag_part = shaped[..., head_size:]
    upper = jnp.concatenate([real_part, imag_part], axis=-1)
    lower = jnp.concatenate([-imag_part, real_part], axis=-1)
    return jnp.concatenate([upper, lower], axis=2)


def exact_gelu(values):
    return jax.nn.gelu(values, approximate=False)


def on_device(
    inputs,
    out_grad,
    modes,
    gates,
    query_weight,
    mixer_weight,
    output_weight,
    inner_weight,
    outer_weight,
    query_momentum,
    query_average,
    mixer_momentum,
    mixer_average,
    output_momentum,
    output_average,
    inner_momentum,
    inner_average,
    outer_momentum,
    outer_average,
):
    windows, length, local_width = inputs.shape
    head_count, mode_count = modes.shape
    head_size = local_width // head_count
    head_parts = lax.axis_size("head")
    me = lax.axis_index("head")
    shifts = list(range(1, head_parts))

    def peer(shift):
        return (me + shift) % head_parts

    def swap(values, shift):
        pairs = [(j, (j + shift) % head_parts) for j in range(head_parts)]
        return lax.ppermute(values, "head", pairs)

    def rows_of(weight, block, size):
        return lax.dynamic_slice_in_dim(weight, block * size, size, 0)

    def cols_of(weight, block, size):
        return lax.dynamic_slice_in_dim(weight, block * size, size, 1)

    def gathered_product(mine, weight_low, size):
        received = {s: swap(mine, s) for s in shifts}
        total = product("wtd,de->wte", mine, rows_of(weight_low, me, size))
        for s in shifts:
            owner = (me - s) % head_parts
            total = total + product("wtd,de->wte", received[s], rows_of(weight_low, owner, size))
        return total, received

    def scattered_product(values, weight_low, size, after=()):
        outgoing = {
            s: product("wte,ed->wtd", values, cols_of(weight_low, peer(s), size)).astype(jnp.bfloat16)
            for s in shifts
        }
        if after:
            outgoing, _ = lax.optimization_barrier((outgoing, tuple(after)))
        sent = {s: swap(outgoing[s], s) for s in shifts}
        total = product("wte,ed->wtd", values, cols_of(weight_low, me, size))
        for s in shifts:
            total = total + sent[s].astype(jnp.float32)
        return total, sent

    def placed_rows(parts, size, total_rows):
        out = jnp.zeros((total_rows,) + parts[0][1].shape[1:], jnp.float32)
        for block, part in parts:
            out = lax.dynamic_update_slice_in_dim(out, part, block * size, 0)
        return out

    model_width = local_width * head_parts
    pools = pool_tables(length)
    fwd_cos, fwd_sin, inv_cos, inv_sin = [
        one_table.astype(jnp.bfloat16) for one_table in spectral_tables(modes, length)
    ]
    query_low = query_weight.astype(jnp.bfloat16)
    output_low = output_weight.astype(jnp.bfloat16)
    inner_low = inner_weight.astype(jnp.bfloat16)
    outer_low = outer_weight.astype(jnp.bfloat16)
    inner_t = jnp.transpose(inner_low)
    query_t = jnp.transpose(query_low)
    block = mixer_block(mixer_weight.astype(jnp.bfloat16), head_size)

    def chunk_pass(inputs, out_grad, first_rows, second_rows):
        windows = inputs.shape[0]
        grad_comb = out_grad - trend_back(out_grad, second_rows)
        grad_feed_mine = grad_comb.astype(jnp.bfloat16)

        inputs_mine = inputs.astype(jnp.bfloat16)
        query, inputs_recv = gathered_product(inputs_mine, query_low, local_width)
        grad_feed_recv = {s: swap(grad_feed_mine, s) for s in shifts}
        query = query.astype(jnp.bfloat16)
        query_heads = query.reshape(windows, length, head_count, head_size)
        spectrum = jnp.concatenate(
            [
                product("hmt,wthe->whme", fwd_cos, query_heads),
                product("hmt,wthe->whme", fwd_sin, query_heads),
            ],
            axis=-1,
        ).astype(jnp.bfloat16)
        mixed = product("whmi,hmio->whmo", spectrum, block).astype(jnp.bfloat16)
        field = product("htm,whme->wthe", inv_cos, mixed[..., :head_size]) + product(
            "htm,whme->wthe", inv_sin, mixed[..., head_size:]
        )
        field = field.reshape(windows, length, local_width).astype(jnp.bfloat16)
        attended, _ = scattered_product(field, output_low, local_width)
        resid_one = inputs + attended
        seasonal = resid_one - trend_local(resid_one, first_rows)
        seasonal_mine = seasonal.astype(jnp.bfloat16)
        pre, seasonal_recv = gathered_product(seasonal_mine, inner_low, local_width)
        activated, gelu_pull = jax.vjp(exact_gelu, pre)
        hidden = activated.astype(jnp.bfloat16)

        outer_grad_t = placed_rows(
            [(me, product("wtd,wtf->df", grad_feed_mine, hidden))]
            + [((me - s) % head_parts, product("wtd,wtf->df", grad_feed_recv[s], hidden)) for s in shifts],
            local_width,
            model_width,
        )
        grad_hidden = product("wtd,fd->wtf", grad_feed_mine, cols_of(outer_low, me, local_width))
        for s in shifts:
            grad_hidden = grad_hidden + product(
                "wtd,fd->wtf", grad_feed_recv[s], cols_of(outer_low, (me - s) % head_parts, local_width)
            )
        grad_pre = gelu_pull(grad_hidden)[0].astype(jnp.bfloat16)
        inner_grad = placed_rows(
            [(me, product("wtd,wtf->df", seasonal_mine, grad_pre))]
            + [((me - s) % head_parts, product("wtd,wtf->df", seasonal_recv[s], grad_pre)) for s in shifts],
            local_width,
            model_width,
        )
        grad_season_part, _ = scattered_product(grad_pre, inner_t, local_width)
        grad_season = grad_comb + grad_season_part
        grad_resid = grad_season - trend_back(grad_season, first_rows)
        grad_attend_mine = grad_resid.astype(jnp.bfloat16)
        grad_attend_recv = {s: swap(grad_attend_mine, s) for s in shifts}
        feed, feed_sent = scattered_product(hidden, outer_low, local_width, after=grad_attend_recv.values())
        combined = seasonal + feed
        output = combined - trend_local(combined, second_rows)
        output_grad_t = placed_rows(
            [(me, product("wtd,wte->de", grad_attend_mine, field))]
            + [((me - s) % head_parts, product("wtd,wte->de", grad_attend_recv[s], field)) for s in shifts],
            local_width,
            model_width,
        )
        grad_field = product("wtd,ed->wte", grad_attend_mine, cols_of(output_low, me, local_width))
        for s in shifts:
            grad_field = grad_field + product(
                "wtd,ed->wte", grad_attend_recv[s], cols_of(output_low, (me - s) % head_parts, local_width)
            )
        grad_field = grad_field.astype(jnp.bfloat16)
        grad_field = grad_field.reshape(windows, length, head_count, head_size)
        grad_mixed = jnp.concatenate(
            [
                product("htm,wthe->whme", inv_cos, grad_field),
                product("htm,wthe->whme", inv_sin, grad_field),
            ],
            axis=-1,
        ).astype(jnp.bfloat16)
        grad_spectrum = product("whmo,hmio->whmi", grad_mixed, block).astype(jnp.bfloat16)
        grad_query = product("hmt,whme->wthe", fwd_cos, grad_spectrum[..., :head_size]) + product(
            "hmt,whme->wthe", fwd_sin, grad_spectrum[..., head_size:]
        )
        grad_query = grad_query.reshape(windows, length, local_width).astype(jnp.bfloat16)
        query_grad = placed_rows(
            [(me, product("wtd,wte->de", inputs_mine, grad_query))]
            + [((me - s) % head_parts, product("wtd,wte->de", inputs_recv[s], grad_query)) for s in shifts],
            local_width,
            model_width,
        )
        input_part, _ = scattered_product(grad_query, query_t, local_width, after=feed_sent.values())
        input_grad = grad_resid + input_part
        spectrum_parts = spectrum.reshape(windows, head_count, mode_count, 2, head_size)
        grad_real = grad_mixed[..., :head_size]
        grad_imag = grad_mixed[..., head_size:]
        paired = jnp.stack(
            [grad_mixed, jnp.concatenate([grad_imag, -grad_real], axis=-1)], axis=3
        )
        mixer_full = product("whmci,whmco->hmio", spectrum_parts, paired).reshape(
            head_count, mode_count * head_size, 2 * head_size
        )
        return output, input_grad, (query_grad, mixer_full, output_grad_t, inner_grad, outer_grad_t)

    chunks = 1
    span = windows // chunks
    first_all = pool_rows(gates[0], length)
    second_all = pool_rows(gates[1], length)
    results = [
        chunk_pass(
            inputs[c * span : (c + 1) * span],
            out_grad[c * span : (c + 1) * span],
            tuple(part[c * span : (c + 1) * span] for part in first_all),
            tuple(part[c * span : (c + 1) * span] for part in second_all),
        )
        for c in range(chunks)
    ]
    output = jnp.concatenate([r[0] for r in results], axis=0)
    input_grad = jnp.concatenate([r[1] for r in results], axis=0)
    query_grad, mixer_full, output_grad_t, inner_grad, outer_grad_t = [
        sum(r[2][i] for r in results[1:]) + results[0][2][i] if chunks > 1 else results[0][2][i]
        for i in range(5)
    ]

    dp_count = lax.axis_size("dp")
    dp_rank = lax.axis_index("dp")

    lanes = 128

    def lead(grad, axis_number):
        shape = grad.shape
        split = shape[:axis_number] + (dp_count, shape[axis_number] // dp_count) + shape[axis_number + 1 :]
        owned_shape = shape[:axis_number] + (shape[axis_number] // dp_count,) + shape[axis_number + 1 :]
        return jnp.moveaxis(grad.reshape(split), axis_number, 0).reshape(dp_count, -1, lanes), owned_shape

    def reduced_over_dp(grads_axes):
        laid = [lead(grad, axis_number) for grad, axis_number in grads_axes]
        joined = jnp.concatenate([flat for flat, _ in laid], axis=1)
        reduced = lax.psum_scatter(
            joined.reshape(-1, lanes), "dp", scatter_dimension=0, tiled=True
        )
        parts = []
        offset = 0
        for flat, owned_shape in laid:
            rows = flat.shape[1]
            parts.append(reduced[offset : offset + rows].reshape(owned_shape))
            offset += rows
        return parts

    def summed_over_dp(grads_axes):
        laid = [lead(grad, axis_number) for grad, axis_number in grads_axes]
        joined = jnp.concatenate([flat for flat, _ in laid], axis=1)
        rows = joined.shape[1]
        arrived = lax.all_to_all(
            joined.astype(jnp.bfloat16).reshape(-1, lanes), "dp", 0, 0, tiled=True
        )
        reduced = jnp.sum(arrived.astype(jnp.float32).reshape(dp_count, rows, lanes), axis=0)
        parts = []
        offset = 0
        for flat, owned_shape in laid:
            size = flat.shape[1]
            parts.append(reduced[offset : offset + size].reshape(owned_shape))
            offset += size
        return parts

    inner_part, outer_part_t = reduced_over_dp([(inner_grad, 0), (outer_grad_t, 0)])
    mixer_part, output_part_t = summed_over_dp([(mixer_full, 1), (output_grad_t, 0)])
    (query_part,) = summed_over_dp([(query_grad, 0)])
    output_part = jnp.transpose(output_part_t)
    outer_part = jnp.transpose(outer_part_t)
    token_total = windows * length * dp_count

    def owned(weight, share, axis_number):
        return lax.dynamic_slice_in_dim(weight, dp_rank * share, share, axis_number)

    def stepped(grad, momentum, average, old_weight, spread):
        rate = 0.5 * spread / math.sqrt(token_total)
        new_momentum = momentum_decay * momentum + grad
        new_weight = old_weight - rate * (grad + momentum_decay * new_momentum)
        new_average = average_decay * average + (1 - average_decay) * new_weight
        return (new_momentum, new_weight, new_average)

    query_new = stepped(
        query_part,
        query_momentum,
        query_average,
        owned(query_weight, query_momentum.shape[0], 0),
        D ** (-0.5),
    )
    mixer_new = stepped(
        mixer_part,
        mixer_momentum,
        mixer_average,
        owned(mixer_weight, mixer_momentum.shape[1], 1),
        mixer_spread,
    )
    output_new = stepped(
        output_part,
        output_momentum,
        output_average,
        owned(output_weight, output_momentum.shape[1], 1),
        D ** (-0.5),
    )
    inner_new = stepped(
        inner_part,
        inner_momentum,
        inner_average,
        owned(inner_weight, inner_momentum.shape[0], 0),
        D ** (-0.5),
    )
    outer_new = stepped(
        outer_part,
        outer_momentum,
        outer_average,
        owned(outer_weight, outer_momentum.shape[1], 1),
        FF ** (-0.5),
    )
    return (
        output,
        input_grad,
        query_new[0],
        query_new[1],
        query_new[2],
        mixer_new[0],
        mixer_new[1],
        mixer_new[2],
        output_new[0],
        output_new[1],
        output_new[2],
        inner_new[0],
        inner_new[1],
        inner_new[2],
        outer_new[0],
        outer_new[1],
        outer_new[2],
    )


def solution(mesh):
    return jax.shard_map(
        on_device,
        mesh=mesh,
        in_specs=(
            P("dp", None, "head"),
            P("dp", None, "head"),
            P("head", None),
            P(None, "dp", None),
            P(None, "head"),
            P("head", None, None),
            P("head", None),
            P(None, "head"),
            P("head", None),
            P("dp", "head"),
            P("dp", "head"),
            P("head", "dp", None),
            P("head", "dp", None),
            P("head", "dp"),
            P("head", "dp"),
            P("dp", "head"),
            P("dp", "head"),
            P("head", "dp"),
            P("head", "dp"),
        ),
        out_specs=(
            P("dp", None, "head"),
            P("dp", None, "head"),
            P("dp", "head"),
            P("dp", "head"),
            P("dp", "head"),
            P("head", "dp", None),
            P("head", "dp", None),
            P("head", "dp", None),
            P("head", "dp"),
            P("head", "dp"),
            P("head", "dp"),
            P("dp", "head"),
            P("dp", "head"),
            P("dp", "head"),
            P("head", "dp"),
            P("head", "dp"),
            P("head", "dp"),
        ),
        check_vma=False,
    )
```

```python
import math

import jax
import jax.numpy as jnp
import numpy as np
from jax import lax
from jax.sharding import PartitionSpec as P


D = 512
FF = 2048


pool_sizes = (7, 12, 14, 24, 48)
mixer_spread = 0.07
momentum_decay = 0.9
average_decay = 0.9


def pool_tables(length):
    tables = np.zeros((len(pool_sizes), length, length), np.float32)
    rows_all = np.arange(length)
    for pool_index, pool_width in enumerate(pool_sizes):
        lead_pad = (pool_width - 1) // 2
        for offset in range(pool_width):
            source = np.clip(rows_all - lead_pad + offset, 0, length - 1)
            tables[pool_index][rows_all, source] += np.float32(1.0 / pool_width)
    return jnp.asarray(tables)


def spectral_tables(modes, length):
    positions = jnp.arange(length, dtype=jnp.int32)
    phase = modes[:, :, None] * positions[None, None, :] % length
    angle = phase.astype(jnp.float32) * (2.0 * math.pi / length)
    cosine = jnp.cos(angle)
    sine = jnp.sin(angle)
    doubled = jnp.where((modes == 0) | (2 * modes == length), 1.0, 2.0).astype(jnp.float32) / length
    inv_cos = jnp.transpose(doubled[:, :, None] * cosine, (0, 2, 1))
    inv_sin = jnp.transpose(-doubled[:, :, None] * sine, (0, 2, 1))
    return (cosine, -sine, inv_cos, inv_sin)


def product(form, left, right):
    return jnp.einsum(form, left, right, preferred_element_type=jnp.float32)


def pool_counts(length):
    counts = np.zeros((len(pool_sizes), length, length), np.float32)
    rows_all = np.arange(length)
    for pool_index, pool_width in enumerate(pool_sizes):
        lead_pad = (pool_width - 1) // 2
        for offset in range(pool_width):
            source = np.clip(rows_all - lead_pad + offset, 0, length - 1)
            counts[pool_index][rows_all, source] += 1.0
    return counts


def pool_rows(picks, length):
    counts = pool_counts(length)
    rows = jnp.zeros(picks.shape + (length,), jnp.float32)
    scale = jnp.zeros(picks.shape, jnp.float32)
    for pool_index, pool_width in enumerate(pool_sizes):
        chosen = picks == pool_index
        rows = jnp.where(chosen[..., None], jnp.asarray(counts[pool_index])[None], rows)
        scale = jnp.where(chosen, np.float32(1.0 / pool_width), scale)
    return rows.astype(jnp.bfloat16), scale


def split_three(values):
    high = values.astype(jnp.bfloat16)
    rest = values - high.astype(jnp.float32)
    middle = rest.astype(jnp.bfloat16)
    low = (rest - middle.astype(jnp.float32)).astype(jnp.bfloat16)
    return high, middle, low


def trend_local(values, rows):
    counts, scale = rows
    parts = jnp.concatenate(split_three(values), axis=1)
    tiled = jnp.concatenate([counts] * 3, axis=2)
    summed = jnp.einsum("wts,wsd->wtd", tiled, parts, preferred_element_type=jnp.float32)
    return summed * scale[..., None]


def trend_back(grads, rows):
    counts, scale = rows
    parts = jnp.concatenate(split_three(grads * scale[..., None]), axis=1)
    tiled = jnp.concatenate([counts] * 3, axis=1)
    return jnp.einsum("wts,wtd->wsd", tiled, parts, preferred_element_type=jnp.float32)


def mixer_block(mixer_low, head_size):
    head_count = mixer_low.shape[0]
    shaped = mixer_low.reshape(head_count, -1, head_size, 2 * head_size)
    real_part = shaped[..., :head_size]
    imag_part = shaped[..., head_size:]
    upper = jnp.concatenate([real_part, imag_part], axis=-1)
    lower = jnp.concatenate([-imag_part, real_part], axis=-1)
    return jnp.concatenate([upper, lower], axis=2)


def exact_gelu(values):
    return jax.nn.gelu(values, approximate=False)


def on_device(
    inputs,
    out_grad,
    modes,
    gates,
    query_weight,
    mixer_weight,
    output_weight,
    inner_weight,
    outer_weight,
    query_momentum,
    query_average,
    mixer_momentum,
    mixer_average,
    output_momentum,
    output_average,
    inner_momentum,
    inner_average,
    outer_momentum,
    outer_average,
):
    windows, length, local_width = inputs.shape
    head_count, mode_count = modes.shape
    head_size = local_width // head_count
    head_parts = lax.axis_size("head")
    me = lax.axis_index("head")
    shifts = list(range(1, head_parts))

    def peer(shift):
        return (me + shift) % head_parts

    def swap(values, shift):
        pairs = [(j, (j + shift) % head_parts) for j in range(head_parts)]
        return lax.ppermute(values, "head", pairs)

    def rows_of(weight, block, size):
        return lax.dynamic_slice_in_dim(weight, block * size, size, 0)

    def cols_of(weight, block, size):
        return lax.dynamic_slice_in_dim(weight, block * size, size, 1)

    def gathered_product(mine, weight_low, size):
        received = {s: swap(mine, s) for s in shifts}
        total = product("wtd,de->wte", mine, rows_of(weight_low, me, size))
        for s in shifts:
            owner = (me - s) % head_parts
            total = total + product("wtd,de->wte", received[s], rows_of(weight_low, owner, size))
        return total, received

    def scattered_product(values, weight_low, size, after=()):
        outgoing = {
            s: product("wte,ed->wtd", values, cols_of(weight_low, peer(s), size)).astype(jnp.bfloat16)
            for s in shifts
        }
        if after:
            outgoing, _ = lax.optimization_barrier((outgoing, tuple(after)))
        sent = {s: swap(outgoing[s], s) for s in shifts}
        total = product("wte,ed->wtd", values, cols_of(weight_low, me, size))
        for s in shifts:
            total = total + sent[s].astype(jnp.float32)
        return total, sent

    def placed_rows(parts, size, total_rows):
        out = jnp.zeros((total_rows,) + parts[0][1].shape[1:], jnp.float32)
        for block, part in parts:
            out = lax.dynamic_update_slice_in_dim(out, part, block * size, 0)
        return out

    model_width = local_width * head_parts
    pools = pool_tables(length)
    fwd_cos, fwd_sin, inv_cos, inv_sin = [
        one_table.astype(jnp.bfloat16) for one_table in spectral_tables(modes, length)
    ]
    query_low = query_weight.astype(jnp.bfloat16)
    output_low = output_weight.astype(jnp.bfloat16)
    inner_low = inner_weight.astype(jnp.bfloat16)
    outer_low = outer_weight.astype(jnp.bfloat16)
    inner_t = jnp.transpose(inner_low)
    query_t = jnp.transpose(query_low)
    block = mixer_block(mixer_weight.astype(jnp.bfloat16), head_size)
    fwd_pairs = jnp.stack([fwd_cos, fwd_sin], axis=2).reshape(head_count, 2 * mode_count, length)
    inv_pairs = jnp.stack([inv_cos, inv_sin], axis=3).reshape(head_count, length, 2 * mode_count)

    def chunk_pass(inputs, out_grad, first_rows, second_rows):
        windows = inputs.shape[0]
        grad_comb = out_grad - trend_back(out_grad, second_rows)
        grad_feed_mine = grad_comb.astype(jnp.bfloat16)

        inputs_mine = inputs.astype(jnp.bfloat16)
        query, inputs_recv = gathered_product(inputs_mine, query_low, local_width)
        grad_feed_recv = {s: swap(grad_feed_mine, s) for s in shifts}
        query = query.astype(jnp.bfloat16)
        query_heads = query.reshape(windows, length, head_count, head_size)
        spectrum = product("hkt,wthe->whke", fwd_pairs, query_heads).astype(jnp.bfloat16)
        spectrum = spectrum.reshape(windows, head_count, mode_count, 2 * head_size)
        mixed = product("whmi,hmio->whmo", spectrum, block).astype(jnp.bfloat16)
        field = product(
            "htk,whke->wthe", inv_pairs, mixed.reshape(windows, head_count, 2 * mode_count, head_size)
        )
        field = field.reshape(windows, length, local_width).astype(jnp.bfloat16)
        attended, _ = scattered_product(field, output_low, local_width)
        resid_one = inputs + attended
        seasonal = resid_one - trend_local(resid_one, first_rows)
        seasonal_mine = seasonal.astype(jnp.bfloat16)
        pre, seasonal_recv = gathered_product(seasonal_mine, inner_low, local_width)
        activated, gelu_pull = jax.vjp(exact_gelu, pre)
        hidden = activated.astype(jnp.bfloat16)

        outer_grad_t = placed_rows(
            [(me, product("wtd,wtf->df", grad_feed_mine, hidden))]
            + [((me - s) % head_parts, product("wtd,wtf->df", grad_feed_recv[s], hidden)) for s in shifts],
            local_width,
            model_width,
        )
        grad_hidden = product("wtd,fd->wtf", grad_feed_mine, cols_of(outer_low, me, local_width))
        for s in shifts:
            grad_hidden = grad_hidden + product(
                "wtd,fd->wtf", grad_feed_recv[s], cols_of(outer_low, (me - s) % head_parts, local_width)
            )
        grad_pre = gelu_pull(grad_hidden)[0].astype(jnp.bfloat16)
        inner_grad = placed_rows(
            [(me, product("wtd,wtf->df", seasonal_mine, grad_pre))]
            + [((me - s) % head_parts, product("wtd,wtf->df", seasonal_recv[s], grad_pre)) for s in shifts],
            local_width,
            model_width,
        )
        grad_season_part, _ = scattered_product(grad_pre, inner_t, local_width)
        grad_season = grad_comb + grad_season_part
        grad_resid = grad_season - trend_back(grad_season, first_rows)
        grad_attend_mine = grad_resid.astype(jnp.bfloat16)
        grad_attend_recv = {s: swap(grad_attend_mine, s) for s in shifts}
        feed, feed_sent = scattered_product(hidden, outer_low, local_width, after=grad_attend_recv.values())
        combined = seasonal + feed
        output = combined - trend_local(combined, second_rows)
        output_grad_t = placed_rows(
            [(me, product("wtd,wte->de", grad_attend_mine, field))]
            + [((me - s) % head_parts, product("wtd,wte->de", grad_attend_recv[s], field)) for s in shifts],
            local_width,
            model_width,
        )
        grad_field = product("wtd,ed->wte", grad_attend_mine, cols_of(output_low, me, local_width))
        for s in shifts:
            grad_field = grad_field + product(
                "wtd,ed->wte", grad_attend_recv[s], cols_of(output_low, (me - s) % head_parts, local_width)
            )
        grad_field = grad_field.astype(jnp.bfloat16)
        grad_field = grad_field.reshape(windows, length, head_count, head_size)
        grad_mixed = product("htk,wthe->whke", inv_pairs, grad_field).astype(jnp.bfloat16)
        grad_mixed = grad_mixed.reshape(windows, head_count, mode_count, 2 * head_size)
        grad_spectrum = product("whmo,hmio->whmi", grad_mixed, block).astype(jnp.bfloat16)
        grad_query = product(
            "hkt,whke->wthe",
            fwd_pairs,
            grad_spectrum.reshape(windows, head_count, 2 * mode_count, head_size),
        )
        grad_query = grad_query.reshape(windows, length, local_width).astype(jnp.bfloat16)
        query_grad = placed_rows(
            [(me, product("wtd,wte->de", inputs_mine, grad_query))]
            + [((me - s) % head_parts, product("wtd,wte->de", inputs_recv[s], grad_query)) for s in shifts],
            local_width,
            model_width,
        )
        input_part, _ = scattered_product(grad_query, query_t, local_width, after=feed_sent.values())
        input_grad = grad_resid + input_part
        spectrum_parts = spectrum.reshape(windows, head_count, mode_count, 2, head_size)
        grad_real = grad_mixed[..., :head_size]
        grad_imag = grad_mixed[..., head_size:]
        paired = jnp.stack(
            [grad_mixed, jnp.concatenate([grad_imag, -grad_real], axis=-1)], axis=3
        )
        mixer_full = product("whmci,whmco->hmio", spectrum_parts, paired).reshape(
            head_count, mode_count * head_size, 2 * head_size
        )
        return output, input_grad, (query_grad, mixer_full, output_grad_t, inner_grad, outer_grad_t)

    chunks = 1
    span = windows // chunks
    first_all = pool_rows(gates[0], length)
    second_all = pool_rows(gates[1], length)
    results = [
        chunk_pass(
            inputs[c * span : (c + 1) * span],
            out_grad[c * span : (c + 1) * span],
            tuple(part[c * span : (c + 1) * span] for part in first_all),
            tuple(part[c * span : (c + 1) * span] for part in second_all),
        )
        for c in range(chunks)
    ]
    output = jnp.concatenate([r[0] for r in results], axis=0)
    input_grad = jnp.concatenate([r[1] for r in results], axis=0)
    query_grad, mixer_full, output_grad_t, inner_grad, outer_grad_t = [
        sum(r[2][i] for r in results[1:]) + results[0][2][i] if chunks > 1 else results[0][2][i]
        for i in range(5)
    ]

    dp_count = lax.axis_size("dp")
    dp_rank = lax.axis_index("dp")

    lanes = 128

    def lead(grad, axis_number):
        shape = grad.shape
        split = shape[:axis_number] + (dp_count, shape[axis_number] // dp_count) + shape[axis_number + 1 :]
        owned_shape = shape[:axis_number] + (shape[axis_number] // dp_count,) + shape[axis_number + 1 :]
        return jnp.moveaxis(grad.reshape(split), axis_number, 0).reshape(dp_count, -1, lanes), owned_shape

    def summed_over_dp(grads_axes):
        laid = [lead(grad, axis_number) for grad, axis_number in grads_axes]
        joined = jnp.concatenate([flat for flat, _ in laid], axis=1)
        rows = joined.shape[1]
        arrived = lax.all_to_all(
            joined.astype(jnp.bfloat16).reshape(-1, lanes), "dp", 0, 0, tiled=True
        )
        reduced = jnp.sum(arrived.astype(jnp.float32).reshape(dp_count, rows, lanes), axis=0)
        parts = []
        offset = 0
        for flat, owned_shape in laid:
            size = flat.shape[1]
            parts.append(reduced[offset : offset + size].reshape(owned_shape))
            offset += size
        return parts

    inner_part, outer_part_t = summed_over_dp([(inner_grad, 0), (outer_grad_t, 0)])
    mixer_part, output_part_t = summed_over_dp([(mixer_full, 1), (output_grad_t, 0)])
    (query_part,) = summed_over_dp([(query_grad, 0)])
    output_part = jnp.transpose(output_part_t)
    outer_part = jnp.transpose(outer_part_t)
    token_total = windows * length * dp_count

    def owned(weight, share, axis_number):
        return lax.dynamic_slice_in_dim(weight, dp_rank * share, share, axis_number)

    def stepped(grad, momentum, average, old_weight, spread):
        rate = 0.5 * spread / math.sqrt(token_total)
        new_momentum = momentum_decay * momentum + grad
        new_weight = old_weight - rate * (grad + momentum_decay * new_momentum)
        new_average = average_decay * average + (1 - average_decay) * new_weight
        return (new_momentum, new_weight, new_average)

    query_new = stepped(
        query_part,
        query_momentum,
        query_average,
        owned(query_weight, query_momentum.shape[0], 0),
        D ** (-0.5),
    )
    mixer_new = stepped(
        mixer_part,
        mixer_momentum,
        mixer_average,
        owned(mixer_weight, mixer_momentum.shape[1], 1),
        mixer_spread,
    )
    output_new = stepped(
        output_part,
        output_momentum,
        output_average,
        owned(output_weight, output_momentum.shape[1], 1),
        D ** (-0.5),
    )
    inner_new = stepped(
        inner_part,
        inner_momentum,
        inner_average,
        owned(inner_weight, inner_momentum.shape[0], 0),
        D ** (-0.5),
    )
    outer_new = stepped(
        outer_part,
        outer_momentum,
        outer_average,
        owned(outer_weight, outer_momentum.shape[1], 1),
        FF ** (-0.5),
    )
    return (
        output,
        input_grad,
        query_new[0],
        query_new[1],
        query_new[2],
        mixer_new[0],
        mixer_new[1],
        mixer_new[2],
        output_new[0],
        output_new[1],
        output_new[2],
        inner_new[0],
        inner_new[1],
        inner_new[2],
        outer_new[0],
        outer_new[1],
        outer_new[2],
    )


def solution(mesh):
    return jax.shard_map(
        on_device,
        mesh=mesh,
        in_specs=(
            P("dp", None, "head"),
            P("dp", None, "head"),
            P("head", None),
            P(None, "dp", None),
            P(None, "head"),
            P("head", None, None),
            P("head", None),
            P(None, "head"),
            P("head", None),
            P("dp", "head"),
            P("dp", "head"),
            P("head", "dp", None),
            P("head", "dp", None),
            P("head", "dp"),
            P("head", "dp"),
            P("dp", "head"),
            P("dp", "head"),
            P("head", "dp"),
            P("head", "dp"),
        ),
        out_specs=(
            P("dp", None, "head"),
            P("dp", None, "head"),
            P("dp", "head"),
            P("dp", "head"),
            P("dp", "head"),
            P("head", "dp", None),
            P("head", "dp", None),
            P("head", "dp", None),
            P("head", "dp"),
            P("head", "dp"),
            P("head", "dp"),
            P("dp", "head"),
            P("dp", "head"),
            P("dp", "head"),
            P("head", "dp"),
            P("head", "dp"),
            P("head", "dp"),
        ),
        check_vma=False,
    )
```

```python
import math

import jax
import jax.numpy as jnp
import numpy as np
from jax import lax
from jax.sharding import PartitionSpec as P


D = 512
FF = 2048


pool_sizes = (7, 12, 14, 24, 48)
mixer_spread = 0.07
momentum_decay = 0.9
average_decay = 0.9


def pool_tables(length):
    tables = np.zeros((len(pool_sizes), length, length), np.float32)
    rows_all = np.arange(length)
    for pool_index, pool_width in enumerate(pool_sizes):
        lead_pad = (pool_width - 1) // 2
        for offset in range(pool_width):
            source = np.clip(rows_all - lead_pad + offset, 0, length - 1)
            tables[pool_index][rows_all, source] += np.float32(1.0 / pool_width)
    return jnp.asarray(tables)


def spectral_tables(modes, length):
    positions = jnp.arange(length, dtype=jnp.int32)
    phase = modes[:, :, None] * positions[None, None, :] % length
    angle = phase.astype(jnp.float32) * (2.0 * math.pi / length)
    cosine = jnp.cos(angle)
    sine = jnp.sin(angle)
    doubled = jnp.where((modes == 0) | (2 * modes == length), 1.0, 2.0).astype(jnp.float32) / length
    inv_cos = jnp.transpose(doubled[:, :, None] * cosine, (0, 2, 1))
    inv_sin = jnp.transpose(-doubled[:, :, None] * sine, (0, 2, 1))
    return (cosine, -sine, inv_cos, inv_sin)


def product(form, left, right):
    return jnp.einsum(form, left, right, preferred_element_type=jnp.float32)


def pool_counts(length):
    counts = np.zeros((len(pool_sizes), length, length), np.float32)
    rows_all = np.arange(length)
    for pool_index, pool_width in enumerate(pool_sizes):
        lead_pad = (pool_width - 1) // 2
        for offset in range(pool_width):
            source = np.clip(rows_all - lead_pad + offset, 0, length - 1)
            counts[pool_index][rows_all, source] += 1.0
    return counts


def pool_rows(picks, length):
    counts = pool_counts(length)
    rows = jnp.zeros(picks.shape + (length,), jnp.float32)
    scale = jnp.zeros(picks.shape, jnp.float32)
    for pool_index, pool_width in enumerate(pool_sizes):
        chosen = picks == pool_index
        rows = jnp.where(chosen[..., None], jnp.asarray(counts[pool_index])[None], rows)
        scale = jnp.where(chosen, np.float32(1.0 / pool_width), scale)
    return rows.astype(jnp.bfloat16), scale


def split_three(values):
    high = values.astype(jnp.bfloat16)
    rest = values - high.astype(jnp.float32)
    middle = rest.astype(jnp.bfloat16)
    low = (rest - middle.astype(jnp.float32)).astype(jnp.bfloat16)
    return high, middle, low


def trend_local(values, rows):
    counts, scale = rows
    parts = jnp.concatenate(split_three(values), axis=1)
    tiled = jnp.concatenate([counts] * 3, axis=2)
    summed = jnp.einsum("wts,wsd->wtd", tiled, parts, preferred_element_type=jnp.float32)
    return summed * scale[..., None]


def trend_back(grads, rows):
    counts, scale = rows
    parts = jnp.concatenate(split_three(grads * scale[..., None]), axis=1)
    tiled = jnp.concatenate([counts] * 3, axis=1)
    return jnp.einsum("wts,wtd->wsd", tiled, parts, preferred_element_type=jnp.float32)


def mixer_block(mixer_low, head_size):
    head_count = mixer_low.shape[0]
    shaped = mixer_low.reshape(head_count, -1, head_size, 2 * head_size)
    real_part = shaped[..., :head_size]
    imag_part = shaped[..., head_size:]
    upper = jnp.concatenate([real_part, imag_part], axis=-1)
    lower = jnp.concatenate([-imag_part, real_part], axis=-1)
    return jnp.concatenate([upper, lower], axis=2)


def exact_gelu(values):
    return jax.nn.gelu(values, approximate=False)


def on_device(
    inputs,
    out_grad,
    modes,
    gates,
    query_weight,
    mixer_weight,
    output_weight,
    inner_weight,
    outer_weight,
    query_momentum,
    query_average,
    mixer_momentum,
    mixer_average,
    output_momentum,
    output_average,
    inner_momentum,
    inner_average,
    outer_momentum,
    outer_average,
):
    windows, length, local_width = inputs.shape
    head_count, mode_count = modes.shape
    head_size = local_width // head_count
    head_parts = lax.axis_size("head")
    me = lax.axis_index("head")
    shifts = list(range(1, head_parts))

    def peer(shift):
        return (me + shift) % head_parts

    def swap(values, shift):
        pairs = [(j, (j + shift) % head_parts) for j in range(head_parts)]
        return lax.ppermute(values, "head", pairs)

    def rows_of(weight, block, size):
        return lax.dynamic_slice_in_dim(weight, block * size, size, 0)

    def cols_of(weight, block, size):
        return lax.dynamic_slice_in_dim(weight, block * size, size, 1)

    def gathered_product(mine, weight_low, size):
        received = {s: swap(mine, s) for s in shifts}
        total = product("wtd,de->wte", mine, rows_of(weight_low, me, size))
        for s in shifts:
            owner = (me - s) % head_parts
            total = total + product("wtd,de->wte", received[s], rows_of(weight_low, owner, size))
        return total, received

    def scattered_product(values, weight_low, size, after=()):
        outgoing = {
            s: product("wte,ed->wtd", values, cols_of(weight_low, peer(s), size)).astype(jnp.bfloat16)
            for s in shifts
        }
        if after:
            outgoing, _ = lax.optimization_barrier((outgoing, tuple(after)))
        sent = {s: swap(outgoing[s], s) for s in shifts}
        total = product("wte,ed->wtd", values, cols_of(weight_low, me, size))
        for s in shifts:
            total = total + sent[s].astype(jnp.float32)
        return total, sent

    def placed_rows(parts, size, total_rows):
        out = jnp.zeros((total_rows,) + parts[0][1].shape[1:], jnp.float32)
        for block, part in parts:
            out = lax.dynamic_update_slice_in_dim(out, part, block * size, 0)
        return out

    model_width = local_width * head_parts
    pools = pool_tables(length)
    fwd_cos, fwd_sin, inv_cos, inv_sin = [
        one_table.astype(jnp.bfloat16) for one_table in spectral_tables(modes, length)
    ]
    query_low = query_weight.astype(jnp.bfloat16)
    output_low = output_weight.astype(jnp.bfloat16)
    inner_low = inner_weight.astype(jnp.bfloat16)
    outer_low = outer_weight.astype(jnp.bfloat16)
    inner_t = jnp.transpose(inner_low)
    query_t = jnp.transpose(query_low)
    block = mixer_block(mixer_weight.astype(jnp.bfloat16), head_size)

    def chunk_pass(inputs, out_grad, first_rows, second_rows):
        windows = inputs.shape[0]
        grad_comb = out_grad - trend_back(out_grad, second_rows)
        grad_feed_mine = grad_comb.astype(jnp.bfloat16)

        inputs_mine = inputs.astype(jnp.bfloat16)
        query, inputs_recv = gathered_product(inputs_mine, query_low, local_width)
        grad_feed_recv = {s: swap(grad_feed_mine, s) for s in shifts}
        query = query.astype(jnp.bfloat16)
        query_heads = query.reshape(windows, length, head_count, head_size)
        spectrum = jnp.concatenate(
            [
                product("hmt,wthe->whme", fwd_cos, query_heads),
                product("hmt,wthe->whme", fwd_sin, query_heads),
            ],
            axis=-1,
        ).astype(jnp.bfloat16)
        mixed = product("whmi,hmio->whmo", spectrum, block).astype(jnp.bfloat16)
        field = product("htm,whme->wthe", inv_cos, mixed[..., :head_size]) + product(
            "htm,whme->wthe", inv_sin, mixed[..., head_size:]
        )
        field = field.reshape(windows, length, local_width).astype(jnp.bfloat16)
        attended, _ = scattered_product(field, output_low, local_width)
        resid_one = inputs + attended
        seasonal = resid_one - trend_local(resid_one, first_rows)
        seasonal_mine = seasonal.astype(jnp.bfloat16)
        pre, seasonal_recv = gathered_product(seasonal_mine, inner_low, local_width)
        activated, gelu_pull = jax.vjp(exact_gelu, pre)
        hidden = activated.astype(jnp.bfloat16)

        outer_grad_t = placed_rows(
            [(me, product("wtd,wtf->df", grad_feed_mine, hidden))]
            + [((me - s) % head_parts, product("wtd,wtf->df", grad_feed_recv[s], hidden)) for s in shifts],
            local_width,
            model_width,
        )
        grad_hidden = product("wtd,fd->wtf", grad_feed_mine, cols_of(outer_low, me, local_width))
        for s in shifts:
            grad_hidden = grad_hidden + product(
                "wtd,fd->wtf", grad_feed_recv[s], cols_of(outer_low, (me - s) % head_parts, local_width)
            )
        grad_pre = gelu_pull(grad_hidden)[0].astype(jnp.bfloat16)
        inner_grad = placed_rows(
            [(me, product("wtd,wtf->df", seasonal_mine, grad_pre))]
            + [((me - s) % head_parts, product("wtd,wtf->df", seasonal_recv[s], grad_pre)) for s in shifts],
            local_width,
            model_width,
        )
        grad_season_part, _ = scattered_product(grad_pre, inner_t, local_width)
        grad_season = grad_comb + grad_season_part
        grad_resid = grad_season - trend_back(grad_season, first_rows)
        grad_attend_mine = grad_resid.astype(jnp.bfloat16)
        grad_attend_recv = {s: swap(grad_attend_mine, s) for s in shifts}
        feed, feed_sent = scattered_product(hidden, outer_low, local_width, after=grad_attend_recv.values())
        combined = seasonal + feed
        output = combined - trend_local(combined, second_rows)
        output_grad_t = placed_rows(
            [(me, product("wtd,wte->de", grad_attend_mine, field))]
            + [((me - s) % head_parts, product("wtd,wte->de", grad_attend_recv[s], field)) for s in shifts],
            local_width,
            model_width,
        )
        grad_field = product("wtd,ed->wte", grad_attend_mine, cols_of(output_low, me, local_width))
        for s in shifts:
            grad_field = grad_field + product(
                "wtd,ed->wte", grad_attend_recv[s], cols_of(output_low, (me - s) % head_parts, local_width)
            )
        grad_field = grad_field.astype(jnp.bfloat16)
        grad_field = grad_field.reshape(windows, length, head_count, head_size)
        grad_mixed = jnp.concatenate(
            [
                product("htm,wthe->whme", inv_cos, grad_field),
                product("htm,wthe->whme", inv_sin, grad_field),
            ],
            axis=-1,
        ).astype(jnp.bfloat16)
        grad_spectrum = product("whmo,hmio->whmi", grad_mixed, block).astype(jnp.bfloat16)
        grad_query = product("hmt,whme->wthe", fwd_cos, grad_spectrum[..., :head_size]) + product(
            "hmt,whme->wthe", fwd_sin, grad_spectrum[..., head_size:]
        )
        grad_query = grad_query.reshape(windows, length, local_width).astype(jnp.bfloat16)
        query_grad = placed_rows(
            [(me, product("wtd,wte->de", inputs_mine, grad_query))]
            + [((me - s) % head_parts, product("wtd,wte->de", inputs_recv[s], grad_query)) for s in shifts],
            local_width,
            model_width,
        )
        input_part, _ = scattered_product(grad_query, query_t, local_width, after=feed_sent.values())
        input_grad = grad_resid + input_part
        spectrum_parts = spectrum.reshape(windows, head_count, mode_count, 2, head_size)
        grad_real = grad_mixed[..., :head_size]
        grad_imag = grad_mixed[..., head_size:]
        paired = jnp.stack(
            [grad_mixed, jnp.concatenate([grad_imag, -grad_real], axis=-1)], axis=3
        )
        mixer_full = product("whmci,whmco->hmio", spectrum_parts, paired).reshape(
            head_count, mode_count * head_size, 2 * head_size
        )
        return output, input_grad, (query_grad, mixer_full, output_grad_t, inner_grad, outer_grad_t)

    chunks = 1
    span = windows // chunks
    first_all = pool_rows(gates[0], length)
    second_all = pool_rows(gates[1], length)
    results = [
        chunk_pass(
            inputs[c * span : (c + 1) * span],
            out_grad[c * span : (c + 1) * span],
            tuple(part[c * span : (c + 1) * span] for part in first_all),
            tuple(part[c * span : (c + 1) * span] for part in second_all),
        )
        for c in range(chunks)
    ]
    output = jnp.concatenate([r[0] for r in results], axis=0)
    input_grad = jnp.concatenate([r[1] for r in results], axis=0)
    query_grad, mixer_full, output_grad_t, inner_grad, outer_grad_t = [
        sum(r[2][i] for r in results[1:]) + results[0][2][i] if chunks > 1 else results[0][2][i]
        for i in range(5)
    ]

    dp_count = lax.axis_size("dp")
    dp_rank = lax.axis_index("dp")

    lanes = 128

    def lead(grad, axis_number):
        shape = grad.shape
        split = shape[:axis_number] + (dp_count, shape[axis_number] // dp_count) + shape[axis_number + 1 :]
        owned_shape = shape[:axis_number] + (shape[axis_number] // dp_count,) + shape[axis_number + 1 :]
        return jnp.moveaxis(grad.reshape(split), axis_number, 0).reshape(dp_count, -1, lanes), owned_shape

    plane = 4 if dp_count % 4 == 0 else 1
    planes = dp_count // plane
    near_groups = [[b * plane + i for i in range(plane)] for b in range(planes)]
    far_groups = [[i + plane * b for b in range(planes)] for i in range(plane)]

    def summed_in_two_stages(joined):
        rows = joined.shape[1]
        by_member = jnp.swapaxes(joined.reshape(planes, plane, rows, lanes), 0, 1)
        first = lax.all_to_all(
            by_member.astype(jnp.bfloat16).reshape(-1, lanes), "dp", 0, 0,
            axis_index_groups=near_groups, tiled=True,
        )
        partial = jnp.sum(first.astype(jnp.float32).reshape(plane, planes * rows, lanes), axis=0)
        second = lax.all_to_all(
            partial.astype(jnp.bfloat16), "dp", 0, 0, axis_index_groups=far_groups, tiled=True
        )
        return jnp.sum(second.astype(jnp.float32).reshape(planes, rows, lanes), axis=0)

    def summed_over_dp(grads_axes):
        laid = [lead(grad, axis_number) for grad, axis_number in grads_axes]
        joined = jnp.concatenate([flat for flat, _ in laid], axis=1)
        reduced = summed_in_two_stages(joined)
        parts = []
        offset = 0
        for flat, owned_shape in laid:
            size = flat.shape[1]
            parts.append(reduced[offset : offset + size].reshape(owned_shape))
            offset += size
        return parts

    inner_part, outer_part_t = summed_over_dp([(inner_grad, 0), (outer_grad_t, 0)])
    mixer_part, output_part_t = summed_over_dp([(mixer_full, 1), (output_grad_t, 0)])
    (query_part,) = summed_over_dp([(query_grad, 0)])
    output_part = jnp.transpose(output_part_t)
    outer_part = jnp.transpose(outer_part_t)
    token_total = windows * length * dp_count

    def owned(weight, share, axis_number):
        return lax.dynamic_slice_in_dim(weight, dp_rank * share, share, axis_number)

    def stepped(grad, momentum, average, old_weight, spread):
        rate = 0.5 * spread / math.sqrt(token_total)
        new_momentum = momentum_decay * momentum + grad
        new_weight = old_weight - rate * (grad + momentum_decay * new_momentum)
        new_average = average_decay * average + (1 - average_decay) * new_weight
        return (new_momentum, new_weight, new_average)

    query_new = stepped(
        query_part,
        query_momentum,
        query_average,
        owned(query_weight, query_momentum.shape[0], 0),
        D ** (-0.5),
    )
    mixer_new = stepped(
        mixer_part,
        mixer_momentum,
        mixer_average,
        owned(mixer_weight, mixer_momentum.shape[1], 1),
        mixer_spread,
    )
    output_new = stepped(
        output_part,
        output_momentum,
        output_average,
        owned(output_weight, output_momentum.shape[1], 1),
        D ** (-0.5),
    )
    inner_new = stepped(
        inner_part,
        inner_momentum,
        inner_average,
        owned(inner_weight, inner_momentum.shape[0], 0),
        D ** (-0.5),
    )
    outer_new = stepped(
        outer_part,
        outer_momentum,
        outer_average,
        owned(outer_weight, outer_momentum.shape[1], 1),
        FF ** (-0.5),
    )
    return (
        output,
        input_grad,
        query_new[0],
        query_new[1],
        query_new[2],
        mixer_new[0],
        mixer_new[1],
        mixer_new[2],
        output_new[0],
        output_new[1],
        output_new[2],
        inner_new[0],
        inner_new[1],
        inner_new[2],
        outer_new[0],
        outer_new[1],
        outer_new[2],
    )


def solution(mesh):
    return jax.shard_map(
        on_device,
        mesh=mesh,
        in_specs=(
            P("dp", None, "head"),
            P("dp", None, "head"),
            P("head", None),
            P(None, "dp", None),
            P(None, "head"),
            P("head", None, None),
            P("head", None),
            P(None, "head"),
            P("head", None),
            P("dp", "head"),
            P("dp", "head"),
            P("head", "dp", None),
            P("head", "dp", None),
            P("head", "dp"),
            P("head", "dp"),
            P("dp", "head"),
            P("dp", "head"),
            P("head", "dp"),
            P("head", "dp"),
        ),
        out_specs=(
            P("dp", None, "head"),
            P("dp", None, "head"),
            P("dp", "head"),
            P("dp", "head"),
            P("dp", "head"),
            P("head", "dp", None),
            P("head", "dp", None),
            P("head", "dp", None),
            P("head", "dp"),
            P("head", "dp"),
            P("head", "dp"),
            P("dp", "head"),
            P("dp", "head"),
            P("dp", "head"),
            P("head", "dp"),
            P("head", "dp"),
            P("head", "dp"),
        ),
        check_vma=False,
    )
```

```python
import math

import jax
import jax.numpy as jnp
import numpy as np
from jax import lax
from jax.sharding import PartitionSpec as P


D = 512
FF = 2048


pool_sizes = (7, 12, 14, 24, 48)
mixer_spread = 0.07
momentum_decay = 0.9
average_decay = 0.9


def pool_tables(length):
    tables = np.zeros((len(pool_sizes), length, length), np.float32)
    rows_all = np.arange(length)
    for pool_index, pool_width in enumerate(pool_sizes):
        lead_pad = (pool_width - 1) // 2
        for offset in range(pool_width):
            source = np.clip(rows_all - lead_pad + offset, 0, length - 1)
            tables[pool_index][rows_all, source] += np.float32(1.0 / pool_width)
    return jnp.asarray(tables)


def spectral_tables(modes, length):
    positions = jnp.arange(length, dtype=jnp.int32)
    phase = modes[:, :, None] * positions[None, None, :] % length
    angle = phase.astype(jnp.float32) * (2.0 * math.pi / length)
    cosine = jnp.cos(angle)
    sine = jnp.sin(angle)
    doubled = jnp.where((modes == 0) | (2 * modes == length), 1.0, 2.0).astype(jnp.float32) / length
    inv_cos = jnp.transpose(doubled[:, :, None] * cosine, (0, 2, 1))
    inv_sin = jnp.transpose(-doubled[:, :, None] * sine, (0, 2, 1))
    return (cosine, -sine, inv_cos, inv_sin)


def product(form, left, right):
    return jnp.einsum(form, left, right, preferred_element_type=jnp.float32)


def pool_counts(length):
    counts = np.zeros((len(pool_sizes), length, length), np.float32)
    rows_all = np.arange(length)
    for pool_index, pool_width in enumerate(pool_sizes):
        lead_pad = (pool_width - 1) // 2
        for offset in range(pool_width):
            source = np.clip(rows_all - lead_pad + offset, 0, length - 1)
            counts[pool_index][rows_all, source] += 1.0
    return counts


def pool_rows(picks, length):
    counts = pool_counts(length)
    rows = jnp.zeros(picks.shape + (length,), jnp.float32)
    scale = jnp.zeros(picks.shape, jnp.float32)
    for pool_index, pool_width in enumerate(pool_sizes):
        chosen = picks == pool_index
        rows = jnp.where(chosen[..., None], jnp.asarray(counts[pool_index])[None], rows)
        scale = jnp.where(chosen, np.float32(1.0 / pool_width), scale)
    return rows.astype(jnp.bfloat16), scale


def split_three(values):
    high = values.astype(jnp.bfloat16)
    rest = values - high.astype(jnp.float32)
    middle = rest.astype(jnp.bfloat16)
    low = (rest - middle.astype(jnp.float32)).astype(jnp.bfloat16)
    return high, middle, low


def trend_local(values, rows):
    counts, scale = rows
    parts = jnp.concatenate(split_three(values), axis=1)
    tiled = jnp.concatenate([counts] * 3, axis=2)
    summed = jnp.einsum("wts,wsd->wtd", tiled, parts, preferred_element_type=jnp.float32)
    return summed * scale[..., None]


def trend_back(grads, rows):
    counts, scale = rows
    parts = jnp.concatenate(split_three(grads * scale[..., None]), axis=1)
    tiled = jnp.concatenate([counts] * 3, axis=1)
    return jnp.einsum("wts,wtd->wsd", tiled, parts, preferred_element_type=jnp.float32)


def mixer_block(mixer_low, head_size):
    head_count = mixer_low.shape[0]
    shaped = mixer_low.reshape(head_count, -1, head_size, 2 * head_size)
    real_part = shaped[..., :head_size]
    imag_part = shaped[..., head_size:]
    upper = jnp.concatenate([real_part, imag_part], axis=-1)
    lower = jnp.concatenate([-imag_part, real_part], axis=-1)
    return jnp.concatenate([upper, lower], axis=2)


def exact_gelu(values):
    return jax.nn.gelu(values, approximate=False)


def on_device(
    inputs,
    out_grad,
    modes,
    gates,
    query_weight,
    mixer_weight,
    output_weight,
    inner_weight,
    outer_weight,
    query_momentum,
    query_average,
    mixer_momentum,
    mixer_average,
    output_momentum,
    output_average,
    inner_momentum,
    inner_average,
    outer_momentum,
    outer_average,
):
    windows, length, local_width = inputs.shape
    head_count, mode_count = modes.shape
    head_size = local_width // head_count
    head_parts = lax.axis_size("head")
    me = lax.axis_index("head")
    shifts = list(range(1, head_parts))

    def peer(shift):
        return (me + shift) % head_parts

    def swap(values, shift):
        pairs = [(j, (j + shift) % head_parts) for j in range(head_parts)]
        return lax.ppermute(values, "head", pairs)

    def rows_of(weight, block, size):
        return lax.dynamic_slice_in_dim(weight, block * size, size, 0)

    def cols_of(weight, block, size):
        return lax.dynamic_slice_in_dim(weight, block * size, size, 1)

    def gathered_product(mine, weight_low, size):
        received = {s: swap(mine, s) for s in shifts}
        total = product("wtd,de->wte", mine, rows_of(weight_low, me, size))
        for s in shifts:
            owner = (me - s) % head_parts
            total = total + product("wtd,de->wte", received[s], rows_of(weight_low, owner, size))
        return total, received

    def scattered_product(values, weight_low, size, after=()):
        outgoing = {
            s: product("wte,ed->wtd", values, cols_of(weight_low, peer(s), size)).astype(jnp.bfloat16)
            for s in shifts
        }
        if after:
            outgoing, _ = lax.optimization_barrier((outgoing, tuple(after)))
        sent = {s: swap(outgoing[s], s) for s in shifts}
        total = product("wte,ed->wtd", values, cols_of(weight_low, me, size))
        for s in shifts:
            total = total + sent[s].astype(jnp.float32)
        return total, sent

    def placed_rows(parts, size, total_rows):
        out = jnp.zeros((total_rows,) + parts[0][1].shape[1:], jnp.float32)
        for block, part in parts:
            out = lax.dynamic_update_slice_in_dim(out, part, block * size, 0)
        return out

    model_width = local_width * head_parts
    pools = pool_tables(length)
    fwd_cos, fwd_sin, inv_cos, inv_sin = [
        one_table.astype(jnp.bfloat16) for one_table in spectral_tables(modes, length)
    ]
    query_low = query_weight.astype(jnp.bfloat16)
    output_low = output_weight.astype(jnp.bfloat16)
    inner_low = inner_weight.astype(jnp.bfloat16)
    outer_low = outer_weight.astype(jnp.bfloat16)
    inner_t = jnp.transpose(inner_low)
    query_t = jnp.transpose(query_low)
    block = mixer_block(mixer_weight.astype(jnp.bfloat16), head_size)

    def chunk_pass(inputs, out_grad, first_rows, second_rows):
        windows = inputs.shape[0]
        grad_comb = out_grad - trend_back(out_grad, second_rows)
        grad_feed_mine = grad_comb.astype(jnp.bfloat16)

        inputs_mine = inputs.astype(jnp.bfloat16)
        query, inputs_recv = gathered_product(inputs_mine, query_low, local_width)
        grad_feed_recv = {s: swap(grad_feed_mine, s) for s in shifts}
        query = query.astype(jnp.bfloat16)
        query_heads = query.reshape(windows, length, head_count, head_size)
        spectrum = jnp.concatenate(
            [
                product("hmt,wthe->whme", fwd_cos, query_heads),
                product("hmt,wthe->whme", fwd_sin, query_heads),
            ],
            axis=-1,
        ).astype(jnp.bfloat16)
        mixed = product("whmi,hmio->whmo", spectrum, block).astype(jnp.bfloat16)
        field = product("htm,whme->wthe", inv_cos, mixed[..., :head_size]) + product(
            "htm,whme->wthe", inv_sin, mixed[..., head_size:]
        )
        field = field.reshape(windows, length, local_width).astype(jnp.bfloat16)
        attended, _ = scattered_product(field, output_low, local_width)
        resid_one = inputs + attended
        seasonal = resid_one - trend_local(resid_one, first_rows)
        seasonal_mine = seasonal.astype(jnp.bfloat16)
        pre, seasonal_recv = gathered_product(seasonal_mine, inner_low, local_width)
        activated, gelu_pull = jax.vjp(exact_gelu, pre)
        hidden = activated.astype(jnp.bfloat16)

        outer_grad_t = placed_rows(
            [(me, product("wtd,wtf->df", grad_feed_mine, hidden))]
            + [((me - s) % head_parts, product("wtd,wtf->df", grad_feed_recv[s], hidden)) for s in shifts],
            local_width,
            model_width,
        )
        grad_hidden = product("wtd,fd->wtf", grad_feed_mine, cols_of(outer_low, me, local_width))
        for s in shifts:
            grad_hidden = grad_hidden + product(
                "wtd,fd->wtf", grad_feed_recv[s], cols_of(outer_low, (me - s) % head_parts, local_width)
            )
        grad_pre = gelu_pull(grad_hidden)[0].astype(jnp.bfloat16)
        inner_grad = placed_rows(
            [(me, product("wtd,wtf->df", seasonal_mine, grad_pre))]
            + [((me - s) % head_parts, product("wtd,wtf->df", seasonal_recv[s], grad_pre)) for s in shifts],
            local_width,
            model_width,
        )
        grad_season_part, _ = scattered_product(grad_pre, inner_t, local_width)
        grad_season = grad_comb + grad_season_part
        grad_resid = grad_season - trend_back(grad_season, first_rows)
        grad_attend_mine = grad_resid.astype(jnp.bfloat16)
        grad_attend_recv = {s: swap(grad_attend_mine, s) for s in shifts}
        feed, feed_sent = scattered_product(hidden, outer_low, local_width, after=grad_attend_recv.values())
        combined = seasonal + feed
        output = combined - trend_local(combined, second_rows)
        output_grad_t = placed_rows(
            [(me, product("wtd,wte->de", grad_attend_mine, field))]
            + [((me - s) % head_parts, product("wtd,wte->de", grad_attend_recv[s], field)) for s in shifts],
            local_width,
            model_width,
        )
        grad_field = product("wtd,ed->wte", grad_attend_mine, cols_of(output_low, me, local_width))
        for s in shifts:
            grad_field = grad_field + product(
                "wtd,ed->wte", grad_attend_recv[s], cols_of(output_low, (me - s) % head_parts, local_width)
            )
        grad_field = grad_field.astype(jnp.bfloat16)
        grad_field = grad_field.reshape(windows, length, head_count, head_size)
        grad_mixed = jnp.concatenate(
            [
                product("htm,wthe->whme", inv_cos, grad_field),
                product("htm,wthe->whme", inv_sin, grad_field),
            ],
            axis=-1,
        ).astype(jnp.bfloat16)
        grad_spectrum = product("whmo,hmio->whmi", grad_mixed, block).astype(jnp.bfloat16)
        grad_query = product("hmt,whme->wthe", fwd_cos, grad_spectrum[..., :head_size]) + product(
            "hmt,whme->wthe", fwd_sin, grad_spectrum[..., head_size:]
        )
        grad_query = grad_query.reshape(windows, length, local_width).astype(jnp.bfloat16)
        query_grad = placed_rows(
            [(me, product("wtd,wte->de", inputs_mine, grad_query))]
            + [((me - s) % head_parts, product("wtd,wte->de", inputs_recv[s], grad_query)) for s in shifts],
            local_width,
            model_width,
        )
        input_part, _ = scattered_product(grad_query, query_t, local_width, after=feed_sent.values())
        input_grad = grad_resid + input_part
        spectrum_parts = spectrum.reshape(windows, head_count, mode_count, 2, head_size)
        grad_real = grad_mixed[..., :head_size]
        grad_imag = grad_mixed[..., head_size:]
        paired = jnp.stack(
            [grad_mixed, jnp.concatenate([grad_imag, -grad_real], axis=-1)], axis=3
        )
        mixer_full = product("whmci,whmco->hmio", spectrum_parts, paired).reshape(
            head_count, mode_count * head_size, 2 * head_size
        )
        return output, input_grad, (query_grad, mixer_full, output_grad_t, inner_grad, outer_grad_t), (spectrum, grad_mixed)

    chunks = 1
    span = windows // chunks
    first_all = pool_rows(gates[0], length)
    second_all = pool_rows(gates[1], length)
    results = [
        chunk_pass(
            inputs[c * span : (c + 1) * span],
            out_grad[c * span : (c + 1) * span],
            tuple(part[c * span : (c + 1) * span] for part in first_all),
            tuple(part[c * span : (c + 1) * span] for part in second_all),
        )
        for c in range(chunks)
    ]
    output = jnp.concatenate([r[0] for r in results], axis=0)
    input_grad = jnp.concatenate([r[1] for r in results], axis=0)
    query_grad, mixer_full, output_grad_t, inner_grad, outer_grad_t = [
        sum(r[2][i] for r in results[1:]) + results[0][2][i] if chunks > 1 else results[0][2][i]
        for i in range(5)
    ]

    dp_count = lax.axis_size("dp")
    dp_rank = lax.axis_index("dp")

    lanes = 128

    def lead(grad, axis_number):
        shape = grad.shape
        split = shape[:axis_number] + (dp_count, shape[axis_number] // dp_count) + shape[axis_number + 1 :]
        owned_shape = shape[:axis_number] + (shape[axis_number] // dp_count,) + shape[axis_number + 1 :]
        return jnp.moveaxis(grad.reshape(split), axis_number, 0).reshape(dp_count, -1, lanes), owned_shape

    def summed_over_dp(grads_axes):
        laid = [lead(grad, axis_number) for grad, axis_number in grads_axes]
        joined = jnp.concatenate([flat for flat, _ in laid], axis=1)
        rows = joined.shape[1]
        arrived = lax.all_to_all(
            joined.astype(jnp.bfloat16).reshape(-1, lanes), "dp", 0, 0, tiled=True
        )
        reduced = jnp.sum(arrived.astype(jnp.float32).reshape(dp_count, rows, lanes), axis=0)
        parts = []
        offset = 0
        for flat, owned_shape in laid:
            size = flat.shape[1]
            parts.append(reduced[offset : offset + size].reshape(owned_shape))
            offset += size
        return parts

    inner_part, outer_part_t = summed_over_dp([(inner_grad, 0), (outer_grad_t, 0)])
    if mode_count % dp_count == 0:
        per = mode_count // dp_count
        spectra = jnp.concatenate([r[3][0] for r in results], axis=0)
        mixed_grads = jnp.concatenate([r[3][1] for r in results], axis=0)
        all_windows = spectra.shape[0]

        def by_owner(values):
            split = values.reshape(all_windows, head_count, dp_count, per, 2 * head_size)
            return jnp.moveaxis(split, 2, 0).reshape(dp_count, -1, lanes)

        spectra_in = lax.all_to_all(by_owner(spectra).reshape(-1, lanes), "dp", 0, 0, tiled=True)
        gm_flat = by_owner(mixed_grads)
        gm_rows = gm_flat.shape[1]
        out_flat, out_shape = lead(output_grad_t, 0)
        joined = jnp.concatenate([gm_flat, out_flat.astype(jnp.bfloat16)], axis=1)
        arrived = lax.all_to_all(joined.reshape(-1, lanes), "dp", 0, 0, tiled=True)
        arrived = arrived.reshape(dp_count, -1, lanes)
        output_part_t = jnp.sum(arrived[:, gm_rows:].astype(jnp.float32), axis=0).reshape(out_shape)
        owned = (dp_count, all_windows, head_count, per)
        spectrum_in = spectra_in.reshape(owned + (2, head_size))
        gm_in = arrived[:, :gm_rows].reshape(owned + (2 * head_size,))
        gm_pairs = jnp.stack(
            [gm_in, jnp.concatenate([gm_in[..., head_size:], -gm_in[..., :head_size]], axis=-1)], axis=4
        )
        mixer_part = product("swhmci,swhmco->hmio", spectrum_in, gm_pairs).reshape(
            head_count, per * head_size, 2 * head_size
        )
    else:
        mixer_part, output_part_t = summed_over_dp([(mixer_full, 1), (output_grad_t, 0)])
    (query_part,) = summed_over_dp([(query_grad, 0)])
    output_part = jnp.transpose(output_part_t)
    outer_part = jnp.transpose(outer_part_t)
    token_total = windows * length * dp_count

    def owned(weight, share, axis_number):
        return lax.dynamic_slice_in_dim(weight, dp_rank * share, share, axis_number)

    def stepped(grad, momentum, average, old_weight, spread):
        rate = 0.5 * spread / math.sqrt(token_total)
        new_momentum = momentum_decay * momentum + grad
        new_weight = old_weight - rate * (grad + momentum_decay * new_momentum)
        new_average = average_decay * average + (1 - average_decay) * new_weight
        return (new_momentum, new_weight, new_average)

    query_new = stepped(
        query_part,
        query_momentum,
        query_average,
        owned(query_weight, query_momentum.shape[0], 0),
        D ** (-0.5),
    )
    mixer_new = stepped(
        mixer_part,
        mixer_momentum,
        mixer_average,
        owned(mixer_weight, mixer_momentum.shape[1], 1),
        mixer_spread,
    )
    output_new = stepped(
        output_part,
        output_momentum,
        output_average,
        owned(output_weight, output_momentum.shape[1], 1),
        D ** (-0.5),
    )
    inner_new = stepped(
        inner_part,
        inner_momentum,
        inner_average,
        owned(inner_weight, inner_momentum.shape[0], 0),
        D ** (-0.5),
    )
    outer_new = stepped(
        outer_part,
        outer_momentum,
        outer_average,
        owned(outer_weight, outer_momentum.shape[1], 1),
        FF ** (-0.5),
    )
    return (
        output,
        input_grad,
        query_new[0],
        query_new[1],
        query_new[2],
        mixer_new[0],
        mixer_new[1],
        mixer_new[2],
        output_new[0],
        output_new[1],
        output_new[2],
        inner_new[0],
        inner_new[1],
        inner_new[2],
        outer_new[0],
        outer_new[1],
        outer_new[2],
    )


def solution(mesh):
    return jax.shard_map(
        on_device,
        mesh=mesh,
        in_specs=(
            P("dp", None, "head"),
            P("dp", None, "head"),
            P("head", None),
            P(None, "dp", None),
            P(None, "head"),
            P("head", None, None),
            P("head", None),
            P(None, "head"),
            P("head", None),
            P("dp", "head"),
            P("dp", "head"),
            P("head", "dp", None),
            P("head", "dp", None),
            P("head", "dp"),
            P("head", "dp"),
            P("dp", "head"),
            P("dp", "head"),
            P("head", "dp"),
            P("head", "dp"),
        ),
        out_specs=(
            P("dp", None, "head"),
            P("dp", None, "head"),
            P("dp", "head"),
            P("dp", "head"),
            P("dp", "head"),
            P("head", "dp", None),
            P("head", "dp", None),
            P("head", "dp", None),
            P("head", "dp"),
            P("head", "dp"),
            P("head", "dp"),
            P("dp", "head"),
            P("dp", "head"),
            P("dp", "head"),
            P("head", "dp"),
            P("head", "dp"),
            P("head", "dp"),
        ),
        check_vma=False,
    )
```

```python
import math

import jax
import jax.numpy as jnp
import numpy as np
from jax import lax
from jax.sharding import PartitionSpec as P


D = 512
FF = 2048


pool_sizes = (7, 12, 14, 24, 48)
mixer_spread = 0.07
momentum_decay = 0.9
average_decay = 0.9


def pool_tables(length):
    tables = np.zeros((len(pool_sizes), length, length), np.float32)
    rows_all = np.arange(length)
    for pool_index, pool_width in enumerate(pool_sizes):
        lead_pad = (pool_width - 1) // 2
        for offset in range(pool_width):
            source = np.clip(rows_all - lead_pad + offset, 0, length - 1)
            tables[pool_index][rows_all, source] += np.float32(1.0 / pool_width)
    return jnp.asarray(tables)


def spectral_tables(modes, length):
    positions = jnp.arange(length, dtype=jnp.int32)
    phase = modes[:, :, None] * positions[None, None, :] % length
    angle = phase.astype(jnp.float32) * (2.0 * math.pi / length)
    cosine = jnp.cos(angle)
    sine = jnp.sin(angle)
    doubled = jnp.where((modes == 0) | (2 * modes == length), 1.0, 2.0).astype(jnp.float32) / length
    inv_cos = jnp.transpose(doubled[:, :, None] * cosine, (0, 2, 1))
    inv_sin = jnp.transpose(-doubled[:, :, None] * sine, (0, 2, 1))
    return (cosine, -sine, inv_cos, inv_sin)


def product(form, left, right):
    return jnp.einsum(form, left, right, preferred_element_type=jnp.float32)


def pool_counts(length):
    counts = np.zeros((len(pool_sizes), length, length), np.float32)
    rows_all = np.arange(length)
    for pool_index, pool_width in enumerate(pool_sizes):
        lead_pad = (pool_width - 1) // 2
        for offset in range(pool_width):
            source = np.clip(rows_all - lead_pad + offset, 0, length - 1)
            counts[pool_index][rows_all, source] += 1.0
    return counts


def pool_rows(picks, length):
    counts = pool_counts(length)
    rows = jnp.zeros(picks.shape + (length,), jnp.float32)
    scale = jnp.zeros(picks.shape, jnp.float32)
    for pool_index, pool_width in enumerate(pool_sizes):
        chosen = picks == pool_index
        rows = jnp.where(chosen[..., None], jnp.asarray(counts[pool_index])[None], rows)
        scale = jnp.where(chosen, np.float32(1.0 / pool_width), scale)
    return rows.astype(jnp.bfloat16), scale


def split_three(values):
    high = values.astype(jnp.bfloat16)
    rest = values - high.astype(jnp.float32)
    middle = rest.astype(jnp.bfloat16)
    low = (rest - middle.astype(jnp.float32)).astype(jnp.bfloat16)
    return high, middle, low


def trend_local(values, rows):
    counts, scale = rows
    parts = jnp.concatenate(split_three(values), axis=1)
    tiled = jnp.concatenate([counts] * 3, axis=2)
    summed = jnp.einsum("wts,wsd->wtd", tiled, parts, preferred_element_type=jnp.float32)
    return summed * scale[..., None]


def trend_back(grads, rows):
    counts, scale = rows
    parts = jnp.concatenate(split_three(grads * scale[..., None]), axis=1)
    tiled = jnp.concatenate([counts] * 3, axis=1)
    return jnp.einsum("wts,wtd->wsd", tiled, parts, preferred_element_type=jnp.float32)


def mixer_block(mixer_low, head_size):
    head_count = mixer_low.shape[0]
    shaped = mixer_low.reshape(head_count, -1, head_size, 2 * head_size)
    real_part = shaped[..., :head_size]
    imag_part = shaped[..., head_size:]
    upper = jnp.concatenate([real_part, imag_part], axis=-1)
    lower = jnp.concatenate([-imag_part, real_part], axis=-1)
    return jnp.concatenate([upper, lower], axis=2)


def exact_gelu(values):
    return jax.nn.gelu(values, approximate=False)


def on_device(
    inputs,
    out_grad,
    modes,
    gates,
    query_weight,
    mixer_weight,
    output_weight,
    inner_weight,
    outer_weight,
    query_momentum,
    query_average,
    mixer_momentum,
    mixer_average,
    output_momentum,
    output_average,
    inner_momentum,
    inner_average,
    outer_momentum,
    outer_average,
):
    windows, length, local_width = inputs.shape
    head_count, mode_count = modes.shape
    head_size = local_width // head_count
    head_parts = lax.axis_size("head")
    me = lax.axis_index("head")
    shifts = list(range(1, head_parts))

    def peer(shift):
        return (me + shift) % head_parts

    def swap(values, shift):
        pairs = [(j, (j + shift) % head_parts) for j in range(head_parts)]
        return lax.ppermute(values, "head", pairs)

    def rows_of(weight, block, size):
        return lax.dynamic_slice_in_dim(weight, block * size, size, 0)

    def cols_of(weight, block, size):
        return lax.dynamic_slice_in_dim(weight, block * size, size, 1)

    def gathered_product(mine, weight_low, size):
        received = {s: swap(mine, s) for s in shifts}
        total = product("wtd,de->wte", mine, rows_of(weight_low, me, size))
        for s in shifts:
            owner = (me - s) % head_parts
            total = total + product("wtd,de->wte", received[s], rows_of(weight_low, owner, size))
        return total, received

    def scattered_product(values, weight_low, size, after=()):
        outgoing = {
            s: product("wte,ed->wtd", values, cols_of(weight_low, peer(s), size)).astype(jnp.bfloat16)
            for s in shifts
        }
        if after:
            outgoing, _ = lax.optimization_barrier((outgoing, tuple(after)))
        sent = {s: swap(outgoing[s], s) for s in shifts}
        total = product("wte,ed->wtd", values, cols_of(weight_low, me, size))
        for s in shifts:
            total = total + sent[s].astype(jnp.float32)
        return total, sent

    def placed_rows(parts, size, total_rows):
        out = jnp.zeros((total_rows,) + parts[0][1].shape[1:], jnp.float32)
        for block, part in parts:
            out = lax.dynamic_update_slice_in_dim(out, part, block * size, 0)
        return out

    model_width = local_width * head_parts
    pools = pool_tables(length)
    fwd_cos, fwd_sin, inv_cos, inv_sin = [
        one_table.astype(jnp.bfloat16) for one_table in spectral_tables(modes, length)
    ]
    query_low = query_weight.astype(jnp.bfloat16)
    output_low = output_weight.astype(jnp.bfloat16)
    inner_low = inner_weight.astype(jnp.bfloat16)
    outer_low = outer_weight.astype(jnp.bfloat16)
    inner_t = jnp.transpose(inner_low)
    query_t = jnp.transpose(query_low)
    block = mixer_block(mixer_weight.astype(jnp.bfloat16), head_size)

    def chunk_pass(inputs, out_grad, first_rows, second_rows):
        windows = inputs.shape[0]
        grad_comb = out_grad - trend_back(out_grad, second_rows)
        grad_feed_mine = grad_comb.astype(jnp.bfloat16)

        inputs_mine = inputs.astype(jnp.bfloat16)
        query, inputs_recv = gathered_product(inputs_mine, query_low, local_width)
        grad_feed_recv = {s: swap(grad_feed_mine, s) for s in shifts}
        query = query.astype(jnp.bfloat16)
        query_heads = query.reshape(windows, length, head_count, head_size)
        spectrum = jnp.concatenate(
            [
                product("hmt,wthe->whme", fwd_cos, query_heads),
                product("hmt,wthe->whme", fwd_sin, query_heads),
            ],
            axis=-1,
        ).astype(jnp.bfloat16)
        mixed = product("whmi,hmio->whmo", spectrum, block).astype(jnp.bfloat16)
        field = product("htm,whme->wthe", inv_cos, mixed[..., :head_size]) + product(
            "htm,whme->wthe", inv_sin, mixed[..., head_size:]
        )
        field = field.reshape(windows, length, local_width).astype(jnp.bfloat16)
        attended, _ = scattered_product(field, output_low, local_width)
        resid_one = inputs + attended
        seasonal = resid_one - trend_local(resid_one, first_rows)
        seasonal_mine = seasonal.astype(jnp.bfloat16)
        pre, seasonal_recv = gathered_product(seasonal_mine, inner_low, local_width)
        activated, gelu_pull = jax.vjp(exact_gelu, pre)
        hidden = activated.astype(jnp.bfloat16)

        outer_grad_t = placed_rows(
            [(me, product("wtd,wtf->df", grad_feed_mine, hidden))]
            + [((me - s) % head_parts, product("wtd,wtf->df", grad_feed_recv[s], hidden)) for s in shifts],
            local_width,
            model_width,
        )
        grad_hidden = product("wtd,fd->wtf", grad_feed_mine, cols_of(outer_low, me, local_width))
        for s in shifts:
            grad_hidden = grad_hidden + product(
                "wtd,fd->wtf", grad_feed_recv[s], cols_of(outer_low, (me - s) % head_parts, local_width)
            )
        grad_pre = gelu_pull(grad_hidden)[0].astype(jnp.bfloat16)
        inner_grad = placed_rows(
            [(me, product("wtd,wtf->df", seasonal_mine, grad_pre))]
            + [((me - s) % head_parts, product("wtd,wtf->df", seasonal_recv[s], grad_pre)) for s in shifts],
            local_width,
            model_width,
        )
        grad_season_part, _ = scattered_product(grad_pre, inner_t, local_width)
        grad_season = grad_comb + grad_season_part
        grad_resid = grad_season - trend_back(grad_season, first_rows)
        grad_attend_mine = grad_resid.astype(jnp.bfloat16)
        grad_attend_recv = {s: swap(grad_attend_mine, s) for s in shifts}
        feed, feed_sent = scattered_product(hidden, outer_low, local_width, after=grad_attend_recv.values())
        combined = seasonal + feed
        output = combined - trend_local(combined, second_rows)
        output_grad_t = placed_rows(
            [(me, product("wtd,wte->de", grad_attend_mine, field))]
            + [((me - s) % head_parts, product("wtd,wte->de", grad_attend_recv[s], field)) for s in shifts],
            local_width,
            model_width,
        )
        grad_field = product("wtd,ed->wte", grad_attend_mine, cols_of(output_low, me, local_width))
        for s in shifts:
            grad_field = grad_field + product(
                "wtd,ed->wte", grad_attend_recv[s], cols_of(output_low, (me - s) % head_parts, local_width)
            )
        grad_field = grad_field.astype(jnp.bfloat16)
        grad_field = grad_field.reshape(windows, length, head_count, head_size)
        grad_mixed = jnp.concatenate(
            [
                product("htm,wthe->whme", inv_cos, grad_field),
                product("htm,wthe->whme", inv_sin, grad_field),
            ],
            axis=-1,
        ).astype(jnp.bfloat16)
        grad_spectrum = product("whmo,hmio->whmi", grad_mixed, block).astype(jnp.bfloat16)
        grad_query = product("hmt,whme->wthe", fwd_cos, grad_spectrum[..., :head_size]) + product(
            "hmt,whme->wthe", fwd_sin, grad_spectrum[..., head_size:]
        )
        grad_query = grad_query.reshape(windows, length, local_width).astype(jnp.bfloat16)
        query_grad = placed_rows(
            [(me, product("wtd,wte->de", inputs_mine, grad_query))]
            + [((me - s) % head_parts, product("wtd,wte->de", inputs_recv[s], grad_query)) for s in shifts],
            local_width,
            model_width,
        )
        input_part, _ = scattered_product(grad_query, query_t, local_width, after=feed_sent.values())
        input_grad = grad_resid + input_part
        spectrum_parts = spectrum.reshape(windows, head_count, mode_count, 2, head_size)
        grad_real = grad_mixed[..., :head_size]
        grad_imag = grad_mixed[..., head_size:]
        paired = jnp.stack(
            [grad_mixed, jnp.concatenate([grad_imag, -grad_real], axis=-1)], axis=3
        )
        mixer_full = product("whmci,whmco->hmio", spectrum_parts, paired).reshape(
            head_count, mode_count * head_size, 2 * head_size
        )
        return output, input_grad, (query_grad, mixer_full, output_grad_t, inner_grad, outer_grad_t)

    chunks = 1
    span = windows // chunks
    first_all = pool_rows(gates[0], length)
    second_all = pool_rows(gates[1], length)
    results = [
        chunk_pass(
            inputs[c * span : (c + 1) * span],
            out_grad[c * span : (c + 1) * span],
            tuple(part[c * span : (c + 1) * span] for part in first_all),
            tuple(part[c * span : (c + 1) * span] for part in second_all),
        )
        for c in range(chunks)
    ]
    output = jnp.concatenate([r[0] for r in results], axis=0)
    input_grad = jnp.concatenate([r[1] for r in results], axis=0)
    query_grad, mixer_full, output_grad_t, inner_grad, outer_grad_t = [
        sum(r[2][i] for r in results[1:]) + results[0][2][i] if chunks > 1 else results[0][2][i]
        for i in range(5)
    ]

    dp_count = lax.axis_size("dp")
    dp_rank = lax.axis_index("dp")

    lanes = 128

    def lead(grad, axis_number):
        shape = grad.shape
        split = shape[:axis_number] + (dp_count, shape[axis_number] // dp_count) + shape[axis_number + 1 :]
        owned_shape = shape[:axis_number] + (shape[axis_number] // dp_count,) + shape[axis_number + 1 :]
        return jnp.moveaxis(grad.reshape(split), axis_number, 0).reshape(dp_count, -1, lanes), owned_shape

    def summed_over_dp(grads_axes):
        laid = [lead(grad, axis_number) for grad, axis_number in grads_axes]
        joined = jnp.concatenate([flat for flat, _ in laid], axis=1)
        rows = joined.shape[1]
        arrived = lax.all_to_all(
            joined.astype(jnp.bfloat16).reshape(-1, lanes), "dp", 0, 0, tiled=True
        )
        reduced = jnp.sum(arrived.astype(jnp.float32).reshape(dp_count, rows, lanes), axis=0)
        parts = []
        offset = 0
        for flat, owned_shape in laid:
            size = flat.shape[1]
            parts.append(reduced[offset : offset + size].reshape(owned_shape))
            offset += size
        return parts

    inner_part, outer_part_t = summed_over_dp([(inner_grad, 0), (outer_grad_t, 0)])
    mixer_part, output_part_t = summed_over_dp([(mixer_full, 1), (output_grad_t, 0)])
    (query_part,) = summed_over_dp([(query_grad, 0)])
    output_part = jnp.transpose(output_part_t)
    outer_part = jnp.transpose(outer_part_t)
    token_total = windows * length * dp_count

    def owned(weight, share, axis_number):
        return lax.dynamic_slice_in_dim(weight, dp_rank * share, share, axis_number)

    def stepped(grad, momentum, average, old_weight, spread):
        rate = 0.5 * spread / math.sqrt(token_total)
        new_momentum = momentum_decay * momentum + grad
        new_weight = old_weight - rate * (grad + momentum_decay * new_momentum)
        new_average = average_decay * average + (1 - average_decay) * new_weight
        return (new_momentum, new_weight, new_average)

    query_new = stepped(
        query_part,
        query_momentum,
        query_average,
        owned(query_weight, query_momentum.shape[0], 0),
        D ** (-0.5),
    )
    mixer_new = stepped(
        mixer_part,
        mixer_momentum,
        mixer_average,
        owned(mixer_weight, mixer_momentum.shape[1], 1),
        mixer_spread,
    )
    output_new = stepped(
        output_part,
        output_momentum,
        output_average,
        owned(output_weight, output_momentum.shape[1], 1),
        D ** (-0.5),
    )
    inner_new = stepped(
        inner_part,
        inner_momentum,
        inner_average,
        owned(inner_weight, inner_momentum.shape[0], 0),
        D ** (-0.5),
    )
    outer_new = stepped(
        outer_part,
        outer_momentum,
        outer_average,
        owned(outer_weight, outer_momentum.shape[1], 1),
        FF ** (-0.5),
    )
    return (
        output,
        input_grad,
        query_new[0],
        query_new[1],
        query_new[2],
        mixer_new[0],
        mixer_new[1],
        mixer_new[2],
        output_new[0],
        output_new[1],
        output_new[2],
        inner_new[0],
        inner_new[1],
        inner_new[2],
        outer_new[0],
        outer_new[1],
        outer_new[2],
    )


def solution(mesh):
    return jax.shard_map(
        on_device,
        mesh=mesh,
        in_specs=(
            P("dp", None, "head"),
            P("dp", None, "head"),
            P("head", None),
            P(None, "dp", None),
            P(None, "head"),
            P("head", None, None),
            P("head", None),
            P(None, "head"),
            P("head", None),
            P("dp", "head"),
            P("dp", "head"),
            P("head", "dp", None),
            P("head", "dp", None),
            P("head", "dp"),
            P("head", "dp"),
            P("dp", "head"),
            P("dp", "head"),
            P("head", "dp"),
            P("head", "dp"),
        ),
        out_specs=(
            P("dp", None, "head"),
            P("dp", None, "head"),
            P("dp", "head"),
            P("dp", "head"),
            P("dp", "head"),
            P("head", "dp", None),
            P("head", "dp", None),
            P("head", "dp", None),
            P("head", "dp"),
            P("head", "dp"),
            P("head", "dp"),
            P("dp", "head"),
            P("dp", "head"),
            P("dp", "head"),
            P("head", "dp"),
            P("head", "dp"),
            P("head", "dp"),
        ),
        check_vma=False,
    )
```

```python
import math

import jax
import jax.numpy as jnp
import numpy as np
from jax import lax
from jax.sharding import PartitionSpec as P


D = 512
FF = 2048


pool_sizes = (7, 12, 14, 24, 48)
mixer_spread = 0.07
momentum_decay = 0.9
average_decay = 0.9


def pool_tables(length):
    tables = np.zeros((len(pool_sizes), length, length), np.float32)
    rows_all = np.arange(length)
    for pool_index, pool_width in enumerate(pool_sizes):
        lead_pad = (pool_width - 1) // 2
        for offset in range(pool_width):
            source = np.clip(rows_all - lead_pad + offset, 0, length - 1)
            tables[pool_index][rows_all, source] += np.float32(1.0 / pool_width)
    return jnp.asarray(tables)


def spectral_tables(modes, length):
    positions = jnp.arange(length, dtype=jnp.int32)
    phase = modes[:, :, None] * positions[None, None, :] % length
    angle = phase.astype(jnp.float32) * (2.0 * math.pi / length)
    cosine = jnp.cos(angle)
    sine = jnp.sin(angle)
    doubled = jnp.where((modes == 0) | (2 * modes == length), 1.0, 2.0).astype(jnp.float32) / length
    inv_cos = jnp.transpose(doubled[:, :, None] * cosine, (0, 2, 1))
    inv_sin = jnp.transpose(-doubled[:, :, None] * sine, (0, 2, 1))
    return (cosine, -sine, inv_cos, inv_sin)


def product(form, left, right):
    return jnp.einsum(form, left, right, preferred_element_type=jnp.float32)


def pool_counts(length):
    counts = np.zeros((len(pool_sizes), length, length), np.float32)
    rows_all = np.arange(length)
    for pool_index, pool_width in enumerate(pool_sizes):
        lead_pad = (pool_width - 1) // 2
        for offset in range(pool_width):
            source = np.clip(rows_all - lead_pad + offset, 0, length - 1)
            counts[pool_index][rows_all, source] += 1.0
    return counts


def pool_rows(picks, length):
    counts = pool_counts(length)
    rows = jnp.zeros(picks.shape + (length,), jnp.float32)
    scale = jnp.zeros(picks.shape, jnp.float32)
    for pool_index, pool_width in enumerate(pool_sizes):
        chosen = picks == pool_index
        rows = jnp.where(chosen[..., None], jnp.asarray(counts[pool_index])[None], rows)
        scale = jnp.where(chosen, np.float32(1.0 / pool_width), scale)
    return rows.astype(jnp.bfloat16), scale


def split_three(values):
    high = values.astype(jnp.bfloat16)
    rest = values - high.astype(jnp.float32)
    middle = rest.astype(jnp.bfloat16)
    low = (rest - middle.astype(jnp.float32)).astype(jnp.bfloat16)
    return high, middle, low


def trend_local(values, rows):
    counts, scale = rows
    parts = jnp.concatenate(split_three(values), axis=1)
    tiled = jnp.concatenate([counts] * 3, axis=2)
    summed = jnp.einsum("wts,wsd->wtd", tiled, parts, preferred_element_type=jnp.float32)
    return summed * scale[..., None]


def trend_back(grads, rows):
    counts, scale = rows
    parts = jnp.concatenate(split_three(grads * scale[..., None]), axis=1)
    tiled = jnp.concatenate([counts] * 3, axis=1)
    return jnp.einsum("wts,wtd->wsd", tiled, parts, preferred_element_type=jnp.float32)


def mixer_block(mixer_low, head_size):
    head_count = mixer_low.shape[0]
    shaped = mixer_low.reshape(head_count, -1, head_size, 2 * head_size)
    real_part = shaped[..., :head_size]
    imag_part = shaped[..., head_size:]
    upper = jnp.concatenate([real_part, imag_part], axis=-1)
    lower = jnp.concatenate([-imag_part, real_part], axis=-1)
    return jnp.concatenate([upper, lower], axis=2)


def exact_gelu(values):
    return jax.nn.gelu(values, approximate=False)


def on_device(
    inputs,
    out_grad,
    modes,
    gates,
    query_weight,
    mixer_weight,
    output_weight,
    inner_weight,
    outer_weight,
    query_momentum,
    query_average,
    mixer_momentum,
    mixer_average,
    output_momentum,
    output_average,
    inner_momentum,
    inner_average,
    outer_momentum,
    outer_average,
):
    windows, length, local_width = inputs.shape
    head_count, mode_count = modes.shape
    head_size = local_width // head_count
    head_parts = lax.axis_size("head")
    me = lax.axis_index("head")
    shifts = list(range(1, head_parts))

    def peer(shift):
        return (me + shift) % head_parts

    def swap(values, shift):
        pairs = [(j, (j + shift) % head_parts) for j in range(head_parts)]
        return lax.ppermute(values, "head", pairs)

    def rows_of(weight, block, size):
        return lax.dynamic_slice_in_dim(weight, block * size, size, 0)

    def cols_of(weight, block, size):
        return lax.dynamic_slice_in_dim(weight, block * size, size, 1)

    def gathered_product(mine, weight_low, size):
        received = {s: swap(mine, s) for s in shifts}
        total = product("wtd,de->wte", mine, rows_of(weight_low, me, size))
        for s in shifts:
            owner = (me - s) % head_parts
            total = total + product("wtd,de->wte", received[s], rows_of(weight_low, owner, size))
        return total, received

    def scattered_product(values, weight_low, size, after=()):
        outgoing = {
            s: product("wte,ed->wtd", values, cols_of(weight_low, peer(s), size)).astype(jnp.bfloat16)
            for s in shifts
        }
        if after:
            outgoing, _ = lax.optimization_barrier((outgoing, tuple(after)))
        sent = {s: swap(outgoing[s], s) for s in shifts}
        total = product("wte,ed->wtd", values, cols_of(weight_low, me, size))
        for s in shifts:
            total = total + sent[s].astype(jnp.float32)
        return total, sent

    def placed_rows(parts, size, total_rows):
        out = jnp.zeros((total_rows,) + parts[0][1].shape[1:], jnp.float32)
        for block, part in parts:
            out = lax.dynamic_update_slice_in_dim(out, part, block * size, 0)
        return out

    model_width = local_width * head_parts
    pools = pool_tables(length)
    fwd_cos, fwd_sin, inv_cos, inv_sin = [
        one_table.astype(jnp.bfloat16) for one_table in spectral_tables(modes, length)
    ]
    query_low = query_weight.astype(jnp.bfloat16)
    output_low = output_weight.astype(jnp.bfloat16)
    inner_low = inner_weight.astype(jnp.bfloat16)
    outer_low = outer_weight.astype(jnp.bfloat16)
    inner_t = jnp.transpose(inner_low)
    query_t = jnp.transpose(query_low)
    block = mixer_block(mixer_weight.astype(jnp.bfloat16), head_size)

    def chunk_pass(inputs, out_grad, first_rows, second_rows):
        windows = inputs.shape[0]
        grad_comb = out_grad - trend_back(out_grad, second_rows)
        grad_feed_mine = grad_comb.astype(jnp.bfloat16)

        inputs_mine = inputs.astype(jnp.bfloat16)
        query, inputs_recv = gathered_product(inputs_mine, query_low, local_width)
        grad_feed_recv = {s: swap(grad_feed_mine, s) for s in shifts}
        query = query.astype(jnp.bfloat16)
        query_heads = query.reshape(windows, length, head_count, head_size)
        spectrum = jnp.concatenate(
            [
                product("hmt,wthe->whme", fwd_cos, query_heads),
                product("hmt,wthe->whme", fwd_sin, query_heads),
            ],
            axis=-1,
        ).astype(jnp.bfloat16)
        mixed = product("whmi,hmio->whmo", spectrum, block).astype(jnp.bfloat16)
        field = product("htm,whme->wthe", inv_cos, mixed[..., :head_size]) + product(
            "htm,whme->wthe", inv_sin, mixed[..., head_size:]
        )
        field = field.reshape(windows, length, local_width).astype(jnp.bfloat16)
        attended, _ = scattered_product(field, output_low, local_width)
        resid_one = inputs + attended
        seasonal = resid_one - trend_local(resid_one, first_rows)
        seasonal_mine = seasonal.astype(jnp.bfloat16)
        pre, seasonal_recv = gathered_product(seasonal_mine, inner_low, local_width)
        activated, gelu_pull = jax.vjp(exact_gelu, pre)
        hidden = activated.astype(jnp.bfloat16)

        outer_grad_t = placed_rows(
            [(me, product("wtd,wtf->df", grad_feed_mine, hidden))]
            + [((me - s) % head_parts, product("wtd,wtf->df", grad_feed_recv[s], hidden)) for s in shifts],
            local_width,
            model_width,
        )
        grad_hidden = product("wtd,fd->wtf", grad_feed_mine, cols_of(outer_low, me, local_width))
        for s in shifts:
            grad_hidden = grad_hidden + product(
                "wtd,fd->wtf", grad_feed_recv[s], cols_of(outer_low, (me - s) % head_parts, local_width)
            )
        grad_pre = gelu_pull(grad_hidden)[0].astype(jnp.bfloat16)
        inner_grad = placed_rows(
            [(me, product("wtd,wtf->df", seasonal_mine, grad_pre))]
            + [((me - s) % head_parts, product("wtd,wtf->df", seasonal_recv[s], grad_pre)) for s in shifts],
            local_width,
            model_width,
        )
        grad_season_part, _ = scattered_product(grad_pre, inner_t, local_width)
        grad_season = grad_comb + grad_season_part
        grad_resid = grad_season - trend_back(grad_season, first_rows)
        grad_attend_mine = grad_resid.astype(jnp.bfloat16)
        grad_attend_recv = {s: swap(grad_attend_mine, s) for s in shifts}
        feed, feed_sent = scattered_product(hidden, outer_low, local_width, after=grad_attend_recv.values())
        combined = seasonal + feed
        output = combined - trend_local(combined, second_rows)
        output_grad_t = placed_rows(
            [(me, product("wtd,wte->de", grad_attend_mine, field))]
            + [((me - s) % head_parts, product("wtd,wte->de", grad_attend_recv[s], field)) for s in shifts],
            local_width,
            model_width,
        )
        grad_field = product("wtd,ed->wte", grad_attend_mine, cols_of(output_low, me, local_width))
        for s in shifts:
            grad_field = grad_field + product(
                "wtd,ed->wte", grad_attend_recv[s], cols_of(output_low, (me - s) % head_parts, local_width)
            )
        grad_field = grad_field.astype(jnp.bfloat16)
        grad_field = grad_field.reshape(windows, length, head_count, head_size)
        grad_mixed = jnp.concatenate(
            [
                product("htm,wthe->whme", inv_cos, grad_field),
                product("htm,wthe->whme", inv_sin, grad_field),
            ],
            axis=-1,
        ).astype(jnp.bfloat16)
        grad_spectrum = product("whmo,hmio->whmi", grad_mixed, block).astype(jnp.bfloat16)
        grad_query = product("hmt,whme->wthe", fwd_cos, grad_spectrum[..., :head_size]) + product(
            "hmt,whme->wthe", fwd_sin, grad_spectrum[..., head_size:]
        )
        grad_query = grad_query.reshape(windows, length, local_width).astype(jnp.bfloat16)
        query_grad = placed_rows(
            [(me, product("wtd,wte->de", inputs_mine, grad_query))]
            + [((me - s) % head_parts, product("wtd,wte->de", inputs_recv[s], grad_query)) for s in shifts],
            local_width,
            model_width,
        )
        input_part, _ = scattered_product(grad_query, query_t, local_width, after=feed_sent.values())
        input_grad = grad_resid + input_part
        spectrum_parts = spectrum.reshape(windows, head_count, mode_count, 2, head_size)
        grad_real = grad_mixed[..., :head_size]
        grad_imag = grad_mixed[..., head_size:]
        paired = jnp.stack(
            [grad_mixed, jnp.concatenate([grad_imag, -grad_real], axis=-1)], axis=3
        )
        mixer_full = product("whmci,whmco->hmio", spectrum_parts, paired).reshape(
            head_count, mode_count * head_size, 2 * head_size
        )
        return output, input_grad, (query_grad, mixer_full, output_grad_t, inner_grad, outer_grad_t), (spectrum, grad_mixed)

    chunks = 1
    span = windows // chunks
    first_all = pool_rows(gates[0], length)
    second_all = pool_rows(gates[1], length)
    results = [
        chunk_pass(
            inputs[c * span : (c + 1) * span],
            out_grad[c * span : (c + 1) * span],
            tuple(part[c * span : (c + 1) * span] for part in first_all),
            tuple(part[c * span : (c + 1) * span] for part in second_all),
        )
        for c in range(chunks)
    ]
    output = jnp.concatenate([r[0] for r in results], axis=0)
    input_grad = jnp.concatenate([r[1] for r in results], axis=0)
    query_grad, mixer_full, output_grad_t, inner_grad, outer_grad_t = [
        sum(r[2][i] for r in results[1:]) + results[0][2][i] if chunks > 1 else results[0][2][i]
        for i in range(5)
    ]

    dp_count = lax.axis_size("dp")
    dp_rank = lax.axis_index("dp")

    lanes = 128

    def lead(grad, axis_number):
        shape = grad.shape
        split = shape[:axis_number] + (dp_count, shape[axis_number] // dp_count) + shape[axis_number + 1 :]
        owned_shape = shape[:axis_number] + (shape[axis_number] // dp_count,) + shape[axis_number + 1 :]
        return jnp.moveaxis(grad.reshape(split), axis_number, 0).reshape(dp_count, -1, lanes), owned_shape

    def summed_over_dp(grads_axes):
        laid = [lead(grad, axis_number) for grad, axis_number in grads_axes]
        joined = jnp.concatenate([flat for flat, _ in laid], axis=1)
        rows = joined.shape[1]
        arrived = lax.all_to_all(
            joined.astype(jnp.bfloat16).reshape(-1, lanes), "dp", 0, 0, tiled=True
        )
        reduced = jnp.sum(arrived.astype(jnp.float32).reshape(dp_count, rows, lanes), axis=0)
        parts = []
        offset = 0
        for flat, owned_shape in laid:
            size = flat.shape[1]
            parts.append(reduced[offset : offset + size].reshape(owned_shape))
            offset += size
        return parts

    inner_part, outer_part_t = summed_over_dp([(inner_grad, 0), (outer_grad_t, 0)])
    if mode_count % dp_count == 0:
        per = mode_count // dp_count
        spectra = jnp.concatenate([r[3][0] for r in results], axis=0)
        mixed_grads = jnp.concatenate([r[3][1] for r in results], axis=0)
        all_windows = spectra.shape[0]

        def by_owner(values):
            split = values.reshape(all_windows, head_count, dp_count, per, 2 * head_size)
            return jnp.moveaxis(split, 2, 0).reshape(dp_count, -1, lanes)

        spectra_in = lax.all_to_all(by_owner(spectra).reshape(-1, lanes), "dp", 0, 0, tiled=True)
        gm_flat = by_owner(mixed_grads)
        gm_rows = gm_flat.shape[1]
        out_flat, out_shape = lead(output_grad_t, 0)
        query_flat, query_shape = lead(query_grad, 0)
        out_rows = out_flat.shape[1]
        joined = jnp.concatenate(
            [gm_flat, out_flat.astype(jnp.bfloat16), query_flat.astype(jnp.bfloat16)], axis=1
        )
        arrived = lax.all_to_all(joined.reshape(-1, lanes), "dp", 0, 0, tiled=True)
        arrived = arrived.reshape(dp_count, -1, lanes)
        summed = jnp.sum(arrived[:, gm_rows:].astype(jnp.float32), axis=0)
        output_part_t = summed[:out_rows].reshape(out_shape)
        query_part = summed[out_rows:].reshape(query_shape)
        owned = (dp_count, all_windows, head_count, per)
        spectrum_in = spectra_in.reshape(owned + (2, head_size))
        gm_in = arrived[:, :gm_rows].reshape(owned + (2 * head_size,))
        gm_pairs = jnp.stack(
            [gm_in, jnp.concatenate([gm_in[..., head_size:], -gm_in[..., :head_size]], axis=-1)], axis=4
        )
        mixer_part = product("swhmci,swhmco->hmio", spectrum_in, gm_pairs).reshape(
            head_count, per * head_size, 2 * head_size
        )
    else:
        mixer_part, output_part_t = summed_over_dp([(mixer_full, 1), (output_grad_t, 0)])
        (query_part,) = summed_over_dp([(query_grad, 0)])
    output_part = jnp.transpose(output_part_t)
    outer_part = jnp.transpose(outer_part_t)
    token_total = windows * length * dp_count

    def owned(weight, share, axis_number):
        return lax.dynamic_slice_in_dim(weight, dp_rank * share, share, axis_number)

    def stepped(grad, momentum, average, old_weight, spread):
        rate = 0.5 * spread / math.sqrt(token_total)
        new_momentum = momentum_decay * momentum + grad
        new_weight = old_weight - rate * (grad + momentum_decay * new_momentum)
        new_average = average_decay * average + (1 - average_decay) * new_weight
        return (new_momentum, new_weight, new_average)

    query_new = stepped(
        query_part,
        query_momentum,
        query_average,
        owned(query_weight, query_momentum.shape[0], 0),
        D ** (-0.5),
    )
    mixer_new = stepped(
        mixer_part,
        mixer_momentum,
        mixer_average,
        owned(mixer_weight, mixer_momentum.shape[1], 1),
        mixer_spread,
    )
    output_new = stepped(
        output_part,
        output_momentum,
        output_average,
        owned(output_weight, output_momentum.shape[1], 1),
        D ** (-0.5),
    )
    inner_new = stepped(
        inner_part,
        inner_momentum,
        inner_average,
        owned(inner_weight, inner_momentum.shape[0], 0),
        D ** (-0.5),
    )
    outer_new = stepped(
        outer_part,
        outer_momentum,
        outer_average,
        owned(outer_weight, outer_momentum.shape[1], 1),
        FF ** (-0.5),
    )
    return (
        output,
        input_grad,
        query_new[0],
        query_new[1],
        query_new[2],
        mixer_new[0],
        mixer_new[1],
        mixer_new[2],
        output_new[0],
        output_new[1],
        output_new[2],
        inner_new[0],
        inner_new[1],
        inner_new[2],
        outer_new[0],
        outer_new[1],
        outer_new[2],
    )


def solution(mesh):
    return jax.shard_map(
        on_device,
        mesh=mesh,
        in_specs=(
            P("dp", None, "head"),
            P("dp", None, "head"),
            P("head", None),
            P(None, "dp", None),
            P(None, "head"),
            P("head", None, None),
            P("head", None),
            P(None, "head"),
            P("head", None),
            P("dp", "head"),
            P("dp", "head"),
            P("head", "dp", None),
            P("head", "dp", None),
            P("head", "dp"),
            P("head", "dp"),
            P("dp", "head"),
            P("dp", "head"),
            P("head", "dp"),
            P("head", "dp"),
        ),
        out_specs=(
            P("dp", None, "head"),
            P("dp", None, "head"),
            P("dp", "head"),
            P("dp", "head"),
            P("dp", "head"),
            P("head", "dp", None),
            P("head", "dp", None),
            P("head", "dp", None),
            P("head", "dp"),
            P("head", "dp"),
            P("head", "dp"),
            P("dp", "head"),
            P("dp", "head"),
            P("dp", "head"),
            P("head", "dp"),
            P("head", "dp"),
            P("head", "dp"),
        ),
        check_vma=False,
    )
```
